32 devices in a mesh: groups: 2 (over y), state: 4 (over z), input: 2 (over x), horizon: 2 (over core).
Axes of the slice: x: 2, y: 2, z: 4, core: 2. Of those that a mesh axis runs over, the one named last changes fastest.
Arguments:
- impulses: bfloat16 [4096, 8, 256], P(('state', 'horizon'), 'input', 'groups'), parts along dimension 2, may hold values from -6 to 6
- expectations: bfloat16 [4, 16, 4096], P('groups', None, ('state', 'horizon')), parts along dimension 0, may hold values from -0.09375 to 0.09375
- region_scale: float32 [32, 2], P('groups'), parts along dimension 0, may hold values from 0.125 to 1
- regions: int32 [32], P(('state', 'horizon')), may hold values from 0 to 15
- tiles: bfloat16 [32, 4, 128, 128], P(('state', 'horizon')), may hold values from -0.5 to 0.5
- offsets: int32 [32, 4], P(('state', 'horizon')), may hold values from -1 to 1, as said below
- counts: int32 [32], P(('state', 'horizon')), may hold values from 2 to 4, as said below
Outputs:
- jacobian: float32 [128, 4, 8, 128], P(('state', 'horizon'), 'groups', 'input'), parts along dimension 1
The draws below stay inside these ranges and needn't reach their ends.
There are 2 independent parts, one for each index of `groups`. The reference program is written for one: setup_inputs(seed, part) draws one part's arguments, and reference() takes and returns one part's arrays. A program takes and returns all parts, laid end to end along the dimension named above; an argument that names none is the same for every part. Nothing has to cross between parts.
Inputs may be any that keep to these rules, and one draw needn't show every extreme that they name: tiles j >= counts[c] of block c are unused; some block uses all 4. `offsets`: tile 0 of every block reads the block below it (offset -1) and tile 1 the block above it (offset 1).
All inputs are finite; a program needn't handle non-finite values.
Results may differ from the reference program's by a relative error of at most 0.0065.
Values sent between devices are 32-bit elements; how exact they have to be, the bound alone decides.
No kernel may reach another device: no remote copies, remote signals or barrier semaphores. Data moves between devices by JAX's collectives and lax.ppermute only.
A program may use at most 64 MiB of HBM per device.

```python
import math
import jax
import jax.numpy as jnp
from jax import lax

BLK = 128
NBAND = 4
BLK_DEV = 4
INPUTS = 8
OUTS = 2
HOR = 128
EXPR = 16
REGIONS = 16
BLOCKS = 32
STATES = 4096


def draw_counts(key, part):
    key_cap, key_each, key_dense = jax.random.split(jax.random.fold_in(key, 17), 3)
    slab_count = BLOCKS // BLK_DEV
    slab_cap = jax.random.randint(key_cap, (slab_count,), 2, NBAND + 1)
    capped = jnp.repeat(slab_cap, BLK_DEV)
    drawn = jax.random.randint(key_each, (BLOCKS,), 0, 1 << 20)
    counts = 2 + drawn % (capped - 1)
    dense_at = jax.random.randint(key_dense, (), 0, BLOCKS)
    return jnp.where(jnp.arange(BLOCKS) == dense_at, NBAND, counts).astype(jnp.int32)


def draw_offsets(key, part):
    key_rest = jax.random.fold_in(key, 29)
    rest = jax.random.randint(key_rest, (BLOCKS, NBAND), -1, 2)
    slot = jnp.arange(NBAND, dtype=jnp.int32)[None, :]
    fixed = jnp.where(slot == 0, -1, 1)
    return jnp.where(slot < 2, fixed, rest).astype(jnp.int32)


def place_ends(values, stream_key, least, top_value):
    longest = values.shape.index(max(values.shape))
    spots = []
    for shift in (0, 1):
        where = [jax.random.randint(jax.random.fold_in(stream_key, axis), (), 0, length) for axis, length in enumerate(values.shape)]
        where[longest] = (where[longest] + shift) % values.shape[longest]
        spots.append(tuple(where))
    return values.at[spots[0]].set(least).at[spots[1]].set(top_value)


def levels(rng, shape, cuts, low, top_value):
    def one(dim, blocks):
        steps = jax.random.uniform(jax.random.fold_in(jax.random.fold_in(rng, 6), dim), (blocks,), jnp.float32, low / len(cuts), top_value / len(cuts))
        return jnp.repeat(jnp.exp(steps), shape[dim] // blocks).reshape((-1,) + (1,) * (len(shape) - dim - 1))

    level = one(*cuts[0])
    for cut in cuts[1:]:
        level = level * one(*cut)
    return level


def normal_values(rng, dims, scale, most, shards=(), kind=jnp.bfloat16):
    loudness = levels(rng, dims, shards, -0.22, 0.18) if shards else 1.0
    values = jax.random.normal(rng, dims, jnp.float32) * scale * loudness
    return jnp.minimum(jnp.maximum(values, -most), most).astype(kind)


def setup_inputs(seed: int = 0, part: int = 0) -> dict:
    key_of = jax.random.split(jax.random.key(seed), 8)
    part_splits = jax.random.split(jax.random.fold_in(key_of[7], part), 8)
    impulses = normal_values(part_splits[0], (STATES, INPUTS, HOR), 1.0, 6.0, ((0, 8), (1, 2)))
    expectations = normal_values(part_splits[1], (OUTS, EXPR, STATES), STATES ** -0.5, 0.09375, ((2, 8),))
    region_scale = jnp.clip(jnp.exp(jax.random.uniform(part_splits[2], (REGIONS, OUTS), jnp.float32, math.log(0.125), math.log(1.0))), 0.125, 1.0)
    regions = place_ends(jax.random.randint(key_of[3], (BLOCKS,), 0, REGIONS), jax.random.fold_in(key_of[3], 1), 0, REGIONS - 1).astype(jnp.int32)
    tiles = normal_values(key_of[4], (BLOCKS, NBAND, BLK, BLK), BLK ** -0.5, 0.5, ((0, 8),))
    offsets = draw_offsets(jax.random.fold_in(key_of[7], 71), part)
    counts = draw_counts(jax.random.fold_in(key_of[7], 71), part)
    return dict(impulses=impulses, expectations=expectations, region_scale=region_scale, regions=regions, tiles=tiles, offsets=offsets, counts=counts)


def next_row(previous, fresh):
    moved = jnp.pad(previous[:, :, :-1], ((0, 0), (0, 0), (1, 0)))
    current = fresh + moved
    return (current, current)

def reference(impulses, expectations, region_scale, regions, tiles, offsets, counts):
    width = INPUTS * HOR
    block_scale = region_scale[regions]
    weighted = expectations.astype(jnp.float32).reshape(OUTS, EXPR, BLOCKS, BLK) * block_scale.T[:, None, :, None]
    weighted = weighted.astype(jnp.bfloat16).reshape(OUTS * EXPR, STATES).astype(jnp.float32)
    in_use = jnp.arange(NBAND, dtype=jnp.int32)[None, :] < counts[:, None]
    masked = jnp.where(in_use[:, :, None, None], tiles, jnp.zeros((), jnp.bfloat16))
    scaling = lax.rsqrt(counts.astype(jnp.float32))
    source = jnp.arange(BLOCKS, dtype=jnp.int32)[:, None] + offsets
    inside = (source >= 0) & (source < BLOCKS)
    source_index = jnp.clip(source, 0, BLOCKS - 1).astype(jnp.int32)
    current = impulses.astype(jnp.float32).reshape(BLOCKS, BLK, width)
    pieces = []
    for section in range(HOR // EXPR):
        if section > 0:
            total = jnp.zeros((BLOCKS, BLK, width), jnp.float32)
            for slot in range(NBAND):
                picked = jnp.take(current, source_index[:, slot], axis=0)
                picked = jnp.where(inside[:, slot, None, None], picked, jnp.zeros((), jnp.float32))
                total = total + jnp.einsum('cuv,cvn->cun', masked[:, slot].astype(jnp.float32), picked, precision=lax.Precision.HIGHEST)
            current = total * scaling[:, None, None]
        product = jnp.dot(weighted, current.reshape(STATES, width), precision=lax.Precision.HIGHEST, preferred_element_type=jnp.float32)
        pieces.append(product.reshape(OUTS, EXPR, INPUTS, HOR).transpose(1, 0, 2, 3))
    fake_news = jnp.concatenate(pieces, axis=0)
    _, jacobian = lax.scan(next_row, jnp.zeros((OUTS, INPUTS, HOR), jnp.float32), fake_news)
    return jacobian
```

```python
import jax
import jax.numpy as jnp
from jax import lax
from jax.sharding import PartitionSpec as P


def with_halo(block, sides, width):
    for axis, dim in sides:
        count = lax.axis_size(axis)
        forward = [(i, i + 1) for i in range(count - 1)]
        backward = [(target, source) for source, target in forward]
        low = lax.ppermute(
            lax.slice_in_dim(block, block.shape[dim] - width, None, axis=dim), axis, forward
        )
        high = lax.ppermute(lax.slice_in_dim(block, 0, width, axis=dim), axis, backward)
        block = jnp.concatenate([low, block, high], axis=dim)
    return block


def diagonal_sums(news):
    rows = news.shape[0]
    width = news.shape[-1]
    total = news
    shift = 1
    while shift < rows:
        moved = lax.pad(
            total[: rows - shift, ..., : width - shift],
            jnp.zeros((), total.dtype),
            [(shift, 0, 0)] + [(0, 0, 0)] * (total.ndim - 2) + [(shift, 0, 0)],
        )
        total = total + moved
        shift *= 2
    return total


def split_product(rows_full, data_half):
    upper = rows_full.astype(jnp.bfloat16)
    remain = rows_full - upper.astype(jnp.float32)
    middle = remain.astype(jnp.bfloat16)
    lower = (remain - middle.astype(jnp.float32)).astype(jnp.bfloat16)
    total = jnp.dot(upper, data_half, preferred_element_type=jnp.float32)
    total = total + jnp.dot(middle, data_half, preferred_element_type=jnp.float32)
    return total + jnp.dot(lower, data_half, preferred_element_type=jnp.float32)


def pull_back(rows, masked, source, scaling):
    block_count = rows.shape[0]
    scaled = rows * scaling[:, None, None]
    contrib = jnp.einsum("cru,cjuv->cjrv", scaled, masked, precision=lax.Precision.HIGHEST)
    target = (
        source[:, :, None] == jnp.arange(block_count + 2, dtype=jnp.int32)[None, None, :]
    ).astype(jnp.float32)
    spread = jnp.einsum("cjb,cjrv->brv", target, contrib, precision=lax.Precision.HIGHEST)
    edges = jnp.stack([spread[0], spread[-1]], axis=0)
    arrived = with_halo(edges, ((("state", "horizon"), 0),), 1)
    inner = spread[1:-1]
    inner = inner.at[0].add(arrived[0])
    inner = inner.at[-1].add(arrived[3])
    return inner


def shards(impulses, expectations, region_scale, regions, tiles, offsets, counts):
    block_count, band_count, tile_size, _ = tiles.shape
    state_count, input_count, horizon = impulses.shape
    output_count, expect_rows, _ = expectations.shape
    region_total = region_scale.shape[0]
    width = input_count * horizon
    sections = horizon // expect_rows
    row_count = output_count * expect_rows
    onehot = (regions[:, None] == jnp.arange(region_total, dtype=jnp.int32)[None, :]).astype(
        jnp.float32
    )
    block_scale = jnp.dot(
        onehot, region_scale, precision=lax.Precision.HIGHEST, preferred_element_type=jnp.float32
    )
    weighted = (
        expectations.astype(jnp.float32).reshape(output_count, expect_rows, block_count, tile_size)
        * block_scale.T[:, None, :, None]
    )
    weighted_half = weighted.astype(jnp.bfloat16).reshape(row_count, state_count)
    in_use = jnp.arange(band_count, dtype=jnp.int32)[None, :] < counts[:, None]
    masked = jnp.where(in_use[:, :, None, None], tiles, jnp.zeros((), jnp.bfloat16)).astype(
        jnp.float32
    )
    scaling = lax.rsqrt(counts.astype(jnp.float32))
    source = jnp.arange(block_count, dtype=jnp.int32)[:, None] + 1 + offsets
    flat_start = impulses.reshape(state_count, width)
    pieces = []
    rows = (
        weighted_half.astype(jnp.float32)
        .reshape(row_count, block_count, tile_size)
        .transpose(1, 0, 2)
    )
    for section in range(sections):
        if section > 0:
            rows = pull_back(rows, masked, source, scaling)
            flat_rows = rows.transpose(1, 0, 2).reshape(row_count, state_count)
            product = split_product(flat_rows, flat_start)
        else:
            product = jnp.dot(weighted_half, flat_start, preferred_element_type=jnp.float32)
        pieces.append(
            product.reshape(output_count, expect_rows, input_count, horizon).transpose(1, 0, 2, 3)
        )
    partial_news = jnp.concatenate(pieces, axis=0)
    own_rows = horizon // lax.axis_size(("state", "horizon"))
    first_row = lax.axis_index(("state", "horizon")) * own_rows
    whole = lax.psum(partial_news, ("state", "horizon"))
    jacobian = diagonal_sums(whole)
    return lax.dynamic_slice_in_dim(jacobian, first_row, own_rows, 0)


def solution(mesh):
    return jax.shard_map(
        shards,
        mesh=mesh,
        in_specs=(
            P(("state", "horizon"), "input", "groups"),
            P("groups", None, ("state", "horizon")),
            P("groups", None),
            P(("state", "horizon")),
            P(("state", "horizon"), None, None, None),
            P(("state", "horizon"), None),
            P(("state", "horizon")),
        ),
        out_specs=P(("state", "horizon"), "groups", "input", None),
        check_vma=False,
    )
```

```python
import jax
import jax.numpy as jnp
from jax import lax
from jax.sharding import PartitionSpec as P


def with_halo(block, sides, width):
    for axis, dim in sides:
        count = lax.axis_size(axis)
        forward = [(i, i + 1) for i in range(count - 1)]
        backward = [(target, source) for source, target in forward]
        low = lax.ppermute(
            lax.slice_in_dim(block, block.shape[dim] - width, None, axis=dim), axis, forward
        )
        high = lax.ppermute(lax.slice_in_dim(block, 0, width, axis=dim), axis, backward)
        block = jnp.concatenate([low, block, high], axis=dim)
    return block


def diagonal_sums(news):
    rows = news.shape[0]
    width = news.shape[-1]
    total = news
    shift = 1
    while shift < rows:
        moved = lax.pad(
            total[: rows - shift, ..., : width - shift],
            jnp.zeros((), total.dtype),
            [(shift, 0, 0)] + [(0, 0, 0)] * (total.ndim - 2) + [(shift, 0, 0)],
        )
        total = total + moved
        shift *= 2
    return total


def split_product(rows_full, data_half):
    upper = rows_full.astype(jnp.bfloat16)
    remain = rows_full - upper.astype(jnp.float32)
    middle = remain.astype(jnp.bfloat16)
    lower = (remain - middle.astype(jnp.float32)).astype(jnp.bfloat16)
    total = jnp.dot(upper, data_half, preferred_element_type=jnp.float32)
    total = total + jnp.dot(middle, data_half, preferred_element_type=jnp.float32)
    return total + jnp.dot(lower, data_half, preferred_element_type=jnp.float32)


def pull_back(rows, masked, source, scaling):
    block_count = rows.shape[0]
    scaled = rows * scaling[:, None, None]
    contrib = jnp.einsum("cru,cjuv->cjrv", scaled, masked, precision=lax.Precision.HIGHEST)
    target = (
        source[:, :, None] == jnp.arange(block_count + 2, dtype=jnp.int32)[None, None, :]
    ).astype(jnp.float32)
    spread = jnp.einsum("cjb,cjrv->brv", target, contrib, precision=lax.Precision.HIGHEST)
    edges = jnp.stack([spread[0], spread[-1]], axis=0)
    arrived = with_halo(edges, ((("state", "horizon"), 0),), 1)
    inner = spread[1:-1]
    inner = inner.at[0].add(arrived[0])
    inner = inner.at[-1].add(arrived[3])
    return inner


def shards(impulses, expectations, region_scale, regions, tiles, offsets, counts):
    block_count, band_count, tile_size, _ = tiles.shape
    state_count, input_count, horizon = impulses.shape
    output_count, expect_rows, _ = expectations.shape
    region_total = region_scale.shape[0]
    width = input_count * horizon
    sections = horizon // expect_rows
    row_count = output_count * expect_rows
    onehot = (regions[:, None] == jnp.arange(region_total, dtype=jnp.int32)[None, :]).astype(
        jnp.float32
    )
    block_scale = jnp.dot(
        onehot, region_scale, precision=lax.Precision.HIGHEST, preferred_element_type=jnp.float32
    )
    weighted = (
        expectations.astype(jnp.float32).reshape(output_count, expect_rows, block_count, tile_size)
        * block_scale.T[:, None, :, None]
    )
    weighted_half = weighted.astype(jnp.bfloat16).reshape(row_count, state_count)
    in_use = jnp.arange(band_count, dtype=jnp.int32)[None, :] < counts[:, None]
    masked = jnp.where(in_use[:, :, None, None], tiles, jnp.zeros((), jnp.bfloat16)).astype(
        jnp.float32
    )
    scaling = lax.rsqrt(counts.astype(jnp.float32))
    source = jnp.arange(block_count, dtype=jnp.int32)[:, None] + 1 + offsets
    flat_start = impulses.reshape(state_count, width)
    pieces = []
    rows = (
        weighted_half.astype(jnp.float32)
        .reshape(row_count, block_count, tile_size)
        .transpose(1, 0, 2)
    )
    for section in range(sections):
        if section > 0:
            rows = pull_back(rows, masked, source, scaling)
            flat_rows = rows.transpose(1, 0, 2).reshape(row_count, state_count)
            product = split_product(flat_rows, flat_start)
        else:
            product = jnp.dot(weighted_half, flat_start, preferred_element_type=jnp.float32)
        pieces.append(
            product.reshape(output_count, expect_rows, input_count, horizon).transpose(1, 0, 2, 3)
        )
    partial_news = jnp.concatenate(pieces, axis=0)
    jacobian = diagonal_sums(partial_news)
    return lax.psum_scatter(jacobian, ("state", "horizon"), scatter_dimension=0, tiled=True)


def solution(mesh):
    return jax.shard_map(
        shards,
        mesh=mesh,
        in_specs=(
            P(("state", "horizon"), "input", "groups"),
            P("groups", None, ("state", "horizon")),
            P("groups", None),
            P(("state", "horizon")),
            P(("state", "horizon"), None, None, None),
            P(("state", "horizon"), None),
            P(("state", "horizon")),
        ),
        out_specs=P(("state", "horizon"), "groups", "input", None),
        check_vma=False,
    )
```

```python
import jax
import jax.numpy as jnp
from jax import lax
from jax.sharding import PartitionSpec as P


def with_halo(block, sides, width):
    for axis, dim in sides:
        count = lax.axis_size(axis)
        forward = [(i, i + 1) for i in range(count - 1)]
        backward = [(target, source) for source, target in forward]
        low = lax.ppermute(
            lax.slice_in_dim(block, block.shape[dim] - width, None, axis=dim), axis, forward
        )
        high = lax.ppermute(lax.slice_in_dim(block, 0, width, axis=dim), axis, backward)
        block = jnp.concatenate([low, block, high], axis=dim)
    return block


def diagonal_sums(news):
    rows = news.shape[0]
    width = news.shape[-1]
    total = news
    shift = 1
    while shift < rows:
        moved = lax.pad(
            total[: rows - shift, ..., : width - shift],
            jnp.zeros((), total.dtype),
            [(shift, 0, 0)] + [(0, 0, 0)] * (total.ndim - 2) + [(shift, 0, 0)],
        )
        total = total + moved
        shift *= 2
    return total


def halving_scatter(full):
    state_count = lax.axis_size("state")
    core_count = lax.axis_size("horizon")
    count = state_count * core_count
    if count & (count - 1) or core_count & (core_count - 1):
        return lax.psum_scatter(full, ("state", "horizon"), scatter_dimension=0, tiled=True)
    index = lax.axis_index(("state", "horizon"))
    held = full.reshape((count, full.shape[0] // count) + full.shape[1:])
    step = 1
    while step < count:
        if step < core_count:
            axis, size, flip = "horizon", core_count, step
        else:
            axis, size, flip = "state", state_count, step // core_count
        pairs = [(member, member ^ flip) for member in range(size)]
        bit = (index // step) % 2
        halves = held.reshape((held.shape[0] // 2, 2) + held.shape[1:])
        keep = jnp.where(bit == 1, halves[:, 1], halves[:, 0])
        send = jnp.where(bit == 1, halves[:, 0], halves[:, 1])
        held = keep + lax.ppermute(send, axis, pairs)
        step *= 2
    return held.reshape(held.shape[1:])


def split_product(rows_full, data_half):
    upper = rows_full.astype(jnp.bfloat16)
    remain = rows_full - upper.astype(jnp.float32)
    middle = remain.astype(jnp.bfloat16)
    lower = (remain - middle.astype(jnp.float32)).astype(jnp.bfloat16)
    total = jnp.dot(upper, data_half, preferred_element_type=jnp.float32)
    total = total + jnp.dot(middle, data_half, preferred_element_type=jnp.float32)
    return total + jnp.dot(lower, data_half, preferred_element_type=jnp.float32)


def pull_back(rows, masked, source, scaling):
    block_count = rows.shape[0]
    scaled = rows * scaling[:, None, None]
    contrib = jnp.einsum("cru,cjuv->cjrv", scaled, masked, precision=lax.Precision.HIGHEST)
    target = (
        source[:, :, None] == jnp.arange(block_count + 2, dtype=jnp.int32)[None, None, :]
    ).astype(jnp.float32)
    spread = jnp.einsum("cjb,cjrv->brv", target, contrib, precision=lax.Precision.HIGHEST)
    edges = jnp.stack([spread[0], spread[-1]], axis=0)
    arrived = with_halo(edges, ((("state", "horizon"), 0),), 1)
    inner = spread[1:-1]
    inner = inner.at[0].add(arrived[0])
    inner = inner.at[-1].add(arrived[3])
    return inner


def shards(impulses, expectations, region_scale, regions, tiles, offsets, counts):
    block_count, band_count, tile_size, _ = tiles.shape
    state_count, input_count, horizon = impulses.shape
    output_count, expect_rows, _ = expectations.shape
    region_total = region_scale.shape[0]
    width = input_count * horizon
    sections = horizon // expect_rows
    row_count = output_count * expect_rows
    onehot = (regions[:, None] == jnp.arange(region_total, dtype=jnp.int32)[None, :]).astype(
        jnp.float32
    )
    block_scale = jnp.dot(
        onehot, region_scale, precision=lax.Precision.HIGHEST, preferred_element_type=jnp.float32
    )
    weighted = (
        expectations.astype(jnp.float32).reshape(output_count, expect_rows, block_count, tile_size)
        * block_scale.T[:, None, :, None]
    )
    weighted_half = weighted.astype(jnp.bfloat16).reshape(row_count, state_count)
    in_use = jnp.arange(band_count, dtype=jnp.int32)[None, :] < counts[:, None]
    masked = jnp.where(in_use[:, :, None, None], tiles, jnp.zeros((), jnp.bfloat16)).astype(
        jnp.float32
    )
    scaling = lax.rsqrt(counts.astype(jnp.float32))
    source = jnp.arange(block_count, dtype=jnp.int32)[:, None] + 1 + offsets
    flat_start = impulses.reshape(state_count, width)
    pieces = []
    rows = (
        weighted_half.astype(jnp.float32)
        .reshape(row_count, block_count, tile_size)
        .transpose(1, 0, 2)
    )
    for section in range(sections):
        if section > 0:
            rows = pull_back(rows, masked, source, scaling)
            flat_rows = rows.transpose(1, 0, 2).reshape(row_count, state_count)
            product = split_product(flat_rows, flat_start)
        else:
            product = jnp.dot(weighted_half, flat_start, preferred_element_type=jnp.float32)
        pieces.append(
            product.reshape(output_count, expect_rows, input_count, horizon).transpose(1, 0, 2, 3)
        )
    partial_news = jnp.concatenate(pieces, axis=0)
    jacobian = diagonal_sums(partial_news)
    return halving_scatter(jacobian)


def solution(mesh):
    return jax.shard_map(
        shards,
        mesh=mesh,
        in_specs=(
            P(("state", "horizon"), "input", "groups"),
            P("groups", None, ("state", "horizon")),
            P("groups", None),
            P(("state", "horizon")),
            P(("state", "horizon"), None, None, None),
            P(("state", "horizon"), None),
            P(("state", "horizon")),
        ),
        out_specs=P(("state", "horizon"), "groups", "input", None),
        check_vma=False,
    )
```

```python
import jax
import jax.numpy as jnp
from jax import lax
from jax.sharding import PartitionSpec as P


def diagonal_sums(news):
    rows = news.shape[0]
    width = news.shape[-1]
    total = news
    shift = 1
    while shift < rows:
        moved = lax.pad(
            total[: rows - shift, ..., : width - shift],
            jnp.zeros((), total.dtype),
            [(shift, 0, 0)] + [(0, 0, 0)] * (total.ndim - 2) + [(shift, 0, 0)],
        )
        total = total + moved
        shift *= 2
    return total


def halving_scatter(full):
    state_count = lax.axis_size("state")
    core_count = lax.axis_size("horizon")
    count = state_count * core_count
    if count & (count - 1) or core_count & (core_count - 1):
        return lax.psum_scatter(full, ("state", "horizon"), scatter_dimension=0, tiled=True)
    index = lax.axis_index(("state", "horizon"))
    held = full.reshape((count, full.shape[0] // count) + full.shape[1:])
    step = 1
    while step < count:
        if step < core_count:
            axis, size, flip = "horizon", core_count, step
        else:
            axis, size, flip = "state", state_count, step // core_count
        pairs = [(member, member ^ flip) for member in range(size)]
        bit = (index // step) % 2
        halves = held.reshape((held.shape[0] // 2, 2) + held.shape[1:])
        keep = jnp.where(bit == 1, halves[:, 1], halves[:, 0])
        send = jnp.where(bit == 1, halves[:, 0], halves[:, 1])
        held = keep + lax.ppermute(send, axis, pairs)
        step *= 2
    return held.reshape(held.shape[1:])


def split_product(rows_full, data_half):
    upper = rows_full.astype(jnp.bfloat16)
    remain = rows_full - upper.astype(jnp.float32)
    middle = remain.astype(jnp.bfloat16)
    lower = (remain - middle.astype(jnp.float32)).astype(jnp.bfloat16)
    total = jnp.dot(upper, data_half, preferred_element_type=jnp.float32)
    total = total + jnp.dot(middle, data_half, preferred_element_type=jnp.float32)
    return total + jnp.dot(lower, data_half, preferred_element_type=jnp.float32)


def shift_pairs(axis, step):
    count = lax.axis_size(axis)
    if step > 0:
        return [(i, i + 1) for i in range(count - 1)]
    return [(i + 1, i) for i in range(count - 1)]


def to_right(value):
    return lax.ppermute(value, ("state", "horizon"), shift_pairs(("state", "horizon"), 1))


def to_left(value):
    return lax.ppermute(value, ("state", "horizon"), shift_pairs(("state", "horizon"), -1))


def band_step(rows, moves):
    parts = jnp.einsum("cru,cduv->cdrv", rows, moves, precision=lax.Precision.HIGHEST)
    down, same, up = parts[:, 0], parts[:, 1], parts[:, 2]
    zero = jnp.zeros_like(same[:1])
    inner = same + jnp.concatenate([down[1:], zero], 0) + jnp.concatenate([zero, up[:-1]], 0)
    return inner, down[0], up[-1]


def mat(rows, matrix):
    return jnp.dot(rows, matrix, precision=lax.Precision.HIGHEST)


def one_step(rows, moves):
    inner, out_low, out_high = band_step(rows, moves)
    from_low = to_right(out_high)
    from_high = to_left(out_low)
    inner = inner.at[0].add(from_low).at[-1].add(from_high)
    return [inner]


def two_steps(rows, moves, low_move, high_move):
    inner, out_low, out_high = band_step(rows, moves)
    from_low = to_right(jnp.stack([out_high, mat(inner[-1], moves[-1, 2])]))
    from_high = to_left(jnp.stack([out_low, mat(inner[0], moves[0, 0])]))
    second, _, _ = band_step(inner, moves)
    first = inner.at[0].add(from_low[0]).at[-1].add(from_high[0])
    second = second.at[0].add(mat(from_low[0], moves[0, 1]))
    second = second.at[1].add(mat(from_low[0], moves[0, 2]))
    second = second.at[-1].add(mat(from_high[0], moves[-1, 1]))
    second = second.at[-2].add(mat(from_high[0], moves[-1, 0]))
    second = second.at[0].add(from_low[1] + mat(out_low, low_move))
    second = second.at[-1].add(from_high[1] + mat(out_high, high_move))
    return [first, second]


def shards(impulses, expectations, region_scale, regions, tiles, offsets, counts):
    block_count, band_count, tile_size, _ = tiles.shape
    state_count, input_count, horizon = impulses.shape
    output_count, expect_rows, _ = expectations.shape
    region_total = region_scale.shape[0]
    width = input_count * horizon
    sections = horizon // expect_rows
    row_count = output_count * expect_rows
    onehot = (regions[:, None] == jnp.arange(region_total, dtype=jnp.int32)[None, :]).astype(
        jnp.float32
    )
    block_scale = jnp.dot(
        onehot, region_scale, precision=lax.Precision.HIGHEST, preferred_element_type=jnp.float32
    )
    weighted = (
        expectations.astype(jnp.float32).reshape(output_count, expect_rows, block_count, tile_size)
        * block_scale.T[:, None, :, None]
    )
    weighted_half = weighted.astype(jnp.bfloat16).reshape(row_count, state_count)
    in_use = jnp.arange(band_count, dtype=jnp.int32)[None, :] < counts[:, None]
    scaling = lax.rsqrt(counts.astype(jnp.float32))
    moves = []
    for shift in (-1, 0, 1):
        chosen = in_use & (offsets == shift)
        total = jnp.zeros((block_count, tile_size, tile_size), jnp.float32)
        for slot in range(band_count):
            total = total + jnp.where(
                chosen[:, slot, None, None], tiles[:, slot].astype(jnp.float32), 0.0
            )
        moves.append(total * scaling[:, None, None])
    moves = jnp.stack(moves, axis=1)
    low_move = to_right(moves[-1, 2])
    high_move = to_left(moves[0, 0])
    flat_start = impulses.reshape(state_count, width)
    rows = (
        weighted_half.astype(jnp.float32)
        .reshape(row_count, block_count, tile_size)
        .transpose(1, 0, 2)
    )
    levels = []
    remaining = sections - 1
    if remaining % 2:
        levels += one_step(rows, moves)
        remaining -= 1
    while remaining:
        levels += two_steps(levels[-1] if levels else rows, moves, low_move, high_move)
        remaining -= 2
    pieces = [jnp.dot(weighted_half, flat_start, preferred_element_type=jnp.float32)]
    for level in levels:
        flat_rows = level.transpose(1, 0, 2).reshape(row_count, state_count)
        pieces.append(split_product(flat_rows, flat_start))
    pieces = [
        piece.reshape(output_count, expect_rows, input_count, horizon).transpose(1, 0, 2, 3)
        for piece in pieces
    ]
    partial_news = jnp.concatenate(pieces, axis=0)
    jacobian = diagonal_sums(partial_news)
    return halving_scatter(jacobian)


def solution(mesh):
    return jax.shard_map(
        shards,
        mesh=mesh,
        in_specs=(
            P(("state", "horizon"), "input", "groups"),
            P("groups", None, ("state", "horizon")),
            P("groups", None),
            P(("state", "horizon")),
            P(("state", "horizon"), None, None, None),
            P(("state", "horizon"), None),
            P(("state", "horizon")),
        ),
        out_specs=P(("state", "horizon"), "groups", "input", None),
        check_vma=False,
    )
```

```python
import jax
import jax.numpy as jnp
from jax import lax
from jax.sharding import PartitionSpec as P


def diagonal_sums(news):
    rows = news.shape[0]
    width = news.shape[-1]
    total = news
    shift = 1
    while shift < rows:
        moved = lax.pad(
            total[: rows - shift, ..., : width - shift],
            jnp.zeros((), total.dtype),
            [(shift, 0, 0)] + [(0, 0, 0)] * (total.ndim - 2) + [(shift, 0, 0)],
        )
        total = total + moved
        shift *= 2
    return total


def halving_scatter(full):
    state_count = lax.axis_size("state")
    core_count = lax.axis_size("horizon")
    count = state_count * core_count
    if count & (count - 1) or core_count & (core_count - 1):
        return lax.psum_scatter(full, ("state", "horizon"), scatter_dimension=0, tiled=True)
    index = lax.axis_index(("state", "horizon"))
    held = full.reshape((count, full.shape[0] // count) + full.shape[1:])
    step = 1
    while step < count:
        if step < core_count:
            axis, size, flip = "horizon", core_count, step
        else:
            axis, size, flip = "state", state_count, step // core_count
        pairs = [(member, member ^ flip) for member in range(size)]
        bit = (index // step) % 2
        halves = held.reshape((held.shape[0] // 2, 2) + held.shape[1:])
        keep = jnp.where(bit == 1, halves[:, 1], halves[:, 0])
        send = jnp.where(bit == 1, halves[:, 0], halves[:, 1])
        held = keep + lax.ppermute(send, axis, pairs)
        step *= 2
    return held.reshape(held.shape[1:])


def split_product(rows_full, data_half):
    upper = rows_full.astype(jnp.bfloat16)
    remain = rows_full - upper.astype(jnp.float32)
    middle = remain.astype(jnp.bfloat16)
    lower = (remain - middle.astype(jnp.float32)).astype(jnp.bfloat16)
    total = jnp.dot(upper, data_half, preferred_element_type=jnp.float32)
    total = total + jnp.dot(middle, data_half, preferred_element_type=jnp.float32)
    return total + jnp.dot(lower, data_half, preferred_element_type=jnp.float32)


def shift_pairs(axis, step):
    count = lax.axis_size(axis)
    if step > 0:
        return [(i, i + 1) for i in range(count - 1)]
    return [(i + 1, i) for i in range(count - 1)]


def to_right(value):
    return lax.ppermute(value, ("state", "horizon"), shift_pairs(("state", "horizon"), 1))


def to_left(value):
    return lax.ppermute(value, ("state", "horizon"), shift_pairs(("state", "horizon"), -1))


def band_step(rows, moves):
    parts = jnp.einsum("cru,cduv->cdrv", rows, moves, precision=lax.Precision.HIGHEST)
    down, same, up = parts[:, 0], parts[:, 1], parts[:, 2]
    zero = jnp.zeros_like(same[:1])
    inner = same + jnp.concatenate([down[1:], zero], 0) + jnp.concatenate([zero, up[:-1]], 0)
    return inner, down[0], up[-1]


def mat(rows, matrix):
    return jnp.dot(rows, matrix, precision=lax.Precision.HIGHEST)


def ext_step(rows, moves):
    parts = jnp.einsum("cru,cduv->cdrv", rows, moves, precision=lax.Precision.HIGHEST)
    down, same, up = parts[:, 0], parts[:, 1], parts[:, 2]
    zero = jnp.zeros_like(same[:1])
    inner = same + jnp.concatenate([down[1:], zero], 0) + jnp.concatenate([zero, up[:-1]], 0)
    return inner, parts[1, 0], parts[-2, 2]


def exchange_round(rows, moves, wide, steps):
    zero = jnp.zeros_like(rows[:1])
    held = jnp.concatenate([zero, rows, zero], 0)
    to_low, to_high, mine = [], [], []
    for _ in range(steps):
        held, out_low, out_high = ext_step(held, wide)
        to_low.append(out_low)
        to_high.append(out_high)
        mine.append(held[1:-1])
    from_low = to_right(jnp.stack(to_high))
    from_high = to_left(jnp.stack(to_low))
    levels = []
    carried = None
    for step in range(steps):
        if carried is None:
            carried = jnp.zeros_like(rows)
        else:
            carried, _, _ = band_step(carried, moves)
        carried = carried.at[0].add(from_low[step]).at[-1].add(from_high[step])
        levels.append(mine[step] + carried)
    return levels


def shards(impulses, expectations, region_scale, regions, tiles, offsets, counts):
    block_count, band_count, tile_size, _ = tiles.shape
    state_count, input_count, horizon = impulses.shape
    output_count, expect_rows, _ = expectations.shape
    region_total = region_scale.shape[0]
    width = input_count * horizon
    sections = horizon // expect_rows
    row_count = output_count * expect_rows
    onehot = (regions[:, None] == jnp.arange(region_total, dtype=jnp.int32)[None, :]).astype(
        jnp.float32
    )
    block_scale = jnp.dot(
        onehot, region_scale, precision=lax.Precision.HIGHEST, preferred_element_type=jnp.float32
    )
    weighted = (
        expectations.astype(jnp.float32).reshape(output_count, expect_rows, block_count, tile_size)
        * block_scale.T[:, None, :, None]
    )
    weighted_half = weighted.astype(jnp.bfloat16).reshape(row_count, state_count)
    in_use = jnp.arange(band_count, dtype=jnp.int32)[None, :] < counts[:, None]
    scaling = lax.rsqrt(counts.astype(jnp.float32))
    moves = []
    for shift in (-1, 0, 1):
        chosen = in_use & (offsets == shift)
        total = jnp.zeros((block_count, tile_size, tile_size), jnp.float32)
        for slot in range(band_count):
            total = total + jnp.where(
                chosen[:, slot, None, None], tiles[:, slot].astype(jnp.float32), 0.0
            )
        moves.append(total * scaling[:, None, None])
    moves = jnp.stack(moves, axis=1)
    flat_start = impulses.reshape(state_count, width)
    rows = (
        weighted_half.astype(jnp.float32)
        .reshape(row_count, block_count, tile_size)
        .transpose(1, 0, 2)
    )
    inner, out_low, out_high = band_step(rows, moves)
    edge_low = jnp.concatenate([out_high, moves[-1, 1], moves[-1, 2]], 0)
    edge_high = jnp.concatenate([out_low, moves[0, 0], moves[0, 1]], 0)
    from_low = to_right(edge_low)
    from_high = to_left(edge_high)
    levels = [rows, inner.at[0].add(from_low[:row_count]).at[-1].add(from_high[:row_count])]
    left_self = from_low[row_count : row_count + tile_size]
    left_up = from_low[row_count + tile_size :]
    right_down = from_high[row_count : row_count + tile_size]
    right_self = from_high[row_count + tile_size :]
    blank = jnp.zeros_like(left_self)
    wide = jnp.concatenate(
        [
            jnp.stack([blank, left_self, left_up])[None],
            moves,
            jnp.stack([right_down, right_self, blank])[None],
        ],
        0,
    )
    remaining = sections - 2
    while remaining > 0:
        steps = min(3, remaining)
        levels += exchange_round(levels[-1], moves, wide, steps)
        remaining -= steps
    stacked = jnp.concatenate(
        [level.transpose(1, 0, 2).reshape(row_count, state_count) for level in levels], 0
    )
    product = split_product(stacked, flat_start)
    pieces = [
        piece.reshape(output_count, expect_rows, input_count, horizon).transpose(1, 0, 2, 3)
        for piece in jnp.split(product, sections, 0)
    ]
    partial_news = jnp.concatenate(pieces, axis=0)
    jacobian = diagonal_sums(partial_news)
    return halving_scatter(jacobian)


def solution(mesh):
    return jax.shard_map(
        shards,
        mesh=mesh,
        in_specs=(
            P(("state", "horizon"), "input", "groups"),
            P("groups", None, ("state", "horizon")),
            P("groups", None),
            P(("state", "horizon")),
            P(("state", "horizon"), None, None, None),
            P(("state", "horizon"), None),
            P(("state", "horizon")),
        ),
        out_specs=P(("state", "horizon"), "groups", "input", None),
        check_vma=False,
    )
```

```python
import jax
import jax.numpy as jnp
from jax import lax
from jax.sharding import PartitionSpec as P


def diagonal_sums(news):
    rows = news.shape[0]
    width = news.shape[-1]
    total = news
    shift = 1
    while shift < rows:
        moved = lax.pad(
            total[: rows - shift, ..., : width - shift],
            jnp.zeros((), total.dtype),
            [(shift, 0, 0)] + [(0, 0, 0)] * (total.ndim - 2) + [(shift, 0, 0)],
        )
        total = total + moved
        shift *= 2
    return total


def halving_scatter(full):
    state_count = lax.axis_size("state")
    core_count = lax.axis_size("horizon")
    count = state_count * core_count
    if count & (count - 1) or core_count & (core_count - 1):
        return lax.psum_scatter(full, ("state", "horizon"), scatter_dimension=0, tiled=True)
    index = lax.axis_index(("state", "horizon"))
    held = full.reshape((count, full.shape[0] // count) + full.shape[1:])
    step = 1
    while step < count:
        if step < core_count:
            axis, size, flip = "horizon", core_count, step
        else:
            axis, size, flip = "state", state_count, step // core_count
        pairs = [(member, member ^ flip) for member in range(size)]
        bit = (index // step) % 2
        halves = held.reshape((held.shape[0] // 2, 2) + held.shape[1:])
        keep = jnp.where(bit == 1, halves[:, 1], halves[:, 0])
        send = jnp.where(bit == 1, halves[:, 0], halves[:, 1])
        held = keep + lax.ppermute(send, axis, pairs)
        step *= 2
    return held.reshape(held.shape[1:])


def split_product(rows_full, data_half):
    upper = rows_full.astype(jnp.bfloat16)
    remain = rows_full - upper.astype(jnp.float32)
    middle = remain.astype(jnp.bfloat16)
    lower = (remain - middle.astype(jnp.float32)).astype(jnp.bfloat16)
    total = jnp.dot(upper, data_half, preferred_element_type=jnp.float32)
    total = total + jnp.dot(middle, data_half, preferred_element_type=jnp.float32)
    return total + jnp.dot(lower, data_half, preferred_element_type=jnp.float32)


def shift_pairs(axis, step):
    count = lax.axis_size(axis)
    if step > 0:
        return [(i, i + 1) for i in range(count - 1)]
    return [(i + 1, i) for i in range(count - 1)]


def to_right(value):
    return lax.ppermute(value, ("state", "horizon"), shift_pairs(("state", "horizon"), 1))


def to_left(value):
    return lax.ppermute(value, ("state", "horizon"), shift_pairs(("state", "horizon"), -1))


def band_step(rows, moves):
    parts = jnp.einsum("cru,cduv->cdrv", rows, moves, precision=lax.Precision.HIGHEST)
    down, same, up = parts[:, 0], parts[:, 1], parts[:, 2]
    zero = jnp.zeros_like(same[:1])
    inner = same + jnp.concatenate([down[1:], zero], 0) + jnp.concatenate([zero, up[:-1]], 0)
    return inner, down[0], up[-1]


def mat(rows, matrix):
    return jnp.dot(rows, matrix, precision=lax.Precision.HIGHEST)


def ext_step(rows, moves):
    parts = jnp.einsum("cru,cduv->cdrv", rows, moves, precision=lax.Precision.HIGHEST)
    down, same, up = parts[:, 0], parts[:, 1], parts[:, 2]
    zero = jnp.zeros_like(same[:1])
    inner = same + jnp.concatenate([down[1:], zero], 0) + jnp.concatenate([zero, up[:-1]], 0)
    return inner, parts[1, 0], parts[-2, 2]


def exchange_round(rows, moves, wide, steps):
    zero = jnp.zeros_like(rows[:1])
    held = jnp.concatenate([zero, rows, zero], 0)
    to_low, to_high, mine = [], [], []
    for _ in range(steps):
        held, out_low, out_high = ext_step(held, wide)
        to_low.append(out_low)
        to_high.append(out_high)
        mine.append(held[1:-1])
    from_low = to_right(jnp.stack(to_high))
    from_high = to_left(jnp.stack(to_low))
    levels = []
    carried = None
    for step in range(steps):
        if carried is None:
            carried = jnp.zeros_like(rows)
        else:
            carried, _, _ = band_step(carried, moves)
        carried = carried.at[0].add(from_low[step]).at[-1].add(from_high[step])
        levels.append(mine[step] + carried)
    return levels


def shards(impulses, expectations, region_scale, regions, tiles, offsets, counts):
    block_count, band_count, tile_size, _ = tiles.shape
    state_count, input_count, horizon = impulses.shape
    output_count, expect_rows, _ = expectations.shape
    region_total = region_scale.shape[0]
    width = input_count * horizon
    sections = horizon // expect_rows
    row_count = output_count * expect_rows
    onehot = (regions[:, None] == jnp.arange(region_total, dtype=jnp.int32)[None, :]).astype(
        jnp.float32
    )
    block_scale = jnp.dot(
        onehot, region_scale, precision=lax.Precision.HIGHEST, preferred_element_type=jnp.float32
    )
    weighted = (
        expectations.astype(jnp.float32).reshape(output_count, expect_rows, block_count, tile_size)
        * block_scale.T[:, None, :, None]
    )
    weighted_half = weighted.astype(jnp.bfloat16).reshape(row_count, state_count)
    in_use = jnp.arange(band_count, dtype=jnp.int32)[None, :] < counts[:, None]
    scaling = lax.rsqrt(counts.astype(jnp.float32))
    shifts = jnp.arange(-1, 2, dtype=jnp.int32)
    chosen = in_use[:, :, None] & (offsets[:, :, None] == shifts[None, None, :])
    weight = chosen.astype(jnp.float32) * scaling[:, None, None]
    moves = jnp.sum(
        weight[:, :, :, None, None] * tiles.astype(jnp.float32)[:, :, None, :, :], axis=1
    )
    flat_start = impulses.reshape(state_count, width)
    rows = (
        weighted_half.astype(jnp.float32)
        .reshape(row_count, block_count, tile_size)
        .transpose(1, 0, 2)
    )
    inner, out_low, out_high = band_step(rows, moves)
    edge_low = jnp.concatenate([out_high, moves[-1, 1], moves[-1, 2]], 0)
    edge_high = jnp.concatenate([out_low, moves[0, 0], moves[0, 1]], 0)
    from_low = to_right(edge_low)
    from_high = to_left(edge_high)
    levels = [rows, inner.at[0].add(from_low[:row_count]).at[-1].add(from_high[:row_count])]
    left_self = from_low[row_count : row_count + tile_size]
    left_up = from_low[row_count + tile_size :]
    right_down = from_high[row_count : row_count + tile_size]
    right_self = from_high[row_count + tile_size :]
    blank = jnp.zeros_like(left_self)
    wide = jnp.concatenate(
        [
            jnp.stack([blank, left_self, left_up])[None],
            moves,
            jnp.stack([right_down, right_self, blank])[None],
        ],
        0,
    )
    remaining = sections - 2
    while remaining > 0:
        steps = min(3, remaining)
        levels += exchange_round(levels[-1], moves, wide, steps)
        remaining -= steps
    stacked = jnp.concatenate(
        [level.transpose(1, 0, 2).reshape(row_count, state_count) for level in levels], 0
    )
    product = split_product(stacked, flat_start)
    pieces = [
        piece.reshape(output_count, expect_rows, input_count, horizon).transpose(1, 0, 2, 3)
        for piece in jnp.split(product, sections, 0)
    ]
    partial_news = jnp.concatenate(pieces, axis=0)
    jacobian = diagonal_sums(partial_news)
    return halving_scatter(jacobian)


def solution(mesh):
    return jax.shard_map(
        shards,
        mesh=mesh,
        in_specs=(
            P(("state", "horizon"), "input", "groups"),
            P("groups", None, ("state", "horizon")),
            P("groups", None),
            P(("state", "horizon")),
            P(("state", "horizon"), None, None, None),
            P(("state", "horizon"), None),
            P(("state", "horizon")),
        ),
        out_specs=P(("state", "horizon"), "groups", "input", None),
        check_vma=False,
    )
```

```python
import jax
import jax.numpy as jnp
from jax import lax
from jax.sharding import PartitionSpec as P


def diagonal_sums(news):
    rows = news.shape[0]
    width = news.shape[-1]
    total = news
    shift = 1
    while shift < rows:
        moved = lax.pad(
            total[: rows - shift, ..., : width - shift],
            jnp.zeros((), total.dtype),
            [(shift, 0, 0)] + [(0, 0, 0)] * (total.ndim - 2) + [(shift, 0, 0)],
        )
        total = total + moved
        shift *= 2
    return total


def halving_scatter(full):
    state_count = lax.axis_size("state")
    core_count = lax.axis_size("horizon")
    count = state_count * core_count
    if count & (count - 1) or core_count & (core_count - 1):
        return lax.psum_scatter(full, ("state", "horizon"), scatter_dimension=0, tiled=True)
    index = lax.axis_index(("state", "horizon"))
    held = full.reshape((count, full.shape[0] // count) + full.shape[1:])
    step = 1
    while step < count:
        if step < core_count:
            axis, size, flip = "horizon", core_count, step
        else:
            axis, size, flip = "state", state_count, step // core_count
        pairs = [(member, member ^ flip) for member in range(size)]
        bit = (index // step) % 2
        halves = held.reshape((held.shape[0] // 2, 2) + held.shape[1:])
        keep = jnp.where(bit == 1, halves[:, 1], halves[:, 0])
        send = jnp.where(bit == 1, halves[:, 0], halves[:, 1])
        held = keep + lax.ppermute(send, axis, pairs)
        step *= 2
    return held.reshape(held.shape[1:])


def split_product(rows_full, data_half):
    upper = rows_full.astype(jnp.bfloat16)
    remain = rows_full - upper.astype(jnp.float32)
    middle = remain.astype(jnp.bfloat16)
    lower = (remain - middle.astype(jnp.float32)).astype(jnp.bfloat16)
    total = jnp.dot(upper, data_half, preferred_element_type=jnp.float32)
    total = total + jnp.dot(middle, data_half, preferred_element_type=jnp.float32)
    return total + jnp.dot(lower, data_half, preferred_element_type=jnp.float32)


def shift_pairs(axis, step):
    count = lax.axis_size(axis)
    if step > 0:
        return [(i, i + 1) for i in range(count - 1)]
    return [(i + 1, i) for i in range(count - 1)]


def to_right(value):
    return lax.ppermute(value, ("state", "horizon"), shift_pairs(("state", "horizon"), 1))


def to_left(value):
    return lax.ppermute(value, ("state", "horizon"), shift_pairs(("state", "horizon"), -1))


def band_step(rows, moves):
    parts = jnp.einsum("cru,cduv->cdrv", rows, moves, precision=lax.Precision.HIGH)
    down, same, up = parts[:, 0], parts[:, 1], parts[:, 2]
    zero = jnp.zeros_like(same[:1])
    inner = same + jnp.concatenate([down[1:], zero], 0) + jnp.concatenate([zero, up[:-1]], 0)
    return inner, down[0], up[-1]


def ext_step(rows, moves):
    parts = jnp.einsum("cru,cduv->cdrv", rows, moves, precision=lax.Precision.HIGH)
    down, same, up = parts[:, 0], parts[:, 1], parts[:, 2]
    zero = jnp.zeros_like(same[:1])
    inner = same + jnp.concatenate([down[1:], zero], 0) + jnp.concatenate([zero, up[:-1]], 0)
    return inner, parts[1, 0], parts[-2, 2]


def exchange_round(rows, moves, wide, steps):
    zero = jnp.zeros_like(rows[:1])
    held = jnp.concatenate([zero, rows, zero], 0)
    to_low, to_high, mine = [], [], []
    for _ in range(steps):
        held, out_low, out_high = ext_step(held, wide)
        to_low.append(out_low)
        to_high.append(out_high)
        mine.append(held[1:-1])
    from_low = to_right(jnp.stack(to_high))
    from_high = to_left(jnp.stack(to_low))
    levels = []
    carried = None
    for step in range(steps):
        if carried is None:
            carried = jnp.zeros_like(rows)
        else:
            carried, _, _ = band_step(carried, moves)
        carried = carried.at[0].add(from_low[step]).at[-1].add(from_high[step])
        levels.append(mine[step] + carried)
    return levels


def shards(impulses, expectations, region_scale, regions, tiles, offsets, counts):
    block_count, band_count, tile_size, _ = tiles.shape
    state_count, input_count, horizon = impulses.shape
    output_count, expect_rows, _ = expectations.shape
    region_total = region_scale.shape[0]
    width = input_count * horizon
    sections = horizon // expect_rows
    row_count = output_count * expect_rows
    onehot = (regions[:, None] == jnp.arange(region_total, dtype=jnp.int32)[None, :]).astype(
        jnp.float32
    )
    block_scale = jnp.dot(
        onehot, region_scale, precision=lax.Precision.HIGHEST, preferred_element_type=jnp.float32
    )
    weighted = (
        expectations.astype(jnp.float32).reshape(output_count, expect_rows, block_count, tile_size)
        * block_scale.T[:, None, :, None]
    )
    weighted_half = weighted.astype(jnp.bfloat16).reshape(row_count, state_count)
    in_use = jnp.arange(band_count, dtype=jnp.int32)[None, :] < counts[:, None]
    scaling = lax.rsqrt(counts.astype(jnp.float32))
    shifts = jnp.arange(-1, 2, dtype=jnp.int32)
    chosen = in_use[:, :, None] & (offsets[:, :, None] == shifts[None, None, :])
    moves = jnp.einsum(
        "cjd,cjuv->cduv",
        chosen.astype(jnp.bfloat16),
        tiles,
        preferred_element_type=jnp.float32,
    ) * scaling[:, None, None, None]
    flat_start = impulses.reshape(state_count, width)
    rows = (
        weighted_half.astype(jnp.float32)
        .reshape(row_count, block_count, tile_size)
        .transpose(1, 0, 2)
    )
    inner, out_low, out_high = band_step(rows, moves)
    edge_low = jnp.concatenate([out_high, moves[-1, 1], moves[-1, 2]], 0)
    edge_high = jnp.concatenate([out_low, moves[0, 0], moves[0, 1]], 0)
    from_low = to_right(edge_low)
    from_high = to_left(edge_high)
    levels = [rows, inner.at[0].add(from_low[:row_count]).at[-1].add(from_high[:row_count])]
    left_self = from_low[row_count : row_count + tile_size]
    left_up = from_low[row_count + tile_size :]
    right_down = from_high[row_count : row_count + tile_size]
    right_self = from_high[row_count + tile_size :]
    blank = jnp.zeros_like(left_self)
    wide = jnp.concatenate(
        [
            jnp.stack([blank, left_self, left_up])[None],
            moves,
            jnp.stack([right_down, right_self, blank])[None],
        ],
        0,
    )
    remaining = sections - 2
    while remaining > 0:
        steps = min(3, remaining)
        levels += exchange_round(levels[-1], moves, wide, steps)
        remaining -= steps
    stacked = jnp.concatenate(
        [level.transpose(1, 0, 2).reshape(row_count, state_count) for level in levels], 0
    )
    product = split_product(stacked, flat_start)
    pieces = [
        piece.reshape(output_count, expect_rows, input_count, horizon).transpose(1, 0, 2, 3)
        for piece in jnp.split(product, sections, 0)
    ]
    partial_news = jnp.concatenate(pieces, axis=0)
    jacobian = diagonal_sums(partial_news)
    return halving_scatter(jacobian)


def solution(mesh):
    return jax.shard_map(
        shards,
        mesh=mesh,
        in_specs=(
            P(("state", "horizon"), "input", "groups"),
            P("groups", None, ("state", "horizon")),
            P("groups", None),
            P(("state", "horizon")),
            P(("state", "horizon"), None, None, None),
            P(("state", "horizon"), None),
            P(("state", "horizon")),
        ),
        out_specs=P(("state", "horizon"), "groups", "input", None),
        check_vma=False,
    )
```

```python
import jax
import jax.numpy as jnp
from jax import lax
from jax.sharding import PartitionSpec as P


def diagonal_sums(news):
    rows = news.shape[0]
    width = news.shape[-1]
    total = news
    shift = 1
    while shift < rows:
        moved = lax.pad(
            total[: rows - shift, ..., : width - shift],
            jnp.zeros((), total.dtype),
            [(shift, 0, 0)] + [(0, 0, 0)] * (total.ndim - 2) + [(shift, 0, 0)],
        )
        total = total + moved
        shift *= 2
    return total


def halving_scatter(full):
    state_count = lax.axis_size("state")
    core_count = lax.axis_size("horizon")
    count = state_count * core_count
    if count & (count - 1) or core_count & (core_count - 1):
        return lax.psum_scatter(full, ("state", "horizon"), scatter_dimension=0, tiled=True)
    index = lax.axis_index(("state", "horizon"))
    held = full.reshape((count, full.shape[0] // count) + full.shape[1:])
    step = 1
    while step < count:
        if step < core_count:
            axis, size, flip = "horizon", core_count, step
        else:
            axis, size, flip = "state", state_count, step // core_count
        pairs = [(member, member ^ flip) for member in range(size)]
        bit = (index // step) % 2
        halves = held.reshape((held.shape[0] // 2, 2) + held.shape[1:])
        keep = jnp.where(bit == 1, halves[:, 1], halves[:, 0])
        send = jnp.where(bit == 1, halves[:, 0], halves[:, 1])
        held = keep + lax.ppermute(send, axis, pairs)
        step *= 2
    return held.reshape(held.shape[1:])


def split_product(rows_full, data_half):
    upper = rows_full.astype(jnp.bfloat16)
    remain = rows_full - upper.astype(jnp.float32)
    middle = remain.astype(jnp.bfloat16)
    lower = (remain - middle.astype(jnp.float32)).astype(jnp.bfloat16)
    total = jnp.dot(upper, data_half, preferred_element_type=jnp.float32)
    total = total + jnp.dot(middle, data_half, preferred_element_type=jnp.float32)
    return total + jnp.dot(lower, data_half, preferred_element_type=jnp.float32)


def shift_pairs(axis, step):
    count = lax.axis_size(axis)
    if step > 0:
        return [(i, i + 1) for i in range(count - 1)]
    return [(i + 1, i) for i in range(count - 1)]


def to_right(value):
    return lax.ppermute(value, ("state", "horizon"), shift_pairs(("state", "horizon"), 1))


def to_left(value):
    return lax.ppermute(value, ("state", "horizon"), shift_pairs(("state", "horizon"), -1))


def swap_edges(to_low, to_high):
    cores = lax.axis_size("horizon")
    if cores != 2:
        return to_right(to_high), to_left(to_low)
    count = lax.axis_size(("state", "horizon"))
    first = lax.axis_index("horizon") == 0
    on_chip = lax.ppermute(jnp.where(first, to_high, to_low), "horizon", [(0, 1), (1, 0)])
    pairs = []
    for chip in range(count // 2 - 1):
        pairs += [(2 * chip + 1, 2 * chip + 2), (2 * chip + 2, 2 * chip + 1)]
    across = lax.ppermute(jnp.where(first, to_low, to_high), ("state", "horizon"), pairs)
    return jnp.where(first, across, on_chip), jnp.where(first, on_chip, across)


def band_step(rows, moves):
    parts = jnp.einsum("cru,cduv->cdrv", rows, moves, precision=lax.Precision.HIGH)
    down, same, up = parts[:, 0], parts[:, 1], parts[:, 2]
    zero = jnp.zeros_like(same[:1])
    inner = same + jnp.concatenate([down[1:], zero], 0) + jnp.concatenate([zero, up[:-1]], 0)
    return inner, down[0], up[-1]


def ext_step(rows, moves):
    parts = jnp.einsum("cru,cduv->cdrv", rows, moves, precision=lax.Precision.HIGH)
    down, same, up = parts[:, 0], parts[:, 1], parts[:, 2]
    zero = jnp.zeros_like(same[:1])
    inner = same + jnp.concatenate([down[1:], zero], 0) + jnp.concatenate([zero, up[:-1]], 0)
    return inner, parts[1, 0], parts[-2, 2]


def exchange_round(rows, moves, wide, steps):
    zero = jnp.zeros_like(rows[:1])
    held = jnp.concatenate([zero, rows, zero], 0)
    to_low, to_high, mine = [], [], []
    for _ in range(steps):
        held, out_low, out_high = ext_step(held, wide)
        to_low.append(out_low)
        to_high.append(out_high)
        mine.append(held[1:-1])
    from_low, from_high = swap_edges(jnp.stack(to_low), jnp.stack(to_high))
    levels = []
    carried = None
    for step in range(steps):
        if carried is None:
            carried = jnp.zeros_like(rows)
        else:
            carried, _, _ = band_step(carried, moves)
        carried = carried.at[0].add(from_low[step]).at[-1].add(from_high[step])
        levels.append(mine[step] + carried)
    return levels


def shards(impulses, expectations, region_scale, regions, tiles, offsets, counts):
    block_count, band_count, tile_size, _ = tiles.shape
    state_count, input_count, horizon = impulses.shape
    output_count, expect_rows, _ = expectations.shape
    region_total = region_scale.shape[0]
    width = input_count * horizon
    sections = horizon // expect_rows
    row_count = output_count * expect_rows
    onehot = (regions[:, None] == jnp.arange(region_total, dtype=jnp.int32)[None, :]).astype(
        jnp.float32
    )
    block_scale = jnp.sum(jnp.where(onehot[:, :, None] > 0, region_scale[None], 0.0), axis=1)
    weighted = (
        expectations.astype(jnp.float32).reshape(output_count, expect_rows, block_count, tile_size)
        * block_scale.T[:, None, :, None]
    )
    weighted_half = weighted.astype(jnp.bfloat16).reshape(row_count, state_count)
    in_use = jnp.arange(band_count, dtype=jnp.int32)[None, :] < counts[:, None]
    scaling = lax.rsqrt(counts.astype(jnp.float32))
    shifts = jnp.arange(-1, 2, dtype=jnp.int32)
    chosen = in_use[:, :, None] & (offsets[:, :, None] == shifts[None, None, :])
    moves = jnp.einsum(
        "cjd,cjuv->cduv",
        chosen.astype(jnp.bfloat16),
        tiles,
        preferred_element_type=jnp.float32,
    ) * scaling[:, None, None, None]
    flat_start = impulses.reshape(state_count, width)
    rows = (
        weighted_half.astype(jnp.float32)
        .reshape(row_count, block_count, tile_size)
        .transpose(1, 0, 2)
    )
    inner, out_low, out_high = band_step(rows, moves)
    edge_low = jnp.concatenate([out_high, moves[-1, 1], moves[-1, 2]], 0)
    edge_high = jnp.concatenate([out_low, moves[0, 0], moves[0, 1]], 0)
    from_low, from_high = swap_edges(edge_high, edge_low)
    levels = [rows, inner.at[0].add(from_low[:row_count]).at[-1].add(from_high[:row_count])]
    left_self = from_low[row_count : row_count + tile_size]
    left_up = from_low[row_count + tile_size :]
    right_down = from_high[row_count : row_count + tile_size]
    right_self = from_high[row_count + tile_size :]
    blank = jnp.zeros_like(left_self)
    wide = jnp.concatenate(
        [
            jnp.stack([blank, left_self, left_up])[None],
            moves,
            jnp.stack([right_down, right_self, blank])[None],
        ],
        0,
    )
    remaining = sections - 2
    while remaining > 0:
        steps = min(3, remaining)
        levels += exchange_round(levels[-1], moves, wide, steps)
        remaining -= steps
    stacked = jnp.concatenate(
        [level.transpose(1, 0, 2).reshape(row_count, state_count) for level in levels], 0
    )
    product = split_product(stacked, flat_start)
    pieces = [
        piece.reshape(output_count, expect_rows, input_count, horizon).transpose(1, 0, 2, 3)
        for piece in jnp.split(product, sections, 0)
    ]
    partial_news = jnp.concatenate(pieces, axis=0)
    jacobian = diagonal_sums(partial_news)
    return halving_scatter(jacobian)


def solution(mesh):
    return jax.shard_map(
        shards,
        mesh=mesh,
        in_specs=(
            P(("state", "horizon"), "input", "groups"),
            P("groups", None, ("state", "horizon")),
            P("groups", None),
            P(("state", "horizon")),
            P(("state", "horizon"), None, None, None),
            P(("state", "horizon"), None),
            P(("state", "horizon")),
        ),
        out_specs=P(("state", "horizon"), "groups", "input", None),
        check_vma=False,
    )
```

```python
import jax
import jax.numpy as jnp
from jax import lax
from jax.sharding import PartitionSpec as P
from jax.experimental import pallas as pl
from jax.experimental.pallas import tpu as pltpu


def diagonal_sums(news):
    rows = news.shape[0]
    width = news.shape[-1]
    total = news
    shift = 1
    while shift < rows:
        moved = lax.pad(
            total[: rows - shift, ..., : width - shift],
            jnp.zeros((), total.dtype),
            [(shift, 0, 0)] + [(0, 0, 0)] * (total.ndim - 2) + [(shift, 0, 0)],
        )
        total = total + moved
        shift *= 2
    return total


def halving_scatter(full):
    state_count = lax.axis_size("state")
    core_count = lax.axis_size("horizon")
    count = state_count * core_count
    if count & (count - 1) or core_count & (core_count - 1):
        return lax.psum_scatter(full, ("state", "horizon"), scatter_dimension=0, tiled=True)
    index = lax.axis_index(("state", "horizon"))
    held = full.reshape((count, full.shape[0] // count) + full.shape[1:])
    step = 1
    while step < count:
        if step < core_count:
            axis, size, flip = "horizon", core_count, step
        else:
            axis, size, flip = "state", state_count, step // core_count
        pairs = [(member, member ^ flip) for member in range(size)]
        bit = (index // step) % 2
        halves = held.reshape((held.shape[0] // 2, 2) + held.shape[1:])
        keep = jnp.where(bit == 1, halves[:, 1], halves[:, 0])
        send = jnp.where(bit == 1, halves[:, 0], halves[:, 1])
        held = keep + lax.ppermute(send, axis, pairs)
        step *= 2
    return held.reshape(held.shape[1:])


def prepare_kernel(counts, offsets, regions, scales, tiles, expect, moves, rows):
    block_count, band_count, tile_size, _ = tiles.shape
    output_count, expect_rows, _ = expect.shape
    for block in range(block_count):
        count = counts[block]
        scale = lax.rsqrt(jnp.full((1, tile_size), count.astype(jnp.float32), jnp.float32))
        for shift in range(3):
            total = jnp.zeros((tile_size, tile_size), jnp.float32)
            for slot in range(band_count):
                use = jnp.logical_and(slot < count, offsets[block, slot] == shift - 1)
                weight = jnp.where(use, 1.0, 0.0).astype(jnp.float32)
                total = total + weight * tiles[block, slot].astype(jnp.float32)
            moves[block, shift] = total * scale
        region = regions[block]
        for out in range(output_count):
            part = expect[out, :, block * tile_size : (block + 1) * tile_size]
            weighted = part.astype(jnp.float32) * scales[region, out]
            rows[block, out * expect_rows : (out + 1) * expect_rows, :] = weighted.astype(
                jnp.bfloat16
            ).astype(jnp.float32)


def prepare(counts, offsets, regions, region_scale, tiles, expectations):
    block_count, band_count, tile_size, _ = tiles.shape
    output_count, expect_rows, _ = expectations.shape
    smem = pl.BlockSpec(memory_space=pltpu.SMEM)
    vmem = pl.BlockSpec(memory_space=pltpu.VMEM)
    return pl.pallas_call(
        prepare_kernel,
        out_shape=(
            jax.ShapeDtypeStruct((block_count, 3, tile_size, tile_size), jnp.float32),
            jax.ShapeDtypeStruct((block_count, output_count * expect_rows, tile_size), jnp.float32),
        ),
        in_specs=[smem, smem, smem, smem, vmem, vmem],
        out_specs=(vmem, vmem),
    )(counts, offsets, regions, region_scale, tiles, expectations)


def split_product(rows_full, data_half):
    upper = rows_full.astype(jnp.bfloat16)
    remain = rows_full - upper.astype(jnp.float32)
    middle = remain.astype(jnp.bfloat16)
    lower = (remain - middle.astype(jnp.float32)).astype(jnp.bfloat16)
    total = jnp.dot(upper, data_half, preferred_element_type=jnp.float32)
    total = total + jnp.dot(middle, data_half, preferred_element_type=jnp.float32)
    return total + jnp.dot(lower, data_half, preferred_element_type=jnp.float32)


def shift_pairs(axis, step):
    count = lax.axis_size(axis)
    if step > 0:
        return [(i, i + 1) for i in range(count - 1)]
    return [(i + 1, i) for i in range(count - 1)]


def to_right(value):
    return lax.ppermute(value, ("state", "horizon"), shift_pairs(("state", "horizon"), 1))


def to_left(value):
    return lax.ppermute(value, ("state", "horizon"), shift_pairs(("state", "horizon"), -1))


def swap_edges(to_low, to_high):
    cores = lax.axis_size("horizon")
    if cores != 2:
        return to_right(to_high), to_left(to_low)
    count = lax.axis_size(("state", "horizon"))
    first = lax.axis_index("horizon") == 0
    on_chip = lax.ppermute(jnp.where(first, to_high, to_low), "horizon", [(0, 1), (1, 0)])
    pairs = []
    for chip in range(count // 2 - 1):
        pairs += [(2 * chip + 1, 2 * chip + 2), (2 * chip + 2, 2 * chip + 1)]
    across = lax.ppermute(jnp.where(first, to_low, to_high), ("state", "horizon"), pairs)
    return jnp.where(first, across, on_chip), jnp.where(first, on_chip, across)


def band_step(rows, moves):
    parts = jnp.einsum("cru,cduv->cdrv", rows, moves, precision=lax.Precision.HIGH)
    down, same, up = parts[:, 0], parts[:, 1], parts[:, 2]
    zero = jnp.zeros_like(same[:1])
    inner = same + jnp.concatenate([down[1:], zero], 0) + jnp.concatenate([zero, up[:-1]], 0)
    return inner, down[0], up[-1]


def ext_step(rows, moves):
    parts = jnp.einsum("cru,cduv->cdrv", rows, moves, precision=lax.Precision.HIGH)
    down, same, up = parts[:, 0], parts[:, 1], parts[:, 2]
    zero = jnp.zeros_like(same[:1])
    inner = same + jnp.concatenate([down[1:], zero], 0) + jnp.concatenate([zero, up[:-1]], 0)
    return inner, parts[1, 0], parts[-2, 2]


def exchange_round(rows, moves, wide, steps):
    zero = jnp.zeros_like(rows[:1])
    held = jnp.concatenate([zero, rows, zero], 0)
    to_low, to_high, mine = [], [], []
    for _ in range(steps):
        held, out_low, out_high = ext_step(held, wide)
        to_low.append(out_low)
        to_high.append(out_high)
        mine.append(held[1:-1])
    from_low, from_high = swap_edges(jnp.stack(to_low), jnp.stack(to_high))
    levels = []
    carried = None
    for step in range(steps):
        if carried is None:
            carried = jnp.zeros_like(rows)
        else:
            carried, _, _ = band_step(carried, moves)
        carried = carried.at[0].add(from_low[step]).at[-1].add(from_high[step])
        levels.append(mine[step] + carried)
    return levels


def shards(impulses, expectations, region_scale, regions, tiles, offsets, counts):
    block_count, band_count, tile_size, _ = tiles.shape
    state_count, input_count, horizon = impulses.shape
    output_count, expect_rows, _ = expectations.shape
    region_total = region_scale.shape[0]
    width = input_count * horizon
    sections = horizon // expect_rows
    row_count = output_count * expect_rows
    moves, rows = prepare(counts, offsets, regions, region_scale, tiles, expectations)
    flat_start = impulses.reshape(state_count, width)
    inner, out_low, out_high = band_step(rows, moves)
    edge_low = jnp.concatenate([out_high, moves[-1, 1], moves[-1, 2]], 0)
    edge_high = jnp.concatenate([out_low, moves[0, 0], moves[0, 1]], 0)
    from_low, from_high = swap_edges(edge_high, edge_low)
    levels = [rows, inner.at[0].add(from_low[:row_count]).at[-1].add(from_high[:row_count])]
    left_self = from_low[row_count : row_count + tile_size]
    left_up = from_low[row_count + tile_size :]
    right_down = from_high[row_count : row_count + tile_size]
    right_self = from_high[row_count + tile_size :]
    blank = jnp.zeros_like(left_self)
    wide = jnp.concatenate(
        [
            jnp.stack([blank, left_self, left_up])[None],
            moves,
            jnp.stack([right_down, right_self, blank])[None],
        ],
        0,
    )
    remaining = sections - 2
    while remaining > 0:
        steps = min(3, remaining)
        levels += exchange_round(levels[-1], moves, wide, steps)
        remaining -= steps
    stacked = jnp.concatenate(
        [level.transpose(1, 0, 2).reshape(row_count, state_count) for level in levels], 0
    )
    product = split_product(stacked, flat_start)
    pieces = [
        piece.reshape(output_count, expect_rows, input_count, horizon).transpose(1, 0, 2, 3)
        for piece in jnp.split(product, sections, 0)
    ]
    partial_news = jnp.concatenate(pieces, axis=0)
    jacobian = diagonal_sums(partial_news)
    return halving_scatter(jacobian)


def solution(mesh):
    return jax.shard_map(
        shards,
        mesh=mesh,
        in_specs=(
            P(("state", "horizon"), "input", "groups"),
            P("groups", None, ("state", "horizon")),
            P("groups", None),
            P(("state", "horizon")),
            P(("state", "horizon"), None, None, None),
            P(("state", "horizon"), None),
            P(("state", "horizon")),
        ),
        out_specs=P(("state", "horizon"), "groups", "input", None),
        check_vma=False,
    )
```

```python
import jax
import jax.numpy as jnp
from jax import lax
from jax.sharding import PartitionSpec as P
from jax.experimental import pallas as pl
from jax.experimental.pallas import tpu as pltpu


def diagonal_sums(news):
    rows = news.shape[0]
    width = news.shape[-1]
    total = news
    shift = 1
    while shift < rows:
        moved = lax.pad(
            total[: rows - shift, ..., : width - shift],
            jnp.zeros((), total.dtype),
            [(shift, 0, 0)] + [(0, 0, 0)] * (total.ndim - 2) + [(shift, 0, 0)],
        )
        total = total + moved
        shift *= 2
    return total


def halving_scatter(full):
    state_count = lax.axis_size("state")
    core_count = lax.axis_size("horizon")
    count = state_count * core_count
    if count & (count - 1) or core_count & (core_count - 1):
        return lax.psum_scatter(full, ("state", "horizon"), scatter_dimension=0, tiled=True)
    index = lax.axis_index(("state", "horizon"))
    held = full.reshape((count, full.shape[0] // count) + full.shape[1:])
    step = 1
    while step < count:
        if step < core_count:
            axis, size, flip = "horizon", core_count, step
        else:
            axis, size, flip = "state", state_count, step // core_count
        pairs = [(member, member ^ flip) for member in range(size)]
        bit = (index // step) % 2
        halves = held.reshape((held.shape[0] // 2, 2) + held.shape[1:])
        keep = jnp.where(bit == 1, halves[:, 1], halves[:, 0])
        send = jnp.where(bit == 1, halves[:, 0], halves[:, 1])
        held = keep + lax.ppermute(send, axis, pairs)
        step *= 2
    return held.reshape(held.shape[1:])


def prepare_kernel(counts, offsets, regions, scales, tiles, expect, moves, rows, edges):
    block_count, band_count, tile_size, _ = tiles.shape
    output_count, expect_rows, _ = expect.shape
    for block in range(block_count):
        count = counts[block]
        scale = lax.rsqrt(jnp.full((1, tile_size), count.astype(jnp.float32), jnp.float32))
        wide = [tiles[block, slot].astype(jnp.float32) for slot in range(band_count)]
        for shift in range(3):
            total = jnp.zeros((tile_size, tile_size), jnp.float32)
            for slot in range(band_count):
                use = jnp.logical_and(slot < count, offsets[block, slot] == shift - 1)
                total = total + jnp.where(use, 1.0, 0.0).astype(jnp.float32) * wide[slot]
            total = total * scale
            moves[block, :, shift * tile_size : (shift + 1) * tile_size] = total
            if block == block_count - 1 and shift > 0:
                edges[0, (shift - 1) * tile_size : shift * tile_size, :] = total
            if block == 0 and shift < 2:
                edges[1, shift * tile_size : (shift + 1) * tile_size, :] = total
        region = regions[block]
        for out in range(output_count):
            part = expect[out, :, block * tile_size : (block + 1) * tile_size]
            weighted = part.astype(jnp.float32) * scales[out, region]
            rows[block, out * expect_rows : (out + 1) * expect_rows, :] = weighted.astype(
                jnp.bfloat16
            ).astype(jnp.float32)


def prepare(counts, offsets, regions, region_scale, tiles, expectations):
    block_count, band_count, tile_size, _ = tiles.shape
    output_count, expect_rows, _ = expectations.shape
    smem = pl.BlockSpec(memory_space=pltpu.SMEM)
    vmem = pl.BlockSpec(memory_space=pltpu.VMEM)
    return pl.pallas_call(
        prepare_kernel,
        out_shape=(
            jax.ShapeDtypeStruct((block_count, tile_size, 3 * tile_size), jnp.float32),
            jax.ShapeDtypeStruct((block_count, output_count * expect_rows, tile_size), jnp.float32),
            jax.ShapeDtypeStruct((2, 2 * tile_size, tile_size), jnp.float32),
        ),
        in_specs=[smem, smem, smem, smem, vmem, vmem],
        out_specs=(vmem, vmem, vmem),
    )(counts, offsets, regions, region_scale.T, tiles, expectations)


def split_product(rows_full, data_half):
    upper = rows_full.astype(jnp.bfloat16)
    remain = rows_full - upper.astype(jnp.float32)
    middle = remain.astype(jnp.bfloat16)
    lower = (remain - middle.astype(jnp.float32)).astype(jnp.bfloat16)
    total = jnp.dot(upper, data_half, preferred_element_type=jnp.float32)
    total = total + jnp.dot(middle, data_half, preferred_element_type=jnp.float32)
    return total + jnp.dot(lower, data_half, preferred_element_type=jnp.float32)


def shift_pairs(axis, step):
    count = lax.axis_size(axis)
    if step > 0:
        return [(i, i + 1) for i in range(count - 1)]
    return [(i + 1, i) for i in range(count - 1)]


def to_right(value):
    return lax.ppermute(value, ("state", "horizon"), shift_pairs(("state", "horizon"), 1))


def to_left(value):
    return lax.ppermute(value, ("state", "horizon"), shift_pairs(("state", "horizon"), -1))


def swap_edges(to_low, to_high):
    cores = lax.axis_size("horizon")
    if cores != 2:
        return to_right(to_high), to_left(to_low)
    count = lax.axis_size(("state", "horizon"))
    first = lax.axis_index("horizon") == 0
    on_chip = lax.ppermute(jnp.where(first, to_high, to_low), "horizon", [(0, 1), (1, 0)])
    pairs = []
    for chip in range(count // 2 - 1):
        pairs += [(2 * chip + 1, 2 * chip + 2), (2 * chip + 2, 2 * chip + 1)]
    across = lax.ppermute(jnp.where(first, to_low, to_high), ("state", "horizon"), pairs)
    return jnp.where(first, across, on_chip), jnp.where(first, on_chip, across)


def band_parts(rows, moves):
    parts = jnp.einsum("cru,cun->crn", rows, moves, precision=lax.Precision.HIGH)
    size = rows.shape[-1]
    down, same, up = parts[..., :size], parts[..., size : 2 * size], parts[..., 2 * size :]
    zero = jnp.zeros_like(same[:1])
    inner = same + jnp.concatenate([down[1:], zero], 0) + jnp.concatenate([zero, up[:-1]], 0)
    return inner, down, up


def band_step(rows, moves):
    inner, down, up = band_parts(rows, moves)
    return inner, down[0], up[-1]


def ext_step(rows, moves):
    inner, down, up = band_parts(rows, moves)
    return inner, down[1], up[-2]


def exchange_round(rows, moves, wide, steps):
    zero = jnp.zeros_like(rows[:1])
    held = jnp.concatenate([zero, rows, zero], 0)
    to_low, to_high, mine = [], [], []
    for _ in range(steps):
        held, out_low, out_high = ext_step(held, wide)
        to_low.append(out_low)
        to_high.append(out_high)
        mine.append(held[1:-1])
    from_low, from_high = swap_edges(jnp.stack(to_low), jnp.stack(to_high))
    levels = []
    carried = None
    for step in range(steps):
        if carried is None:
            carried = jnp.zeros_like(rows)
        else:
            carried, _, _ = band_step(carried, moves)
        carried = carried.at[0].add(from_low[step]).at[-1].add(from_high[step])
        levels.append(mine[step] + carried)
    return levels


def shards(impulses, expectations, region_scale, regions, tiles, offsets, counts):
    block_count, band_count, tile_size, _ = tiles.shape
    state_count, input_count, horizon = impulses.shape
    output_count, expect_rows, _ = expectations.shape
    region_total = region_scale.shape[0]
    width = input_count * horizon
    sections = horizon // expect_rows
    row_count = output_count * expect_rows
    moves, rows, edges = prepare(counts, offsets, regions, region_scale, tiles, expectations)
    flat_start = impulses.reshape(state_count, width)
    inner, out_low, out_high = band_step(rows, moves)
    edge_low = jnp.concatenate([out_high, edges[0]], 0)
    edge_high = jnp.concatenate([out_low, edges[1]], 0)
    from_low, from_high = swap_edges(edge_high, edge_low)
    levels = [rows, inner.at[0].add(from_low[:row_count]).at[-1].add(from_high[:row_count])]
    left_self = from_low[row_count : row_count + tile_size]
    left_up = from_low[row_count + tile_size :]
    right_down = from_high[row_count : row_count + tile_size]
    right_self = from_high[row_count + tile_size :]
    blank = jnp.zeros_like(left_self)
    wide = jnp.concatenate(
        [
            jnp.concatenate([blank, left_self, left_up], 1)[None],
            moves,
            jnp.concatenate([right_down, right_self, blank], 1)[None],
        ],
        0,
    )
    remaining = sections - 2
    while remaining > 0:
        steps = min(3, remaining)
        levels += exchange_round(levels[-1], moves, wide, steps)
        remaining -= steps
    stacked = jnp.concatenate(
        [level.transpose(1, 0, 2).reshape(row_count, state_count) for level in levels], 0
    )
    product = split_product(stacked, flat_start)
    pieces = [
        piece.reshape(output_count, expect_rows, input_count, horizon).transpose(1, 0, 2, 3)
        for piece in jnp.split(product, sections, 0)
    ]
    partial_news = jnp.concatenate(pieces, axis=0)
    jacobian = diagonal_sums(partial_news)
    return halving_scatter(jacobian)


def solution(mesh):
    return jax.shard_map(
        shards,
        mesh=mesh,
        in_specs=(
            P(("state", "horizon"), "input", "groups"),
            P("groups", None, ("state", "horizon")),
            P("groups", None),
            P(("state", "horizon")),
            P(("state", "horizon"), None, None, None),
            P(("state", "horizon"), None),
            P(("state", "horizon")),
        ),
        out_specs=P(("state", "horizon"), "groups", "input", None),
        check_vma=False,
    )
```

```python
import jax
import jax.numpy as jnp
from jax import lax
from jax.sharding import PartitionSpec as P
from jax.experimental import pallas as pl
from jax.experimental.pallas import tpu as pltpu


def diagonal_sums(news):
    rows = news.shape[0]
    width = news.shape[-1]
    total = news
    stride = 1
    while stride < rows:
        summed = total
        for step in range(1, 8):
            shift = step * stride
            if shift >= rows:
                break
            summed = summed + lax.pad(
                total[: rows - shift, ..., : max(width - shift, 0)],
                jnp.zeros((), total.dtype),
                [(shift, 0, 0)] + [(0, 0, 0)] * (total.ndim - 2) + [(min(shift, width), 0, 0)],
            )
        total = summed
        stride *= 8
    return total


def halving_scatter(full):
    state_count = lax.axis_size("state")
    core_count = lax.axis_size("horizon")
    count = state_count * core_count
    if count & (count - 1) or core_count & (core_count - 1):
        return lax.psum_scatter(full, ("state", "horizon"), scatter_dimension=0, tiled=True)
    index = lax.axis_index(("state", "horizon"))
    held = full.reshape((count, full.shape[0] // count) + full.shape[1:])
    step = 1
    while step < count:
        if step < core_count:
            axis, size, flip = "horizon", core_count, step
        else:
            axis, size, flip = "state", state_count, step // core_count
        pairs = [(member, member ^ flip) for member in range(size)]
        bit = (index // step) % 2
        halves = held.reshape((held.shape[0] // 2, 2) + held.shape[1:])
        keep = jnp.where(bit == 1, halves[:, 1], halves[:, 0])
        send = jnp.where(bit == 1, halves[:, 0], halves[:, 1])
        held = keep + lax.ppermute(send, axis, pairs)
        step *= 2
    return held.reshape(held.shape[1:])


def prepare_kernel(counts, offsets, regions, scales, tiles, expect, moves, rows, inner, up, down):
    block_count, band_count, tile_size, _ = tiles.shape
    output_count, expect_rows, _ = expect.shape
    row_count = output_count * expect_rows
    parts = []
    for block in range(block_count):
        count = counts[block]
        scale = lax.rsqrt(jnp.full((1, tile_size), count.astype(jnp.float32), jnp.float32))
        region = regions[block]
        pieces = []
        for out in range(output_count):
            part = expect[out, :, block * tile_size : (block + 1) * tile_size]
            pieces.append((part.astype(jnp.float32) * scales[out, region]).astype(jnp.bfloat16))
        half = jnp.concatenate(pieces, 0)
        rows[block] = half.astype(jnp.float32)
        carried = [
            jnp.dot(half, tiles[block, slot], preferred_element_type=jnp.float32)
            for slot in range(band_count)
        ]
        wide = [tiles[block, slot].astype(jnp.float32) for slot in range(band_count)]
        block_parts = []
        for shift in range(3):
            total = jnp.zeros((tile_size, tile_size), jnp.float32)
            flow = jnp.zeros((row_count, tile_size), jnp.float32)
            for slot in range(band_count):
                use = jnp.logical_and(slot < count, offsets[block, slot] == shift - 1)
                weight = jnp.where(use, 1.0, 0.0).astype(jnp.float32)
                total = total + weight * wide[slot]
                flow = flow + weight * carried[slot]
            total = total * scale
            moves[block, :, shift * tile_size : (shift + 1) * tile_size] = total
            block_parts.append(flow * scale)
            if block == block_count - 1 and shift > 0:
                up[row_count + (shift - 1) * tile_size : row_count + shift * tile_size, :] = total
            if block == 0 and shift < 2:
                down[row_count + shift * tile_size : row_count + (shift + 1) * tile_size, :] = total
        parts.append(block_parts)
    for block in range(block_count):
        total = parts[block][1]
        if block + 1 < block_count:
            total = total + parts[block + 1][0]
        if block > 0:
            total = total + parts[block - 1][2]
        inner[block] = total
    up[:row_count, :] = parts[-1][2]
    down[:row_count, :] = parts[0][0]


def prepare(counts, offsets, regions, region_scale, tiles, expectations):
    block_count, band_count, tile_size, _ = tiles.shape
    output_count, expect_rows, _ = expectations.shape
    row_count = output_count * expect_rows
    smem = pl.BlockSpec(memory_space=pltpu.SMEM)
    vmem = pl.BlockSpec(memory_space=pltpu.VMEM)
    edge = jax.ShapeDtypeStruct((row_count + 2 * tile_size, tile_size), jnp.float32)
    return pl.pallas_call(
        prepare_kernel,
        out_shape=(
            jax.ShapeDtypeStruct((block_count, tile_size, 3 * tile_size), jnp.float32),
            jax.ShapeDtypeStruct((block_count, row_count, tile_size), jnp.float32),
            jax.ShapeDtypeStruct((block_count, row_count, tile_size), jnp.float32),
            edge,
            edge,
        ),
        in_specs=[smem, smem, smem, smem, vmem, vmem],
        out_specs=(vmem, vmem, vmem, vmem, vmem),
    )(counts, offsets, regions, region_scale.T, tiles, expectations)


def split_product(rows_full, data_half):
    upper = rows_full.astype(jnp.bfloat16)
    remain = rows_full - upper.astype(jnp.float32)
    middle = remain.astype(jnp.bfloat16)
    lower = (remain - middle.astype(jnp.float32)).astype(jnp.bfloat16)
    total = jnp.dot(upper, data_half, preferred_element_type=jnp.float32)
    total = total + jnp.dot(middle, data_half, preferred_element_type=jnp.float32)
    return total + jnp.dot(lower, data_half, preferred_element_type=jnp.float32)


def shift_pairs(axis, step):
    count = lax.axis_size(axis)
    if step > 0:
        return [(i, i + 1) for i in range(count - 1)]
    return [(i + 1, i) for i in range(count - 1)]


def to_right(value):
    return lax.ppermute(value, ("state", "horizon"), shift_pairs(("state", "horizon"), 1))


def to_left(value):
    return lax.ppermute(value, ("state", "horizon"), shift_pairs(("state", "horizon"), -1))


def swap_edges(to_low, to_high):
    cores = lax.axis_size("horizon")
    if cores != 2:
        return to_right(to_high), to_left(to_low)
    count = lax.axis_size(("state", "horizon"))
    first = lax.axis_index("horizon") == 0
    on_chip = lax.ppermute(jnp.where(first, to_high, to_low), "horizon", [(0, 1), (1, 0)])
    pairs = []
    for chip in range(count // 2 - 1):
        pairs += [(2 * chip + 1, 2 * chip + 2), (2 * chip + 2, 2 * chip + 1)]
    across = lax.ppermute(jnp.where(first, to_low, to_high), ("state", "horizon"), pairs)
    return jnp.where(first, across, on_chip), jnp.where(first, on_chip, across)


def band_parts(rows, moves):
    parts = jnp.einsum("cru,cun->crn", rows, moves, precision=lax.Precision.HIGH)
    size = rows.shape[-1]
    down, same, up = parts[..., :size], parts[..., size : 2 * size], parts[..., 2 * size :]
    zero = jnp.zeros_like(same[:1])
    inner = same + jnp.concatenate([down[1:], zero], 0) + jnp.concatenate([zero, up[:-1]], 0)
    return inner, down, up


def band_step(rows, moves):
    inner, down, up = band_parts(rows, moves)
    return inner, down[0], up[-1]


def ext_step(rows, moves):
    inner, down, up = band_parts(rows, moves)
    return inner, down[1], up[-2]


def exchange_round(rows, moves, wide, steps):
    zero = jnp.zeros_like(rows[:1])
    held = jnp.concatenate([zero, rows, zero], 0)
    to_low, to_high, mine = [], [], []
    for _ in range(steps):
        held, out_low, out_high = ext_step(held, wide)
        to_low.append(out_low)
        to_high.append(out_high)
        mine.append(held[1:-1])
    from_low, from_high = swap_edges(jnp.stack(to_low), jnp.stack(to_high))
    levels = []
    carried = None
    for step in range(steps):
        if carried is None:
            carried = jnp.zeros_like(rows)
        else:
            carried, _, _ = band_step(carried, moves)
        carried = carried.at[0].add(from_low[step]).at[-1].add(from_high[step])
        levels.append(mine[step] + carried)
    return levels


def shards(impulses, expectations, region_scale, regions, tiles, offsets, counts):
    block_count, band_count, tile_size, _ = tiles.shape
    state_count, input_count, horizon = impulses.shape
    output_count, expect_rows, _ = expectations.shape
    region_total = region_scale.shape[0]
    width = input_count * horizon
    sections = horizon // expect_rows
    row_count = output_count * expect_rows
    moves, rows, inner, edge_low, edge_high = prepare(
        counts, offsets, regions, region_scale, tiles, expectations
    )
    flat_start = impulses.reshape(state_count, width)
    from_low, from_high = swap_edges(edge_high, edge_low)
    levels = [rows, inner.at[0].add(from_low[:row_count]).at[-1].add(from_high[:row_count])]
    left_self = from_low[row_count : row_count + tile_size]
    left_up = from_low[row_count + tile_size :]
    right_down = from_high[row_count : row_count + tile_size]
    right_self = from_high[row_count + tile_size :]
    blank = jnp.zeros_like(left_self)
    wide = jnp.concatenate(
        [
            jnp.concatenate([blank, left_self, left_up], 1)[None],
            moves,
            jnp.concatenate([right_down, right_self, blank], 1)[None],
        ],
        0,
    )
    remaining = sections - 2
    while remaining > 0:
        steps = min(3, remaining)
        levels += exchange_round(levels[-1], moves, wide, steps)
        remaining -= steps
    stacked = jnp.concatenate(
        [level.transpose(1, 0, 2).reshape(row_count, state_count) for level in levels], 0
    )
    product = split_product(stacked, flat_start)
    pieces = [
        piece.reshape(output_count, expect_rows, input_count, horizon).transpose(1, 0, 2, 3)
        for piece in jnp.split(product, sections, 0)
    ]
    partial_news = jnp.concatenate(pieces, axis=0)
    jacobian = diagonal_sums(partial_news)
    return halving_scatter(jacobian)


def solution(mesh):
    return jax.shard_map(
        shards,
        mesh=mesh,
        in_specs=(
            P(("state", "horizon"), "input", "groups"),
            P("groups", None, ("state", "horizon")),
            P("groups", None),
            P(("state", "horizon")),
            P(("state", "horizon"), None, None, None),
            P(("state", "horizon"), None),
            P(("state", "horizon")),
        ),
        out_specs=P(("state", "horizon"), "groups", "input", None),
        check_vma=False,
    )
```

```python
import jax
import jax.numpy as jnp
from jax import lax
from jax.sharding import PartitionSpec as P
from jax.experimental import pallas as pl
from jax.experimental.pallas import tpu as pltpu


def diagonal_sums(news):
    rows = news.shape[0]
    width = news.shape[-1]
    total = news
    shift = 1
    while shift < rows:
        moved = lax.pad(
            total[: rows - shift, ..., : width - shift],
            jnp.zeros((), total.dtype),
            [(shift, 0, 0)] + [(0, 0, 0)] * (total.ndim - 2) + [(shift, 0, 0)],
        )
        total = total + moved
        shift *= 2
    return total


def halving_scatter(full):
    state_count = lax.axis_size("state")
    core_count = lax.axis_size("horizon")
    count = state_count * core_count
    if count & (count - 1) or core_count & (core_count - 1):
        return lax.psum_scatter(full, ("state", "horizon"), scatter_dimension=0, tiled=True)
    index = lax.axis_index(("state", "horizon"))
    held = full.reshape((count, full.shape[0] // count) + full.shape[1:])
    step = 1
    while step < count:
        if step < core_count:
            axis, size, flip = "horizon", core_count, step
        else:
            axis, size, flip = "state", state_count, step // core_count
        pairs = [(member, member ^ flip) for member in range(size)]
        bit = (index // step) % 2
        halves = held.reshape((held.shape[0] // 2, 2) + held.shape[1:])
        keep = jnp.where(bit == 1, halves[:, 1], halves[:, 0])
        send = jnp.where(bit == 1, halves[:, 0], halves[:, 1])
        held = keep + lax.ppermute(send, axis, pairs)
        step *= 2
    return held.reshape(held.shape[1:])


def prepare_kernel(counts, offsets, regions, scales, tiles, expect, moves, rows, inner, up, down):
    block_count, band_count, tile_size, _ = tiles.shape
    output_count, expect_rows, _ = expect.shape
    row_count = output_count * expect_rows
    parts = []
    for block in range(block_count):
        count = counts[block]
        scale = lax.rsqrt(jnp.full((1, tile_size), count.astype(jnp.float32), jnp.float32))
        region = regions[block]
        pieces = []
        for out in range(output_count):
            part = expect[out, :, block * tile_size : (block + 1) * tile_size]
            pieces.append((part.astype(jnp.float32) * scales[out, region]).astype(jnp.bfloat16))
        half = jnp.concatenate(pieces, 0)
        rows[block] = half.astype(jnp.float32)
        carried = [
            jnp.dot(half, tiles[block, slot], preferred_element_type=jnp.float32)
            for slot in range(band_count)
        ]
        wide = [tiles[block, slot].astype(jnp.float32) for slot in range(band_count)]
        block_parts = []
        for shift in range(3):
            total = jnp.zeros((tile_size, tile_size), jnp.float32)
            flow = jnp.zeros((row_count, tile_size), jnp.float32)
            for slot in range(band_count):
                use = jnp.logical_and(slot < count, offsets[block, slot] == shift - 1)
                weight = jnp.where(use, 1.0, 0.0).astype(jnp.float32)
                total = total + weight * wide[slot]
                flow = flow + weight * carried[slot]
            total = total * scale
            moves[block, :, shift * tile_size : (shift + 1) * tile_size] = total
            block_parts.append(flow * scale)
            if block == block_count - 1 and shift > 0:
                up[row_count + (shift - 1) * tile_size : row_count + shift * tile_size, :] = total
            if block == 0 and shift < 2:
                down[row_count + shift * tile_size : row_count + (shift + 1) * tile_size, :] = total
        parts.append(block_parts)
    for block in range(block_count):
        total = parts[block][1]
        if block + 1 < block_count:
            total = total + parts[block + 1][0]
        if block > 0:
            total = total + parts[block - 1][2]
        inner[block] = total
    up[:row_count, :] = parts[-1][2]
    down[:row_count, :] = parts[0][0]


def prepare(counts, offsets, regions, region_scale, tiles, expectations):
    block_count, band_count, tile_size, _ = tiles.shape
    output_count, expect_rows, _ = expectations.shape
    row_count = output_count * expect_rows
    smem = pl.BlockSpec(memory_space=pltpu.SMEM)
    vmem = pl.BlockSpec(memory_space=pltpu.VMEM)
    edge = jax.ShapeDtypeStruct((row_count + 2 * tile_size, tile_size), jnp.float32)
    return pl.pallas_call(
        prepare_kernel,
        out_shape=(
            jax.ShapeDtypeStruct((block_count, tile_size, 3 * tile_size), jnp.float32),
            jax.ShapeDtypeStruct((block_count, row_count, tile_size), jnp.float32),
            jax.ShapeDtypeStruct((block_count, row_count, tile_size), jnp.float32),
            edge,
            edge,
        ),
        in_specs=[smem, smem, smem, smem, vmem, vmem],
        out_specs=(vmem, vmem, vmem, vmem, vmem),
    )(counts, offsets, regions, region_scale.T, tiles, expectations)


def split_product(rows_full, data_half):
    upper = rows_full.astype(jnp.bfloat16)
    remain = rows_full - upper.astype(jnp.float32)
    middle = remain.astype(jnp.bfloat16)
    lower = (remain - middle.astype(jnp.float32)).astype(jnp.bfloat16)
    total = jnp.dot(upper, data_half, preferred_element_type=jnp.float32)
    total = total + jnp.dot(middle, data_half, preferred_element_type=jnp.float32)
    return total + jnp.dot(lower, data_half, preferred_element_type=jnp.float32)


def shift_pairs(axis, step):
    count = lax.axis_size(axis)
    if step > 0:
        return [(i, i + 1) for i in range(count - 1)]
    return [(i + 1, i) for i in range(count - 1)]


def to_right(value):
    return lax.ppermute(value, ("state", "horizon"), shift_pairs(("state", "horizon"), 1))


def to_left(value):
    return lax.ppermute(value, ("state", "horizon"), shift_pairs(("state", "horizon"), -1))


def swap_edges(to_low, to_high):
    cores = lax.axis_size("horizon")
    if cores != 2:
        return to_right(to_high), to_left(to_low)
    count = lax.axis_size(("state", "horizon"))
    first = lax.axis_index("horizon") == 0
    on_chip = lax.ppermute(jnp.where(first, to_high, to_low), "horizon", [(0, 1), (1, 0)])
    pairs = []
    for chip in range(count // 2 - 1):
        pairs += [(2 * chip + 1, 2 * chip + 2), (2 * chip + 2, 2 * chip + 1)]
    across = lax.ppermute(jnp.where(first, to_low, to_high), ("state", "horizon"), pairs)
    return jnp.where(first, across, on_chip), jnp.where(first, on_chip, across)


def band_parts(rows, moves):
    parts = jnp.einsum("cru,cun->crn", rows, moves, precision=lax.Precision.HIGH)
    size = rows.shape[-1]
    down, same, up = parts[..., :size], parts[..., size : 2 * size], parts[..., 2 * size :]
    zero = jnp.zeros_like(same[:1])
    inner = same + jnp.concatenate([down[1:], zero], 0) + jnp.concatenate([zero, up[:-1]], 0)
    return inner, down, up


def band_step(rows, moves):
    inner, down, up = band_parts(rows, moves)
    return inner, down[0], up[-1]


def ext_step(rows, moves):
    inner, down, up = band_parts(rows, moves)
    return inner, down[1], up[-2]


def exchange_round(rows, moves, wide, steps):
    zero = jnp.zeros_like(rows[:1])
    held = jnp.concatenate([zero, rows, zero], 0)
    to_low, to_high, mine = [], [], []
    for _ in range(steps):
        held, out_low, out_high = ext_step(held, wide)
        to_low.append(out_low)
        to_high.append(out_high)
        mine.append(held[1:-1])
    from_low, from_high = swap_edges(jnp.stack(to_low), jnp.stack(to_high))
    levels = []
    carried = None
    for step in range(steps):
        if carried is None:
            carried = jnp.zeros_like(rows)
        else:
            carried, _, _ = band_step(carried, moves)
        carried = carried.at[0].add(from_low[step]).at[-1].add(from_high[step])
        levels.append(mine[step] + carried)
    return levels


def shards(impulses, expectations, region_scale, regions, tiles, offsets, counts):
    block_count, band_count, tile_size, _ = tiles.shape
    state_count, input_count, horizon = impulses.shape
    output_count, expect_rows, _ = expectations.shape
    region_total = region_scale.shape[0]
    width = input_count * horizon
    sections = horizon // expect_rows
    row_count = output_count * expect_rows
    moves, rows, inner, edge_low, edge_high = prepare(
        counts, offsets, regions, region_scale, tiles, expectations
    )
    flat_start = impulses.reshape(state_count, width)
    from_low, from_high = swap_edges(edge_high, edge_low)
    edge_in = jnp.zeros_like(inner[1:-1])
    levels = [
        rows,
        inner
        + jnp.concatenate([from_low[None, :row_count], edge_in, from_high[None, :row_count]], 0),
    ]
    left_self = from_low[row_count : row_count + tile_size]
    left_up = from_low[row_count + tile_size :]
    right_down = from_high[row_count : row_count + tile_size]
    right_self = from_high[row_count + tile_size :]
    blank = jnp.zeros_like(left_self)
    wide = jnp.concatenate(
        [
            jnp.concatenate([blank, left_self, left_up], 1)[None],
            moves,
            jnp.concatenate([right_down, right_self, blank], 1)[None],
        ],
        0,
    )
    remaining = sections - 2
    while remaining > 0:
        steps = min(3, remaining)
        levels += exchange_round(levels[-1], moves, wide, steps)
        remaining -= steps
    stacked = jnp.concatenate(
        [level.transpose(1, 0, 2).reshape(row_count, state_count) for level in levels], 0
    )
    product = split_product(stacked, flat_start)
    pieces = [
        piece.reshape(output_count, expect_rows, input_count, horizon).transpose(1, 0, 2, 3)
        for piece in jnp.split(product, sections, 0)
    ]
    partial_news = jnp.concatenate(pieces, axis=0)
    jacobian = diagonal_sums(partial_news)
    return halving_scatter(jacobian)


def solution(mesh):
    return jax.shard_map(
        shards,
        mesh=mesh,
        in_specs=(
            P(("state", "horizon"), "input", "groups"),
            P("groups", None, ("state", "horizon")),
            P("groups", None),
            P(("state", "horizon")),
            P(("state", "horizon"), None, None, None),
            P(("state", "horizon"), None),
            P(("state", "horizon")),
        ),
        out_specs=P(("state", "horizon"), "groups", "input", None),
        check_vma=False,
    )
```

```python
import jax
import jax.numpy as jnp
from jax import lax
from jax.sharding import PartitionSpec as P
from jax.experimental import pallas as pl
from jax.experimental.pallas import tpu as pltpu


def diagonal_sums(news):
    rows = news.shape[0]
    width = news.shape[-1]
    total = news
    shift = 1
    while shift < rows:
        moved = lax.pad(
            total[: rows - shift, ..., : width - shift],
            jnp.zeros((), total.dtype),
            [(shift, 0, 0)] + [(0, 0, 0)] * (total.ndim - 2) + [(shift, 0, 0)],
        )
        total = total + moved
        shift *= 2
    return total


def halving_scatter(full):
    state_count = lax.axis_size("state")
    core_count = lax.axis_size("horizon")
    count = state_count * core_count
    if count & (count - 1) or core_count & (core_count - 1):
        return lax.psum_scatter(full, ("state", "horizon"), scatter_dimension=0, tiled=True)
    index = lax.axis_index(("state", "horizon"))
    held = full.reshape((count, full.shape[0] // count) + full.shape[1:])
    step = 1
    while step < count:
        if step < core_count:
            axis, size, flip = "horizon", core_count, step
        else:
            axis, size, flip = "state", state_count, step // core_count
        pairs = [(member, member ^ flip) for member in range(size)]
        bit = (index // step) % 2
        halves = held.reshape((held.shape[0] // 2, 2) + held.shape[1:])
        keep = jnp.where(bit == 1, halves[:, 1], halves[:, 0])
        send = jnp.where(bit == 1, halves[:, 0], halves[:, 1])
        held = keep + lax.ppermute(send, axis, pairs)
        step *= 2
    return held.reshape(held.shape[1:])


def prepare_kernel(flip, counts, offsets, regions, scales, tiles, expect, moves, rows, inner, up, down):
    block_count, band_count, tile_size, _ = tiles.shape
    output_count, expect_rows, _ = expect.shape
    row_count = output_count * expect_rows
    parts = []
    for block in range(block_count):
        count = counts[block]
        scale = lax.rsqrt(jnp.full((1, tile_size), count.astype(jnp.float32), jnp.float32))
        region = regions[block]
        pieces = []
        for out in range(output_count):
            part = expect[out, :, block * tile_size : (block + 1) * tile_size]
            pieces.append((part.astype(jnp.float32) * scales[out, region]).astype(jnp.bfloat16))
        half = jnp.concatenate(pieces, 0)
        rows[block] = half.astype(jnp.float32)
        carried = [
            jnp.dot(half, tiles[block, slot], preferred_element_type=jnp.float32)
            for slot in range(band_count)
        ]
        wide = [tiles[block, slot].astype(jnp.float32) for slot in range(band_count)]
        block_parts = []
        for shift in range(3):
            total = jnp.zeros((tile_size, tile_size), jnp.float32)
            flow = jnp.zeros((row_count, tile_size), jnp.float32)
            for slot in range(band_count):
                use = jnp.logical_and(slot < count, offsets[block, slot] == shift - 1)
                weight = jnp.where(use, 1.0, 0.0).astype(jnp.float32)
                total = total + weight * wide[slot]
                flow = flow + weight * carried[slot]
            total = total * scale
            moves[block, :, shift * tile_size : (shift + 1) * tile_size] = total
            block_parts.append(flow * scale)
            if block == block_count - 1 and shift > 0:
                up[row_count + (shift - 1) * tile_size : row_count + shift * tile_size, :] = total
            if block == 0 and shift < 2:
                down[row_count + shift * tile_size : row_count + (shift + 1) * tile_size, :] = total
        parts.append(block_parts)
    for block in range(block_count):
        total = parts[block][1]
        if block + 1 < block_count:
            total = total + parts[block + 1][0]
        if block > 0:
            total = total + parts[block - 1][2]
        inner[block] = total
    up[:row_count, :] = parts[-1][2]
    down[:row_count, :] = parts[0][0]
    keep_up = up[...]
    keep_down = down[...]
    swap = flip[0] == 1
    up[...] = jnp.where(swap, keep_up, keep_down)
    down[...] = jnp.where(swap, keep_down, keep_up)


def prepare(flip, counts, offsets, regions, region_scale, tiles, expectations):
    block_count, band_count, tile_size, _ = tiles.shape
    output_count, expect_rows, _ = expectations.shape
    row_count = output_count * expect_rows
    smem = pl.BlockSpec(memory_space=pltpu.SMEM)
    vmem = pl.BlockSpec(memory_space=pltpu.VMEM)
    edge = jax.ShapeDtypeStruct((row_count + 2 * tile_size, tile_size), jnp.float32)
    return pl.pallas_call(
        prepare_kernel,
        out_shape=(
            jax.ShapeDtypeStruct((block_count, tile_size, 3 * tile_size), jnp.float32),
            jax.ShapeDtypeStruct((block_count, row_count, tile_size), jnp.float32),
            jax.ShapeDtypeStruct((block_count, row_count, tile_size), jnp.float32),
            edge,
            edge,
        ),
        in_specs=[smem, smem, smem, smem, smem, vmem, vmem],
        out_specs=(vmem, vmem, vmem, vmem, vmem),
    )(flip, counts, offsets, regions, region_scale.T, tiles, expectations)


def split_product(rows_full, data_half):
    upper = rows_full.astype(jnp.bfloat16)
    remain = rows_full - upper.astype(jnp.float32)
    middle = remain.astype(jnp.bfloat16)
    lower = (remain - middle.astype(jnp.float32)).astype(jnp.bfloat16)
    total = jnp.dot(upper, data_half, preferred_element_type=jnp.float32)
    total = total + jnp.dot(middle, data_half, preferred_element_type=jnp.float32)
    return total + jnp.dot(lower, data_half, preferred_element_type=jnp.float32)


def shift_pairs(axis, step):
    count = lax.axis_size(axis)
    if step > 0:
        return [(i, i + 1) for i in range(count - 1)]
    return [(i + 1, i) for i in range(count - 1)]


def to_right(value):
    return lax.ppermute(value, ("state", "horizon"), shift_pairs(("state", "horizon"), 1))


def to_left(value):
    return lax.ppermute(value, ("state", "horizon"), shift_pairs(("state", "horizon"), -1))


def swap_edges(to_low, to_high):
    if lax.axis_size("horizon") != 2:
        return to_right(to_high), to_left(to_low)
    first = lax.axis_index("horizon") == 0
    return swap_links(jnp.where(first, to_high, to_low), jnp.where(first, to_low, to_high))


def swap_links(chip_part, cross_part):
    count = lax.axis_size(("state", "horizon"))
    first = lax.axis_index("horizon") == 0
    on_chip = lax.ppermute(chip_part, "horizon", [(0, 1), (1, 0)])
    pairs = []
    for chip in range(count // 2 - 1):
        pairs += [(2 * chip + 1, 2 * chip + 2), (2 * chip + 2, 2 * chip + 1)]
    across = lax.ppermute(cross_part, ("state", "horizon"), pairs)
    return jnp.where(first, across, on_chip), jnp.where(first, on_chip, across)


def band_parts(rows, moves):
    parts = jnp.einsum("cru,cun->crn", rows, moves, precision=lax.Precision.HIGH)
    size = rows.shape[-1]
    down, same, up = parts[..., :size], parts[..., size : 2 * size], parts[..., 2 * size :]
    zero = jnp.zeros_like(same[:1])
    inner = same + jnp.concatenate([down[1:], zero], 0) + jnp.concatenate([zero, up[:-1]], 0)
    return inner, down, up


def band_step(rows, moves):
    inner, down, up = band_parts(rows, moves)
    return inner, down[0], up[-1]


def ext_step(rows, moves):
    inner, down, up = band_parts(rows, moves)
    return inner, down[1], up[-2]


def exchange_round(rows, moves, wide, steps):
    zero = jnp.zeros_like(rows[:1])
    held = jnp.concatenate([zero, rows, zero], 0)
    to_low, to_high, mine = [], [], []
    for _ in range(steps):
        held, out_low, out_high = ext_step(held, wide)
        to_low.append(out_low)
        to_high.append(out_high)
        mine.append(held[1:-1])
    from_low, from_high = swap_edges(jnp.stack(to_low), jnp.stack(to_high))
    levels = []
    carried = None
    for step in range(steps):
        if carried is None:
            carried = jnp.zeros_like(rows)
        else:
            carried, _, _ = band_step(carried, moves)
        carried = carried.at[0].add(from_low[step]).at[-1].add(from_high[step])
        levels.append(mine[step] + carried)
    return levels


def shards(impulses, expectations, region_scale, regions, tiles, offsets, counts):
    block_count, band_count, tile_size, _ = tiles.shape
    state_count, input_count, horizon = impulses.shape
    output_count, expect_rows, _ = expectations.shape
    region_total = region_scale.shape[0]
    width = input_count * horizon
    sections = horizon // expect_rows
    row_count = output_count * expect_rows
    paired = lax.axis_size("horizon") == 2
    flip = jnp.where(lax.axis_index("horizon") == 0, 1, 0) if paired else 0
    flip = jnp.full((1,), flip, jnp.int32)
    moves, rows, inner, first_part, second_part = prepare(
        flip, counts, offsets, regions, region_scale, tiles, expectations
    )
    flat_start = impulses.reshape(state_count, width)
    if paired:
        from_low, from_high = swap_links(first_part, second_part)
    else:
        from_low, from_high = swap_edges(second_part, first_part)
    edge_in = jnp.zeros_like(inner[1:-1])
    levels = [
        rows,
        inner
        + jnp.concatenate([from_low[None, :row_count], edge_in, from_high[None, :row_count]], 0),
    ]
    left_self = from_low[row_count : row_count + tile_size]
    left_up = from_low[row_count + tile_size :]
    right_down = from_high[row_count : row_count + tile_size]
    right_self = from_high[row_count + tile_size :]
    blank = jnp.zeros_like(left_self)
    wide = jnp.concatenate(
        [
            jnp.concatenate([blank, left_self, left_up], 1)[None],
            moves,
            jnp.concatenate([right_down, right_self, blank], 1)[None],
        ],
        0,
    )
    remaining = sections - 2
    while remaining > 0:
        steps = min(3, remaining)
        levels += exchange_round(levels[-1], moves, wide, steps)
        remaining -= steps
    stacked = jnp.concatenate(
        [level.transpose(1, 0, 2).reshape(row_count, state_count) for level in levels], 0
    )
    product = split_product(stacked, flat_start)
    pieces = [
        piece.reshape(output_count, expect_rows, input_count, horizon).transpose(1, 0, 2, 3)
        for piece in jnp.split(product, sections, 0)
    ]
    partial_news = jnp.concatenate(pieces, axis=0)
    jacobian = diagonal_sums(partial_news)
    return halving_scatter(jacobian)


def solution(mesh):
    return jax.shard_map(
        shards,
        mesh=mesh,
        in_specs=(
            P(("state", "horizon"), "input", "groups"),
            P("groups", None, ("state", "horizon")),
            P("groups", None),
            P(("state", "horizon")),
            P(("state", "horizon"), None, None, None),
            P(("state", "horizon"), None),
            P(("state", "horizon")),
        ),
        out_specs=P(("state", "horizon"), "groups", "input", None),
        check_vma=False,
    )
```

```python
import jax
import jax.numpy as jnp
from jax import lax
from jax.sharding import PartitionSpec as P
from jax.experimental import pallas as pl
from jax.experimental.pallas import tpu as pltpu


def diagonal_sums(news):
    rows = news.shape[0]
    width = news.shape[-1]
    total = news
    shift = 1
    while shift < rows:
        moved = lax.pad(
            total[: rows - shift, ..., : width - shift],
            jnp.zeros((), total.dtype),
            [(shift, 0, 0)] + [(0, 0, 0)] * (total.ndim - 2) + [(shift, 0, 0)],
        )
        total = total + moved
        shift *= 2
    return total


def halving_scatter(full):
    state_count = lax.axis_size("state")
    core_count = lax.axis_size("horizon")
    count = state_count * core_count
    if count & (count - 1) or core_count & (core_count - 1):
        return lax.psum_scatter(full, ("state", "horizon"), scatter_dimension=0, tiled=True)
    index = lax.axis_index(("state", "horizon"))
    held = full.reshape((count, full.shape[0] // count) + full.shape[1:])
    step = 1
    while step < count:
        if step < core_count:
            axis, size, flip = "horizon", core_count, step
        else:
            axis, size, flip = "state", state_count, step // core_count
        pairs = [(member, member ^ flip) for member in range(size)]
        bit = (index // step) % 2
        halves = held.reshape((held.shape[0] // 2, 2) + held.shape[1:])
        keep = jnp.where(bit == 1, halves[:, 1], halves[:, 0])
        send = jnp.where(bit == 1, halves[:, 0], halves[:, 1])
        held = keep + lax.ppermute(send, axis, pairs)
        step *= 2
    return held.reshape(held.shape[1:])


def prepare_kernel(flip, counts, offsets, regions, scales, tiles, expect, moves, rows, inner, up, down):
    block_count, band_count, tile_size, _ = tiles.shape
    output_count, expect_rows, _ = expect.shape
    row_count = output_count * expect_rows
    parts = []
    for block in range(block_count):
        count = counts[block]
        scale = lax.rsqrt(jnp.full((1, tile_size), count.astype(jnp.float32), jnp.float32))
        region = regions[block]
        pieces = []
        for out in range(output_count):
            part = expect[out, :, block * tile_size : (block + 1) * tile_size]
            pieces.append((part.astype(jnp.float32) * scales[out, region]).astype(jnp.bfloat16))
        half = jnp.concatenate(pieces, 0)
        rows[:, block * tile_size : (block + 1) * tile_size] = half
        carried = [
            jnp.dot(half, tiles[block, slot], preferred_element_type=jnp.float32)
            for slot in range(band_count)
        ]
        wide = [tiles[block, slot].astype(jnp.float32) for slot in range(band_count)]
        block_parts = []
        for shift in range(3):
            total = jnp.zeros((tile_size, tile_size), jnp.float32)
            flow = jnp.zeros((row_count, tile_size), jnp.float32)
            for slot in range(band_count):
                use = jnp.logical_and(slot < count, offsets[block, slot] == shift - 1)
                weight = jnp.where(use, 1.0, 0.0).astype(jnp.float32)
                total = total + weight * wide[slot]
                flow = flow + weight * carried[slot]
            total = total * scale
            moves[block, :, shift * tile_size : (shift + 1) * tile_size] = total
            block_parts.append(flow * scale)
            if block == block_count - 1 and shift > 0:
                up[row_count + (shift - 1) * tile_size : row_count + shift * tile_size, :] = total
            if block == 0 and shift < 2:
                down[row_count + shift * tile_size : row_count + (shift + 1) * tile_size, :] = total
        parts.append(block_parts)
    for block in range(block_count):
        total = parts[block][1]
        if block + 1 < block_count:
            total = total + parts[block + 1][0]
        if block > 0:
            total = total + parts[block - 1][2]
        inner[block] = total
    up[:row_count, :] = parts[-1][2]
    down[:row_count, :] = parts[0][0]
    keep_up = up[...]
    keep_down = down[...]
    swap = flip[0] == 1
    up[...] = jnp.where(swap, keep_up, keep_down)
    down[...] = jnp.where(swap, keep_down, keep_up)


def prepare(flip, counts, offsets, regions, region_scale, tiles, expectations):
    block_count, band_count, tile_size, _ = tiles.shape
    output_count, expect_rows, _ = expectations.shape
    row_count = output_count * expect_rows
    smem = pl.BlockSpec(memory_space=pltpu.SMEM)
    vmem = pl.BlockSpec(memory_space=pltpu.VMEM)
    edge = jax.ShapeDtypeStruct((row_count + 2 * tile_size, tile_size), jnp.float32)
    return pl.pallas_call(
        prepare_kernel,
        out_shape=(
            jax.ShapeDtypeStruct((block_count, tile_size, 3 * tile_size), jnp.float32),
            jax.ShapeDtypeStruct((row_count, block_count * tile_size), jnp.bfloat16),
            jax.ShapeDtypeStruct((block_count, row_count, tile_size), jnp.float32),
            edge,
            edge,
        ),
        in_specs=[smem, smem, smem, smem, smem, vmem, vmem],
        out_specs=(vmem, vmem, vmem, vmem, vmem),
    )(flip, counts, offsets, regions, region_scale.T, tiles, expectations)


def split_product(rows_full, data_half):
    upper = rows_full.astype(jnp.bfloat16)
    remain = rows_full - upper.astype(jnp.float32)
    middle = remain.astype(jnp.bfloat16)
    lower = (remain - middle.astype(jnp.float32)).astype(jnp.bfloat16)
    total = jnp.dot(upper, data_half, preferred_element_type=jnp.float32)
    total = total + jnp.dot(middle, data_half, preferred_element_type=jnp.float32)
    return total + jnp.dot(lower, data_half, preferred_element_type=jnp.float32)


def shift_pairs(axis, step):
    count = lax.axis_size(axis)
    if step > 0:
        return [(i, i + 1) for i in range(count - 1)]
    return [(i + 1, i) for i in range(count - 1)]


def to_right(value):
    return lax.ppermute(value, ("state", "horizon"), shift_pairs(("state", "horizon"), 1))


def to_left(value):
    return lax.ppermute(value, ("state", "horizon"), shift_pairs(("state", "horizon"), -1))


def swap_edges(to_low, to_high):
    if lax.axis_size("horizon") != 2:
        return to_right(to_high), to_left(to_low)
    first = lax.axis_index("horizon") == 0
    return swap_links(jnp.where(first, to_high, to_low), jnp.where(first, to_low, to_high))


def swap_links(chip_part, cross_part):
    count = lax.axis_size(("state", "horizon"))
    first = lax.axis_index("horizon") == 0
    on_chip = lax.ppermute(chip_part, "horizon", [(0, 1), (1, 0)])
    pairs = []
    for chip in range(count // 2 - 1):
        pairs += [(2 * chip + 1, 2 * chip + 2), (2 * chip + 2, 2 * chip + 1)]
    across = lax.ppermute(cross_part, ("state", "horizon"), pairs)
    return jnp.where(first, across, on_chip), jnp.where(first, on_chip, across)


def band_parts(rows, moves):
    parts = jnp.einsum("cru,cun->crn", rows, moves, precision=lax.Precision.HIGH)
    size = rows.shape[-1]
    down, same, up = parts[..., :size], parts[..., size : 2 * size], parts[..., 2 * size :]
    zero = jnp.zeros_like(same[:1])
    inner = same + jnp.concatenate([down[1:], zero], 0) + jnp.concatenate([zero, up[:-1]], 0)
    return inner, down, up


def band_step(rows, moves):
    inner, down, up = band_parts(rows, moves)
    return inner, down[0], up[-1]


def ext_step(rows, moves):
    inner, down, up = band_parts(rows, moves)
    return inner, down[1], up[-2]


def exchange_round(rows, moves, wide, steps):
    zero = jnp.zeros_like(rows[:1])
    held = jnp.concatenate([zero, rows, zero], 0)
    to_low, to_high, mine = [], [], []
    for _ in range(steps):
        held, out_low, out_high = ext_step(held, wide)
        to_low.append(out_low)
        to_high.append(out_high)
        mine.append(held[1:-1])
    from_low, from_high = swap_edges(jnp.stack(to_low), jnp.stack(to_high))
    levels = []
    carried = None
    for step in range(steps):
        if carried is None:
            carried = jnp.zeros_like(rows)
        else:
            carried, _, _ = band_step(carried, moves)
        carried = carried.at[0].add(from_low[step]).at[-1].add(from_high[step])
        levels.append(mine[step] + carried)
    return levels


def shards(impulses, expectations, region_scale, regions, tiles, offsets, counts):
    block_count, band_count, tile_size, _ = tiles.shape
    state_count, input_count, horizon = impulses.shape
    output_count, expect_rows, _ = expectations.shape
    region_total = region_scale.shape[0]
    width = input_count * horizon
    sections = horizon // expect_rows
    row_count = output_count * expect_rows
    paired = lax.axis_size("horizon") == 2
    flip = jnp.where(lax.axis_index("horizon") == 0, 1, 0) if paired else 0
    flip = jnp.full((1,), flip, jnp.int32)
    moves, rows, inner, first_part, second_part = prepare(
        flip, counts, offsets, regions, region_scale, tiles, expectations
    )
    flat_start = impulses.reshape(state_count, width)
    if paired:
        from_low, from_high = swap_links(first_part, second_part)
    else:
        from_low, from_high = swap_edges(second_part, first_part)
    edge_in = jnp.zeros_like(inner[1:-1])
    levels = [
        inner
        + jnp.concatenate([from_low[None, :row_count], edge_in, from_high[None, :row_count]], 0),
    ]
    left_self = from_low[row_count : row_count + tile_size]
    left_up = from_low[row_count + tile_size :]
    right_down = from_high[row_count : row_count + tile_size]
    right_self = from_high[row_count + tile_size :]
    blank = jnp.zeros_like(left_self)
    wide = jnp.concatenate(
        [
            jnp.concatenate([blank, left_self, left_up], 1)[None],
            moves,
            jnp.concatenate([right_down, right_self, blank], 1)[None],
        ],
        0,
    )
    remaining = sections - 2
    while remaining > 0:
        steps = min(3, remaining)
        levels += exchange_round(levels[-1], moves, wide, steps)
        remaining -= steps
    stacked = jnp.concatenate(
        [level.transpose(1, 0, 2).reshape(row_count, state_count) for level in levels], 0
    )
    product = split_product(stacked, flat_start)
    first = jnp.dot(rows, flat_start, preferred_element_type=jnp.float32)
    pieces = [
        piece.reshape(output_count, expect_rows, input_count, horizon).transpose(1, 0, 2, 3)
        for piece in [first] + jnp.split(product, sections - 1, 0)
    ]
    partial_news = jnp.concatenate(pieces, axis=0)
    jacobian = diagonal_sums(partial_news)
    return halving_scatter(jacobian)


def solution(mesh):
    return jax.shard_map(
        shards,
        mesh=mesh,
        in_specs=(
            P(("state", "horizon"), "input", "groups"),
            P("groups", None, ("state", "horizon")),
            P("groups", None),
            P(("state", "horizon")),
            P(("state", "horizon"), None, None, None),
            P(("state", "horizon"), None),
            P(("state", "horizon")),
        ),
        out_specs=P(("state", "horizon"), "groups", "input", None),
        check_vma=False,
    )
```

```python
import jax
import jax.numpy as jnp
from jax import lax
from jax.sharding import PartitionSpec as P
from jax.experimental import pallas as pl
from jax.experimental.pallas import tpu as pltpu


def diagonal_sums(news):
    rows = news.shape[0]
    width = news.shape[-1]
    total = news
    shift = 1
    while shift < rows:
        moved = lax.pad(
            total[: rows - shift, ..., : width - shift],
            jnp.zeros((), total.dtype),
            [(shift, 0, 0)] + [(0, 0, 0)] * (total.ndim - 2) + [(shift, 0, 0)],
        )
        total = total + moved
        shift *= 2
    return total


def halving_scatter(full):
    state_count = lax.axis_size("state")
    core_count = lax.axis_size("horizon")
    count = state_count * core_count
    if count & (count - 1) or core_count & (core_count - 1):
        return lax.psum_scatter(full, ("state", "horizon"), scatter_dimension=0, tiled=True)
    index = lax.axis_index(("state", "horizon"))
    held = full.reshape((count, full.shape[0] // count) + full.shape[1:])
    step = 1
    while step < count:
        if step < core_count:
            axis, size, flip = "horizon", core_count, step
        else:
            axis, size, flip = "state", state_count, step // core_count
        pairs = [(member, member ^ flip) for member in range(size)]
        bit = (index // step) % 2
        halves = held.reshape((held.shape[0] // 2, 2) + held.shape[1:])
        keep = jnp.where(bit == 1, halves[:, 1], halves[:, 0])
        send = jnp.where(bit == 1, halves[:, 0], halves[:, 1])
        held = keep + lax.ppermute(send, axis, pairs)
        step *= 2
    return held.reshape(held.shape[1:])


def prepare_kernel(flip, counts, offsets, regions, scales, tiles, expect, moves, rows, inner, up, down):
    block_count, band_count, tile_size, _ = tiles.shape
    output_count, expect_rows, _ = expect.shape
    row_count = output_count * expect_rows
    parts = []
    for block in range(block_count):
        count = counts[block]
        scale = lax.rsqrt(jnp.full((1, tile_size), count.astype(jnp.float32), jnp.float32))
        region = regions[block]
        pieces = []
        for out in range(output_count):
            part = expect[out, :, block * tile_size : (block + 1) * tile_size]
            pieces.append((part.astype(jnp.float32) * scales[out, region]).astype(jnp.bfloat16))
        half = jnp.concatenate(pieces, 0)
        rows[:, block * tile_size : (block + 1) * tile_size] = half
        carried = [
            jnp.dot(half, tiles[block, slot], preferred_element_type=jnp.float32)
            for slot in range(band_count)
        ]
        wide = [tiles[block, slot].astype(jnp.float32) for slot in range(band_count)]
        block_parts = []
        for shift in range(3):
            total = jnp.zeros((tile_size, tile_size), jnp.float32)
            flow = jnp.zeros((row_count, tile_size), jnp.float32)
            for slot in range(band_count):
                use = jnp.logical_and(slot < count, offsets[block, slot] == shift - 1)
                weight = jnp.where(use, 1.0, 0.0).astype(jnp.float32)
                total = total + weight * wide[slot]
                flow = flow + weight * carried[slot]
            total = total * scale
            moves[block, :, shift * tile_size : (shift + 1) * tile_size] = total
            block_parts.append(flow * scale)
            if block == block_count - 1 and shift > 0:
                up[row_count + (shift - 1) * tile_size : row_count + shift * tile_size, :] = total
            if block == 0 and shift < 2:
                down[row_count + shift * tile_size : row_count + (shift + 1) * tile_size, :] = total
        parts.append(block_parts)
    for block in range(block_count):
        total = parts[block][1]
        if block + 1 < block_count:
            total = total + parts[block + 1][0]
        if block > 0:
            total = total + parts[block - 1][2]
        inner[block] = total
    up[:row_count, :] = parts[-1][2]
    down[:row_count, :] = parts[0][0]
    keep_up = up[...]
    keep_down = down[...]
    swap = flip[0] == 1
    up[...] = jnp.where(swap, keep_up, keep_down)
    down[...] = jnp.where(swap, keep_down, keep_up)


def prepare(flip, counts, offsets, regions, region_scale, tiles, expectations):
    block_count, band_count, tile_size, _ = tiles.shape
    output_count, expect_rows, _ = expectations.shape
    row_count = output_count * expect_rows
    smem = pl.BlockSpec(memory_space=pltpu.SMEM)
    vmem = pl.BlockSpec(memory_space=pltpu.VMEM)
    edge = jax.ShapeDtypeStruct((row_count + 2 * tile_size, tile_size), jnp.float32)
    return pl.pallas_call(
        prepare_kernel,
        out_shape=(
            jax.ShapeDtypeStruct((block_count, tile_size, 3 * tile_size), jnp.float32),
            jax.ShapeDtypeStruct((row_count, block_count * tile_size), jnp.bfloat16),
            jax.ShapeDtypeStruct((block_count, row_count, tile_size), jnp.float32),
            edge,
            edge,
        ),
        in_specs=[smem, smem, smem, smem, smem, vmem, vmem],
        out_specs=(vmem, vmem, vmem, vmem, vmem),
    )(flip, counts, offsets, regions, region_scale.T, tiles, expectations)


def split_product(rows_full, data_half):
    upper = rows_full.astype(jnp.bfloat16)
    remain = rows_full - upper.astype(jnp.float32)
    middle = remain.astype(jnp.bfloat16)
    lower = (remain - middle.astype(jnp.float32)).astype(jnp.bfloat16)
    total = jnp.dot(upper, data_half, preferred_element_type=jnp.float32)
    total = total + jnp.dot(middle, data_half, preferred_element_type=jnp.float32)
    return total + jnp.dot(lower, data_half, preferred_element_type=jnp.float32)


def shift_pairs(axis, step):
    count = lax.axis_size(axis)
    if step > 0:
        return [(i, i + 1) for i in range(count - 1)]
    return [(i + 1, i) for i in range(count - 1)]


def to_right(value):
    return lax.ppermute(value, ("state", "horizon"), shift_pairs(("state", "horizon"), 1))


def to_left(value):
    return lax.ppermute(value, ("state", "horizon"), shift_pairs(("state", "horizon"), -1))


def swap_edges(to_low, to_high):
    if lax.axis_size("horizon") != 2:
        return to_right(to_high), to_left(to_low)
    first = lax.axis_index("horizon") == 0
    return swap_links(jnp.where(first, to_high, to_low), jnp.where(first, to_low, to_high))


def swap_links(chip_part, cross_part):
    count = lax.axis_size(("state", "horizon"))
    first = lax.axis_index("horizon") == 0
    on_chip = lax.ppermute(chip_part, "horizon", [(0, 1), (1, 0)])
    pairs = []
    for chip in range(count // 2 - 1):
        pairs += [(2 * chip + 1, 2 * chip + 2), (2 * chip + 2, 2 * chip + 1)]
    across = lax.ppermute(cross_part, ("state", "horizon"), pairs)
    return jnp.where(first, across, on_chip), jnp.where(first, on_chip, across)


def band_parts(rows, moves):
    size = rows.shape[-1]
    split = moves.reshape(moves.shape[:2] + (3, size))
    parts = jnp.einsum("cru,cudv->dcrv", rows, split, precision=lax.Precision.HIGH)
    down, same, up = parts[0], parts[1], parts[2]
    zero = jnp.zeros_like(same[:1])
    inner = same + jnp.concatenate([down[1:], zero], 0) + jnp.concatenate([zero, up[:-1]], 0)
    return inner, down, up


def band_step(rows, moves):
    inner, down, up = band_parts(rows, moves)
    return inner, down[0], up[-1]


def ext_step(rows, moves):
    inner, down, up = band_parts(rows, moves)
    return inner, down[1], up[-2]


def exchange_round(rows, moves, wide, steps):
    zero = jnp.zeros_like(rows[:1])
    held = jnp.concatenate([zero, rows, zero], 0)
    to_low, to_high, mine = [], [], []
    for _ in range(steps):
        held, out_low, out_high = ext_step(held, wide)
        to_low.append(out_low)
        to_high.append(out_high)
        mine.append(held[1:-1])
    from_low, from_high = swap_edges(jnp.stack(to_low), jnp.stack(to_high))
    levels = []
    carried = None
    for step in range(steps):
        if carried is None:
            carried = jnp.zeros_like(rows)
        else:
            carried, _, _ = band_step(carried, moves)
        carried = carried.at[0].add(from_low[step]).at[-1].add(from_high[step])
        levels.append(mine[step] + carried)
    return levels


def shards(impulses, expectations, region_scale, regions, tiles, offsets, counts):
    block_count, band_count, tile_size, _ = tiles.shape
    state_count, input_count, horizon = impulses.shape
    output_count, expect_rows, _ = expectations.shape
    region_total = region_scale.shape[0]
    width = input_count * horizon
    sections = horizon // expect_rows
    row_count = output_count * expect_rows
    paired = lax.axis_size("horizon") == 2
    flip = jnp.where(lax.axis_index("horizon") == 0, 1, 0) if paired else 0
    flip = jnp.full((1,), flip, jnp.int32)
    moves, rows, inner, first_part, second_part = prepare(
        flip, counts, offsets, regions, region_scale, tiles, expectations
    )
    flat_start = impulses.reshape(state_count, width)
    if paired:
        from_low, from_high = swap_links(first_part, second_part)
    else:
        from_low, from_high = swap_edges(second_part, first_part)
    edge_in = jnp.zeros_like(inner[1:-1])
    levels = [
        inner
        + jnp.concatenate([from_low[None, :row_count], edge_in, from_high[None, :row_count]], 0),
    ]
    left_self = from_low[row_count : row_count + tile_size]
    left_up = from_low[row_count + tile_size :]
    right_down = from_high[row_count : row_count + tile_size]
    right_self = from_high[row_count + tile_size :]
    blank = jnp.zeros_like(left_self)
    wide = jnp.concatenate(
        [
            jnp.concatenate([blank, left_self, left_up], 1)[None],
            moves,
            jnp.concatenate([right_down, right_self, blank], 1)[None],
        ],
        0,
    )
    remaining = sections - 2
    while remaining > 0:
        steps = min(3, remaining)
        levels += exchange_round(levels[-1], moves, wide, steps)
        remaining -= steps
    stacked = jnp.concatenate(
        [level.transpose(1, 0, 2).reshape(row_count, state_count) for level in levels], 0
    )
    product = split_product(stacked, flat_start)
    first = jnp.dot(rows, flat_start, preferred_element_type=jnp.float32)
    pieces = [
        piece.reshape(output_count, expect_rows, input_count, horizon).transpose(1, 0, 2, 3)
        for piece in [first] + jnp.split(product, sections - 1, 0)
    ]
    partial_news = jnp.concatenate(pieces, axis=0)
    jacobian = diagonal_sums(partial_news)
    return halving_scatter(jacobian)


def solution(mesh):
    return jax.shard_map(
        shards,
        mesh=mesh,
        in_specs=(
            P(("state", "horizon"), "input", "groups"),
            P("groups", None, ("state", "horizon")),
            P("groups", None),
            P(("state", "horizon")),
            P(("state", "horizon"), None, None, None),
            P(("state", "horizon"), None),
            P(("state", "horizon")),
        ),
        out_specs=P(("state", "horizon"), "groups", "input", None),
        check_vma=False,
    )
```

```python
import jax
import jax.numpy as jnp
from jax import lax
from jax.sharding import PartitionSpec as P
from jax.experimental import pallas as pl
from jax.experimental.pallas import tpu as pltpu


def diagonal_sums(news):
    rows = news.shape[0]
    width = news.shape[-1]
    total = news
    shift = 1
    while shift < rows:
        moved = lax.pad(
            total[: rows - shift, ..., : width - shift],
            jnp.zeros((), total.dtype),
            [(shift, 0, 0)] + [(0, 0, 0)] * (total.ndim - 2) + [(shift, 0, 0)],
        )
        total = total + moved
        shift *= 2
    return total


def halving_scatter(full):
    state_count = lax.axis_size("state")
    core_count = lax.axis_size("horizon")
    count = state_count * core_count
    if count & (count - 1) or core_count & (core_count - 1):
        return lax.psum_scatter(full, ("state", "horizon"), scatter_dimension=0, tiled=True)
    index = lax.axis_index(("state", "horizon"))
    held = full.reshape((count, full.shape[0] // count) + full.shape[1:])
    step = 1
    while step < count:
        if step < core_count:
            axis, size, flip = "horizon", core_count, step
        else:
            axis, size, flip = "state", state_count, step // core_count
        pairs = [(member, member ^ flip) for member in range(size)]
        bit = (index // step) % 2
        halves = held.reshape((held.shape[0] // 2, 2) + held.shape[1:])
        keep = jnp.where(bit == 1, halves[:, 1], halves[:, 0])
        send = jnp.where(bit == 1, halves[:, 0], halves[:, 1])
        held = keep + lax.ppermute(send, axis, pairs)
        step *= 2
    return held.reshape(held.shape[1:])


def prepare_kernel(flip, counts, offsets, regions, scales, tiles, expect, moves, rows, inner, up, down):
    block_count, band_count, tile_size, _ = tiles.shape
    output_count, expect_rows, _ = expect.shape
    row_count = output_count * expect_rows
    parts = []
    for block in range(block_count):
        count = counts[block]
        scale = lax.rsqrt(jnp.full((1, tile_size), count.astype(jnp.float32), jnp.float32))
        region = regions[block]
        pieces = []
        for out in range(output_count):
            part = expect[out, :, block * tile_size : (block + 1) * tile_size]
            pieces.append((part.astype(jnp.float32) * scales[out, region]).astype(jnp.bfloat16))
        half = jnp.concatenate(pieces, 0)
        rows[:, block * tile_size : (block + 1) * tile_size] = half
        carried = [
            jnp.dot(half, tiles[block, slot], preferred_element_type=jnp.float32)
            for slot in range(band_count)
        ]
        wide = [tiles[block, slot].astype(jnp.float32) for slot in range(band_count)]
        block_parts = []
        for shift in range(3):
            total = jnp.zeros((tile_size, tile_size), jnp.float32)
            flow = jnp.zeros((row_count, tile_size), jnp.float32)
            for slot in range(band_count):
                use = jnp.logical_and(slot < count, offsets[block, slot] == shift - 1)
                weight = jnp.where(use, 1.0, 0.0).astype(jnp.float32)
                total = total + weight * wide[slot]
                flow = flow + weight * carried[slot]
            total = total * scale
            moves[block, :, shift * tile_size : (shift + 1) * tile_size] = total
            block_parts.append(flow * scale)
            if block == block_count - 1 and shift > 0:
                up[row_count + (shift - 1) * tile_size : row_count + shift * tile_size, :] = total
            if block == 0 and shift < 2:
                down[row_count + shift * tile_size : row_count + (shift + 1) * tile_size, :] = total
        parts.append(block_parts)
    for block in range(block_count):
        total = parts[block][1]
        if block + 1 < block_count:
            total = total + parts[block + 1][0]
        if block > 0:
            total = total + parts[block - 1][2]
        inner[block] = total
    up[:row_count, :] = parts[-1][2]
    down[:row_count, :] = parts[0][0]
    keep_up = up[...]
    keep_down = down[...]
    swap = flip[0] == 1
    up[...] = jnp.where(swap, keep_up, keep_down)
    down[...] = jnp.where(swap, keep_down, keep_up)


def prepare(flip, counts, offsets, regions, region_scale, tiles, expectations):
    block_count, band_count, tile_size, _ = tiles.shape
    output_count, expect_rows, _ = expectations.shape
    row_count = output_count * expect_rows
    smem = pl.BlockSpec(memory_space=pltpu.SMEM)
    vmem = pl.BlockSpec(memory_space=pltpu.VMEM)
    edge = jax.ShapeDtypeStruct((row_count + 2 * tile_size, tile_size), jnp.float32)
    return pl.pallas_call(
        prepare_kernel,
        out_shape=(
            jax.ShapeDtypeStruct((block_count, tile_size, 3 * tile_size), jnp.float32),
            jax.ShapeDtypeStruct((row_count, block_count * tile_size), jnp.bfloat16),
            jax.ShapeDtypeStruct((block_count, row_count, tile_size), jnp.float32),
            edge,
            edge,
        ),
        in_specs=[smem, smem, smem, smem, smem, vmem, vmem],
        out_specs=(vmem, vmem, vmem, vmem, vmem),
    )(flip, counts, offsets, regions, region_scale.T, tiles, expectations)


def split_product(rows_full, data_half):
    upper = rows_full.astype(jnp.bfloat16)
    remain = rows_full - upper.astype(jnp.float32)
    middle = remain.astype(jnp.bfloat16)
    lower = (remain - middle.astype(jnp.float32)).astype(jnp.bfloat16)
    total = jnp.dot(upper, data_half, preferred_element_type=jnp.float32)
    total = total + jnp.dot(middle, data_half, preferred_element_type=jnp.float32)
    return total + jnp.dot(lower, data_half, preferred_element_type=jnp.float32)


def shift_pairs(axis, step):
    count = lax.axis_size(axis)
    if step > 0:
        return [(i, i + 1) for i in range(count - 1)]
    return [(i + 1, i) for i in range(count - 1)]


def to_right(value):
    return lax.ppermute(value, ("state", "horizon"), shift_pairs(("state", "horizon"), 1))


def to_left(value):
    return lax.ppermute(value, ("state", "horizon"), shift_pairs(("state", "horizon"), -1))


def swap_edges(to_low, to_high):
    if lax.axis_size("horizon") != 2:
        return to_right(to_high), to_left(to_low)
    first = lax.axis_index("horizon") == 0
    return swap_links(jnp.where(first, to_high, to_low), jnp.where(first, to_low, to_high))


def swap_links(chip_part, cross_part):
    count = lax.axis_size(("state", "horizon"))
    first = lax.axis_index("horizon") == 0
    on_chip = lax.ppermute(chip_part, "horizon", [(0, 1), (1, 0)])
    pairs = []
    for chip in range(count // 2 - 1):
        pairs += [(2 * chip + 1, 2 * chip + 2), (2 * chip + 2, 2 * chip + 1)]
    across = lax.ppermute(cross_part, ("state", "horizon"), pairs)
    return jnp.where(first, across, on_chip), jnp.where(first, on_chip, across)


def band_parts(rows, moves):
    parts = jnp.einsum("cru,cun->crn", rows, moves, precision=lax.Precision.HIGH)
    size = rows.shape[-1]
    down, same, up = parts[..., :size], parts[..., size : 2 * size], parts[..., 2 * size :]
    zero = jnp.zeros_like(same[:1])
    inner = same + jnp.concatenate([down[1:], zero], 0) + jnp.concatenate([zero, up[:-1]], 0)
    return inner, down, up


def band_step(rows, moves):
    inner, down, up = band_parts(rows, moves)
    return inner, down[0], up[-1]


def ext_step(rows, moves):
    inner, down, up = band_parts(rows, moves)
    return inner, down[1], up[-2]


def exchange_round(rows, moves, wide, steps):
    zero = jnp.zeros_like(rows[:1])
    held = jnp.concatenate([zero, rows, zero], 0)
    to_low, to_high, mine = [], [], []
    for _ in range(steps):
        held, out_low, out_high = ext_step(held, wide)
        to_low.append(out_low)
        to_high.append(out_high)
        mine.append(held[1:-1])
    from_low, from_high = swap_edges(jnp.stack(to_low), jnp.stack(to_high))
    levels = []
    carried = None
    for step in range(steps):
        if carried is None:
            carried = jnp.zeros_like(rows)
        else:
            carried, _, _ = band_step(carried, moves)
        carried = carried.at[0].add(from_low[step]).at[-1].add(from_high[step])
        levels.append(mine[step] + carried)
    return levels


def shards(impulses, expectations, region_scale, regions, tiles, offsets, counts):
    block_count, band_count, tile_size, _ = tiles.shape
    state_count, input_count, horizon = impulses.shape
    output_count, expect_rows, _ = expectations.shape
    region_total = region_scale.shape[0]
    width = input_count * horizon
    sections = horizon // expect_rows
    row_count = output_count * expect_rows
    paired = lax.axis_size("horizon") == 2
    flip = jnp.where(lax.axis_index("horizon") == 0, 1, 0) if paired else 0
    flip = jnp.full((1,), flip, jnp.int32)
    moves, rows, inner, first_part, second_part = prepare(
        flip, counts, offsets, regions, region_scale, tiles, expectations
    )
    flat_start = impulses.reshape(state_count, width)
    if paired:
        from_low, from_high = swap_links(first_part, second_part)
    else:
        from_low, from_high = swap_edges(second_part, first_part)
    edge_in = jnp.zeros_like(inner[1:-1])
    levels = [
        inner
        + jnp.concatenate([from_low[None, :row_count], edge_in, from_high[None, :row_count]], 0),
    ]
    left_self = from_low[row_count : row_count + tile_size]
    left_up = from_low[row_count + tile_size :]
    right_down = from_high[row_count : row_count + tile_size]
    right_self = from_high[row_count + tile_size :]
    blank = jnp.zeros_like(left_self)
    wide = jnp.concatenate(
        [
            jnp.concatenate([blank, left_self, left_up], 1)[None],
            moves,
            jnp.concatenate([right_down, right_self, blank], 1)[None],
        ],
        0,
    )
    remaining = sections - 2
    while remaining > 0:
        steps = min(3, remaining)
        levels += exchange_round(levels[-1], moves, wide, steps)
        remaining -= steps
    stacked = jnp.concatenate(
        [level.transpose(1, 0, 2).reshape(row_count, state_count) for level in levels], 0
    )
    product = split_product(stacked, flat_start)
    first = jnp.dot(rows, flat_start, preferred_element_type=jnp.float32)
    pieces = [
        piece.reshape(output_count, expect_rows, input_count, horizon).transpose(1, 0, 2, 3)
        for piece in [first] + jnp.split(product, sections - 1, 0)
    ]
    partial_news = jnp.concatenate(pieces, axis=0)
    merged = partial_news.reshape(horizon, output_count * input_count, horizon)
    jacobian = halving_scatter(diagonal_sums(merged))
    return jacobian.reshape((jacobian.shape[0], output_count, input_count, horizon))


def solution(mesh):
    return jax.shard_map(
        shards,
        mesh=mesh,
        in_specs=(
            P(("state", "horizon"), "input", "groups"),
            P("groups", None, ("state", "horizon")),
            P("groups", None),
            P(("state", "horizon")),
            P(("state", "horizon"), None, None, None),
            P(("state", "horizon"), None),
            P(("state", "horizon")),
        ),
        out_specs=P(("state", "horizon"), "groups", "input", None),
        check_vma=False,
    )
```

```python
import jax
import jax.numpy as jnp
from jax import lax
from jax.sharding import PartitionSpec as P
from jax.experimental import pallas as pl
from jax.experimental.pallas import tpu as pltpu


def diagonal_sums(news):
    rows = news.shape[0]
    width = news.shape[-1]
    total = news
    shift = 1
    while shift < rows:
        moved = lax.pad(
            total[: rows - shift, ..., : width - shift],
            jnp.zeros((), total.dtype),
            [(shift, 0, 0)] + [(0, 0, 0)] * (total.ndim - 2) + [(shift, 0, 0)],
        )
        total = total + moved
        shift *= 2
    return total


def halving_scatter(full):
    state_count = lax.axis_size("state")
    core_count = lax.axis_size("horizon")
    count = state_count * core_count
    if count & (count - 1) or core_count & (core_count - 1):
        return lax.psum_scatter(full, ("state", "horizon"), scatter_dimension=0, tiled=True)
    index = lax.axis_index(("state", "horizon"))
    held = full.reshape((count, full.shape[0] // count) + full.shape[1:])
    step = 1
    while step < count:
        if step < core_count:
            axis, size, flip = "horizon", core_count, step
        else:
            axis, size, flip = "state", state_count, step // core_count
        pairs = [(member, member ^ flip) for member in range(size)]
        bit = (index // step) % 2
        halves = held.reshape((held.shape[0] // 2, 2) + held.shape[1:])
        keep = jnp.where(bit == 1, halves[:, 1], halves[:, 0])
        send = jnp.where(bit == 1, halves[:, 0], halves[:, 1])
        held = keep + lax.ppermute(send, axis, pairs)
        step *= 2
    return held.reshape(held.shape[1:])


def prepare_kernel(flip, counts, offsets, regions, scales, tiles, expect, moves, rows, inner, up, down):
    block_count, band_count, tile_size, _ = tiles.shape
    output_count, expect_rows, _ = expect.shape
    row_count = output_count * expect_rows
    parts = []
    for block in range(block_count):
        count = counts[block]
        scale = lax.rsqrt(jnp.full((1, tile_size), count.astype(jnp.float32), jnp.float32))
        region = regions[block]
        pieces = []
        for out in range(output_count):
            part = expect[out, :, block * tile_size : (block + 1) * tile_size]
            pieces.append((part.astype(jnp.float32) * scales[out, region]).astype(jnp.bfloat16))
        half = jnp.concatenate(pieces, 0)
        rows[:, block * tile_size : (block + 1) * tile_size] = half
        carried = [
            jnp.dot(half, tiles[block, slot], preferred_element_type=jnp.float32)
            for slot in range(band_count)
        ]
        wide = [tiles[block, slot].astype(jnp.float32) for slot in range(band_count)]
        block_parts = []
        for shift in range(3):
            total = jnp.zeros((tile_size, tile_size), jnp.float32)
            flow = jnp.zeros((row_count, tile_size), jnp.float32)
            for slot in range(band_count):
                use = jnp.logical_and(slot < count, offsets[block, slot] == shift - 1)
                weight = jnp.where(use, 1.0, 0.0).astype(jnp.float32)
                total = total + weight * wide[slot]
                flow = flow + weight * carried[slot]
            total = total * scale
            moves[block, :, shift * tile_size : (shift + 1) * tile_size] = total
            block_parts.append(flow * scale)
            if block == block_count - 1 and shift > 0:
                up[row_count + (shift - 1) * tile_size : row_count + shift * tile_size, :] = total
            if block == 0 and shift < 2:
                down[row_count + shift * tile_size : row_count + (shift + 1) * tile_size, :] = total
        parts.append(block_parts)
    for block in range(block_count):
        total = parts[block][1]
        if block + 1 < block_count:
            total = total + parts[block + 1][0]
        if block > 0:
            total = total + parts[block - 1][2]
        inner[block] = total
    up[:row_count, :] = parts[-1][2]
    down[:row_count, :] = parts[0][0]
    keep_up = up[...]
    keep_down = down[...]
    swap = flip[0] == 1
    up[...] = jnp.where(swap, keep_up, keep_down)
    down[...] = jnp.where(swap, keep_down, keep_up)


def prepare(flip, counts, offsets, regions, region_scale, tiles, expectations):
    block_count, band_count, tile_size, _ = tiles.shape
    output_count, expect_rows, _ = expectations.shape
    row_count = output_count * expect_rows
    smem = pl.BlockSpec(memory_space=pltpu.SMEM)
    vmem = pl.BlockSpec(memory_space=pltpu.VMEM)
    edge = jax.ShapeDtypeStruct((row_count + 2 * tile_size, tile_size), jnp.float32)
    return pl.pallas_call(
        prepare_kernel,
        out_shape=(
            jax.ShapeDtypeStruct((block_count, tile_size, 3 * tile_size), jnp.float32),
            jax.ShapeDtypeStruct((row_count, block_count * tile_size), jnp.bfloat16),
            jax.ShapeDtypeStruct((block_count, row_count, tile_size), jnp.float32),
            edge,
            edge,
        ),
        in_specs=[smem, smem, smem, smem, smem, vmem, vmem],
        out_specs=(vmem, vmem, vmem, vmem, vmem),
    )(flip, counts, offsets, regions, region_scale.T, tiles, expectations)


def split_product(rows_full, data_half):
    upper = rows_full.astype(jnp.bfloat16)
    remain = rows_full - upper.astype(jnp.float32)
    middle = remain.astype(jnp.bfloat16)
    lower = (remain - middle.astype(jnp.float32)).astype(jnp.bfloat16)
    total = jnp.dot(upper, data_half, preferred_element_type=jnp.float32)
    total = total + jnp.dot(middle, data_half, preferred_element_type=jnp.float32)
    return total + jnp.dot(lower, data_half, preferred_element_type=jnp.float32)


def shift_pairs(axis, step):
    count = lax.axis_size(axis)
    if step > 0:
        return [(i, i + 1) for i in range(count - 1)]
    return [(i + 1, i) for i in range(count - 1)]


def to_right(value):
    return lax.ppermute(value, ("state", "horizon"), shift_pairs(("state", "horizon"), 1))


def to_left(value):
    return lax.ppermute(value, ("state", "horizon"), shift_pairs(("state", "horizon"), -1))


def swap_edges(to_low, to_high):
    if lax.axis_size("horizon") != 2:
        return to_right(to_high), to_left(to_low)
    first = lax.axis_index("horizon") == 0
    return swap_links(jnp.where(first, to_high, to_low), jnp.where(first, to_low, to_high))


def swap_links(chip_part, cross_part):
    count = lax.axis_size(("state", "horizon"))
    first = lax.axis_index("horizon") == 0
    on_chip = lax.ppermute(chip_part, "horizon", [(0, 1), (1, 0)])
    pairs = []
    for chip in range(count // 2 - 1):
        pairs += [(2 * chip + 1, 2 * chip + 2), (2 * chip + 2, 2 * chip + 1)]
    across = lax.ppermute(cross_part, ("state", "horizon"), pairs)
    return jnp.where(first, across, on_chip), jnp.where(first, on_chip, across)


def band_parts(rows, moves):
    parts = jnp.einsum("cru,cun->crn", rows, moves, precision=lax.Precision.HIGH)
    size = rows.shape[-1]
    down, same, up = parts[..., :size], parts[..., size : 2 * size], parts[..., 2 * size :]
    zero = jnp.zeros_like(same[:1])
    inner = same + jnp.concatenate([down[1:], zero], 0) + jnp.concatenate([zero, up[:-1]], 0)
    return inner, down, up


def band_step(rows, moves):
    inner, down, up = band_parts(rows, moves)
    return inner, down[0], up[-1]


def ext_step(rows, moves):
    inner, down, up = band_parts(rows, moves)
    return inner, down[1], up[-2]


def exchange_round(rows, moves, wide, steps):
    zero = jnp.zeros_like(rows[:1])
    held = jnp.concatenate([zero, rows, zero], 0)
    to_low, to_high, mine = [], [], []
    for _ in range(steps):
        held, out_low, out_high = ext_step(held, wide)
        to_low.append(out_low)
        to_high.append(out_high)
        mine.append(held[1:-1])
    from_low, from_high = swap_edges(jnp.stack(to_low), jnp.stack(to_high))
    levels = []
    carried = None
    for step in range(steps):
        if carried is None:
            carried = jnp.zeros_like(rows)
        else:
            carried, _, _ = band_step(carried, moves)
        carried = carried.at[0].add(from_low[step]).at[-1].add(from_high[step])
        levels.append(mine[step] + carried)
    return levels


def shards(impulses, expectations, region_scale, regions, tiles, offsets, counts):
    block_count, band_count, tile_size, _ = tiles.shape
    state_count, input_count, horizon = impulses.shape
    output_count, expect_rows, _ = expectations.shape
    region_total = region_scale.shape[0]
    width = input_count * horizon
    sections = horizon // expect_rows
    row_count = output_count * expect_rows
    paired = lax.axis_size("horizon") == 2
    flip = jnp.where(lax.axis_index("horizon") == 0, 1, 0) if paired else 0
    flip = jnp.full((1,), flip, jnp.int32)
    moves, rows, inner, first_part, second_part = prepare(
        flip, counts, offsets, regions, region_scale, tiles, expectations
    )
    flat_start = impulses.reshape(state_count, width)
    if paired:
        from_low, from_high = swap_links(first_part, second_part)
    else:
        from_low, from_high = swap_edges(second_part, first_part)
    edge_in = jnp.zeros_like(inner[1:-1])
    levels = [
        inner
        + jnp.concatenate([from_low[None, :row_count], edge_in, from_high[None, :row_count]], 0),
    ]
    left_self = from_low[row_count : row_count + tile_size]
    left_up = from_low[row_count + tile_size :]
    right_down = from_high[row_count : row_count + tile_size]
    right_self = from_high[row_count + tile_size :]
    blank = jnp.zeros_like(left_self)
    wide = jnp.concatenate(
        [
            jnp.concatenate([blank, left_self, left_up], 1)[None],
            moves,
            jnp.concatenate([right_down, right_self, blank], 1)[None],
        ],
        0,
    )
    remaining = sections - 2
    while remaining > 0:
        steps = min(3, remaining)
        levels += exchange_round(levels[-1], moves, wide, steps)
        remaining -= steps
    stacked = jnp.concatenate(
        [level.transpose(1, 0, 2).reshape(row_count, state_count) for level in levels], 0
    )
    product = jnp.dot(
        stacked,
        flat_start.astype(jnp.float32),
        precision=lax.Precision.HIGH,
        preferred_element_type=jnp.float32,
    )
    first = jnp.dot(rows, flat_start, preferred_element_type=jnp.float32)
    pieces = [
        piece.reshape(output_count, expect_rows, input_count, horizon).transpose(1, 0, 2, 3)
        for piece in [first] + jnp.split(product, sections - 1, 0)
    ]
    partial_news = jnp.concatenate(pieces, axis=0)
    jacobian = diagonal_sums(partial_news)
    return halving_scatter(jacobian)


def solution(mesh):
    return jax.shard_map(
        shards,
        mesh=mesh,
        in_specs=(
            P(("state", "horizon"), "input", "groups"),
            P("groups", None, ("state", "horizon")),
            P("groups", None),
            P(("state", "horizon")),
            P(("state", "horizon"), None, None, None),
            P(("state", "horizon"), None),
            P(("state", "horizon")),
        ),
        out_specs=P(("state", "horizon"), "groups", "input", None),
        check_vma=False,
    )
```

```python
import jax
import jax.numpy as jnp
from jax import lax
from jax.sharding import PartitionSpec as P
from jax.experimental import pallas as pl
from jax.experimental.pallas import tpu as pltpu


def diagonal_sums(news):
    rows = news.shape[0]
    width = news.shape[-1]
    total = news
    shift = 1
    while shift < rows:
        moved = lax.pad(
            total[: rows - shift, ..., : width - shift],
            jnp.zeros((), total.dtype),
            [(shift, 0, 0)] + [(0, 0, 0)] * (total.ndim - 2) + [(shift, 0, 0)],
        )
        total = total + moved
        shift *= 2
    return total


def halving_scatter(full):
    state_count = lax.axis_size("state")
    core_count = lax.axis_size("horizon")
    count = state_count * core_count
    if count & (count - 1) or core_count & (core_count - 1):
        return lax.psum_scatter(full, ("state", "horizon"), scatter_dimension=0, tiled=True)
    index = lax.axis_index(("state", "horizon"))
    held = full.reshape((count, full.shape[0] // count) + full.shape[1:])
    step = 1
    while step < count:
        if step < core_count:
            axis, size, flip = "horizon", core_count, step
        else:
            axis, size, flip = "state", state_count, step // core_count
        pairs = [(member, member ^ flip) for member in range(size)]
        bit = (index // step) % 2
        halves = held.reshape((held.shape[0] // 2, 2) + held.shape[1:])
        keep = jnp.where(bit == 1, halves[:, 1], halves[:, 0])
        send = jnp.where(bit == 1, halves[:, 0], halves[:, 1])
        held = keep + lax.ppermute(send, axis, pairs)
        step *= 2
    return held.reshape(held.shape[1:])


def prepare_kernel(flip, counts, offsets, regions, scales, tiles, expect, moves, rows, inner, up, down):
    block_count, band_count, tile_size, _ = tiles.shape
    output_count, expect_rows, _ = expect.shape
    row_count = output_count * expect_rows
    parts = []
    for block in range(block_count):
        count = counts[block]
        scale = lax.rsqrt(jnp.full((1, tile_size), count.astype(jnp.float32), jnp.float32))
        region = regions[block]
        pieces = []
        for out in range(output_count):
            part = expect[out, :, block * tile_size : (block + 1) * tile_size]
            pieces.append((part.astype(jnp.float32) * scales[out, region]).astype(jnp.bfloat16))
        half = jnp.concatenate(pieces, 0)
        rows[:, block * tile_size : (block + 1) * tile_size] = half
        carried = [
            jnp.dot(half, tiles[block, slot], preferred_element_type=jnp.float32)
            for slot in range(band_count)
        ]
        wide = [tiles[block, slot].astype(jnp.float32) for slot in range(band_count)]
        block_parts = []
        for shift in range(3):
            total = jnp.zeros((tile_size, tile_size), jnp.float32)
            flow = jnp.zeros((row_count, tile_size), jnp.float32)
            for slot in range(band_count):
                use = jnp.logical_and(slot < count, offsets[block, slot] == shift - 1)
                weight = jnp.where(use, 1.0, 0.0).astype(jnp.float32)
                total = total + weight * wide[slot]
                flow = flow + weight * carried[slot]
            total = total * scale
            moves[block, :, shift * tile_size : (shift + 1) * tile_size] = total
            block_parts.append(flow * scale)
            if block == block_count - 1 and shift > 0:
                up[row_count + (shift - 1) * tile_size : row_count + shift * tile_size, :] = total
            if block == 0 and shift < 2:
                down[row_count + shift * tile_size : row_count + (shift + 1) * tile_size, :] = total
        parts.append(block_parts)
    for block in range(block_count):
        total = parts[block][1]
        if block + 1 < block_count:
            total = total + parts[block + 1][0]
        if block > 0:
            total = total + parts[block - 1][2]
        inner[block] = total
    up[:row_count, :] = parts[-1][2]
    down[:row_count, :] = parts[0][0]
    keep_up = up[...]
    keep_down = down[...]
    swap = flip[0] == 1
    up[...] = jnp.where(swap, keep_up, keep_down)
    down[...] = jnp.where(swap, keep_down, keep_up)


def prepare(flip, counts, offsets, regions, region_scale, tiles, expectations):
    block_count, band_count, tile_size, _ = tiles.shape
    output_count, expect_rows, _ = expectations.shape
    row_count = output_count * expect_rows
    smem = pl.BlockSpec(memory_space=pltpu.SMEM)
    vmem = pl.BlockSpec(memory_space=pltpu.VMEM)
    edge = jax.ShapeDtypeStruct((row_count + 2 * tile_size, tile_size), jnp.float32)
    return pl.pallas_call(
        prepare_kernel,
        out_shape=(
            jax.ShapeDtypeStruct((block_count, tile_size, 3 * tile_size), jnp.float32),
            jax.ShapeDtypeStruct((row_count, block_count * tile_size), jnp.bfloat16),
            jax.ShapeDtypeStruct((block_count, row_count, tile_size), jnp.float32),
            edge,
            edge,
        ),
        in_specs=[smem, smem, smem, smem, smem, vmem, vmem],
        out_specs=(vmem, vmem, vmem, vmem, vmem),
    )(flip, counts, offsets, regions, region_scale.T, tiles, expectations)


def split_product(rows_full, data_half):
    upper = rows_full.astype(jnp.bfloat16)
    remain = rows_full - upper.astype(jnp.float32)
    middle = remain.astype(jnp.bfloat16)
    lower = (remain - middle.astype(jnp.float32)).astype(jnp.bfloat16)
    total = jnp.dot(upper, data_half, preferred_element_type=jnp.float32)
    total = total + jnp.dot(middle, data_half, preferred_element_type=jnp.float32)
    return total + jnp.dot(lower, data_half, preferred_element_type=jnp.float32)


def shift_pairs(axis, step):
    count = lax.axis_size(axis)
    if step > 0:
        return [(i, i + 1) for i in range(count - 1)]
    return [(i + 1, i) for i in range(count - 1)]


def to_right(value):
    return lax.ppermute(value, ("state", "horizon"), shift_pairs(("state", "horizon"), 1))


def to_left(value):
    return lax.ppermute(value, ("state", "horizon"), shift_pairs(("state", "horizon"), -1))


def swap_edges(to_low, to_high):
    if lax.axis_size("horizon") != 2:
        return to_right(to_high), to_left(to_low)
    first = lax.axis_index("horizon") == 0
    return swap_links(jnp.where(first, to_high, to_low), jnp.where(first, to_low, to_high))


def swap_links(chip_part, cross_part):
    count = lax.axis_size(("state", "horizon"))
    first = lax.axis_index("horizon") == 0
    on_chip = lax.ppermute(chip_part, "horizon", [(0, 1), (1, 0)])
    pairs = []
    for chip in range(count // 2 - 1):
        pairs += [(2 * chip + 1, 2 * chip + 2), (2 * chip + 2, 2 * chip + 1)]
    across = lax.ppermute(cross_part, ("state", "horizon"), pairs)
    return jnp.where(first, across, on_chip), jnp.where(first, on_chip, across)


def band_parts(rows, moves):
    parts = jnp.einsum("cru,cun->crn", rows, moves, precision=lax.Precision.HIGH)
    size = rows.shape[-1]
    down, same, up = parts[..., :size], parts[..., size : 2 * size], parts[..., 2 * size :]
    zero = jnp.zeros_like(same[:1])
    inner = same + jnp.concatenate([down[1:], zero], 0) + jnp.concatenate([zero, up[:-1]], 0)
    return inner, down, up


def band_step(rows, moves):
    inner, down, up = band_parts(rows, moves)
    return inner, down[0], up[-1]


def ext_step(rows, moves):
    inner, down, up = band_parts(rows, moves)
    return inner, down[1], up[-2]


def exchange_round(rows, moves, wide, steps):
    zero = jnp.zeros_like(rows[:1])
    held = jnp.concatenate([zero, rows, zero], 0)
    to_low, to_high, mine = [], [], []
    for _ in range(steps):
        held, out_low, out_high = ext_step(held, wide)
        to_low.append(out_low)
        to_high.append(out_high)
        mine.append(held[1:-1])
    from_low, from_high = swap_edges(jnp.stack(to_low), jnp.stack(to_high))
    levels = []
    carried = None
    for step in range(steps):
        if carried is None:
            carried = jnp.zeros_like(rows)
        else:
            carried, _, _ = band_step(carried, moves)
        carried = carried.at[0].add(from_low[step]).at[-1].add(from_high[step])
        levels.append(mine[step] + carried)
    return levels


def shards(impulses, expectations, region_scale, regions, tiles, offsets, counts):
    block_count, band_count, tile_size, _ = tiles.shape
    state_count, input_count, horizon = impulses.shape
    output_count, expect_rows, _ = expectations.shape
    region_total = region_scale.shape[0]
    width = input_count * horizon
    sections = horizon // expect_rows
    row_count = output_count * expect_rows
    paired = lax.axis_size("horizon") == 2
    flip = jnp.where(lax.axis_index("horizon") == 0, 1, 0) if paired else 0
    flip = jnp.full((1,), flip, jnp.int32)
    moves, rows, inner, first_part, second_part = prepare(
        flip, counts, offsets, regions, region_scale, tiles, expectations
    )
    flat_start = impulses.reshape(state_count, width)
    if paired:
        from_low, from_high = swap_links(first_part, second_part)
    else:
        from_low, from_high = swap_edges(second_part, first_part)
    edge_in = jnp.zeros_like(inner[1:-1])
    levels = [
        inner
        + jnp.concatenate([from_low[None, :row_count], edge_in, from_high[None, :row_count]], 0),
    ]
    left_self = from_low[row_count : row_count + tile_size]
    left_up = from_low[row_count + tile_size :]
    right_down = from_high[row_count : row_count + tile_size]
    right_self = from_high[row_count + tile_size :]
    blank = jnp.zeros_like(left_self)
    wide = jnp.concatenate(
        [
            jnp.concatenate([blank, left_self, left_up], 1)[None],
            moves,
            jnp.concatenate([right_down, right_self, blank], 1)[None],
        ],
        0,
    )
    remaining = sections - 2
    while remaining > 0:
        steps = min(3, remaining)
        levels += exchange_round(levels[-1], moves, wide, steps)
        remaining -= steps
    stacked = jnp.concatenate(
        [rows.astype(jnp.float32)]
        + [level.transpose(1, 0, 2).reshape(row_count, state_count) for level in levels],
        0,
    )
    product = jnp.dot(
        stacked,
        flat_start.astype(jnp.float32),
        precision=lax.Precision.HIGH,
        preferred_element_type=jnp.float32,
    )
    pieces = [
        piece.reshape(output_count, expect_rows, input_count, horizon).transpose(1, 0, 2, 3)
        for piece in jnp.split(product, sections, 0)
    ]
    partial_news = jnp.concatenate(pieces, axis=0)
    jacobian = diagonal_sums(partial_news)
    return halving_scatter(jacobian)


def solution(mesh):
    return jax.shard_map(
        shards,
        mesh=mesh,
        in_specs=(
            P(("state", "horizon"), "input", "groups"),
            P("groups", None, ("state", "horizon")),
            P("groups", None),
            P(("state", "horizon")),
            P(("state", "horizon"), None, None, None),
            P(("state", "horizon"), None),
            P(("state", "horizon")),
        ),
        out_specs=P(("state", "horizon"), "groups", "input", None),
        check_vma=False,
    )
```

```python
import jax
import jax.numpy as jnp
from jax import lax
from jax.sharding import PartitionSpec as P
from jax.experimental import pallas as pl
from jax.experimental.pallas import tpu as pltpu


def diagonal_sums(news):
    rows = news.shape[0]
    width = news.shape[-1]
    total = news
    shift = 1
    while shift < rows:
        moved = lax.pad(
            total[: rows - shift, ..., : width - shift],
            jnp.zeros((), total.dtype),
            [(shift, 0, 0)] + [(0, 0, 0)] * (total.ndim - 2) + [(shift, 0, 0)],
        )
        total = total + moved
        shift *= 2
    return total


def halving_scatter(full):
    state_count = lax.axis_size("state")
    core_count = lax.axis_size("horizon")
    count = state_count * core_count
    if count & (count - 1) or core_count & (core_count - 1):
        return lax.psum_scatter(full, ("state", "horizon"), scatter_dimension=0, tiled=True)
    index = lax.axis_index(("state", "horizon"))
    held = full.reshape((count, full.shape[0] // count) + full.shape[1:])
    step = 1
    while step < count:
        if step < core_count:
            axis, size, flip = "horizon", core_count, step
        else:
            axis, size, flip = "state", state_count, step // core_count
        pairs = [(member, member ^ flip) for member in range(size)]
        bit = (index // step) % 2
        halves = held.reshape((held.shape[0] // 2, 2) + held.shape[1:])
        keep = jnp.where(bit == 1, halves[:, 1], halves[:, 0])
        send = jnp.where(bit == 1, halves[:, 0], halves[:, 1])
        held = keep + lax.ppermute(send, axis, pairs)
        step *= 2
    return held.reshape(held.shape[1:])


def prepare_kernel(flip, counts, offsets, regions, scales, tiles, expect, moves, rows, inner, up, down):
    block_count, band_count, tile_size, _ = tiles.shape
    output_count, expect_rows, _ = expect.shape
    row_count = output_count * expect_rows
    parts = []
    moves[0] = jnp.zeros(moves.shape[1:], jnp.float32)
    moves[block_count + 1] = jnp.zeros(moves.shape[1:], jnp.float32)
    for block in range(block_count):
        count = counts[block]
        scale = lax.rsqrt(jnp.full((1, tile_size), count.astype(jnp.float32), jnp.float32))
        region = regions[block]
        pieces = []
        for out in range(output_count):
            part = expect[out, :, block * tile_size : (block + 1) * tile_size]
            pieces.append((part.astype(jnp.float32) * scales[out, region]).astype(jnp.bfloat16))
        half = jnp.concatenate(pieces, 0)
        rows[:, block * tile_size : (block + 1) * tile_size] = half
        carried = [
            jnp.dot(half, tiles[block, slot], preferred_element_type=jnp.float32)
            for slot in range(band_count)
        ]
        wide = [tiles[block, slot].astype(jnp.float32) for slot in range(band_count)]
        block_parts = []
        for shift in range(3):
            total = jnp.zeros((tile_size, tile_size), jnp.float32)
            flow = jnp.zeros((row_count, tile_size), jnp.float32)
            for slot in range(band_count):
                use = jnp.logical_and(slot < count, offsets[block, slot] == shift - 1)
                weight = jnp.where(use, 1.0, 0.0).astype(jnp.float32)
                total = total + weight * wide[slot]
                flow = flow + weight * carried[slot]
            total = total * scale
            moves[block + 1, :, shift * tile_size : (shift + 1) * tile_size] = total
            block_parts.append(flow * scale)
            if block == block_count - 1 and shift > 0:
                up[row_count + (shift - 1) * tile_size : row_count + shift * tile_size, :] = total
            if block == 0 and shift < 2:
                down[row_count + shift * tile_size : row_count + (shift + 1) * tile_size, :] = total
        parts.append(block_parts)
    for block in range(block_count):
        total = parts[block][1]
        if block + 1 < block_count:
            total = total + parts[block + 1][0]
        if block > 0:
            total = total + parts[block - 1][2]
        inner[block] = total
    up[:row_count, :] = parts[-1][2]
    down[:row_count, :] = parts[0][0]
    keep_up = up[...]
    keep_down = down[...]
    swap = flip[0] == 1
    up[...] = jnp.where(swap, keep_up, keep_down)
    down[...] = jnp.where(swap, keep_down, keep_up)


def prepare(flip, counts, offsets, regions, region_scale, tiles, expectations):
    block_count, band_count, tile_size, _ = tiles.shape
    output_count, expect_rows, _ = expectations.shape
    row_count = output_count * expect_rows
    smem = pl.BlockSpec(memory_space=pltpu.SMEM)
    vmem = pl.BlockSpec(memory_space=pltpu.VMEM)
    edge = jax.ShapeDtypeStruct((row_count + 2 * tile_size, tile_size), jnp.float32)
    return pl.pallas_call(
        prepare_kernel,
        out_shape=(
            jax.ShapeDtypeStruct((block_count + 2, tile_size, 3 * tile_size), jnp.float32),
            jax.ShapeDtypeStruct((row_count, block_count * tile_size), jnp.bfloat16),
            jax.ShapeDtypeStruct((block_count, row_count, tile_size), jnp.float32),
            edge,
            edge,
        ),
        in_specs=[smem, smem, smem, smem, smem, vmem, vmem],
        out_specs=(vmem, vmem, vmem, vmem, vmem),
    )(flip, counts, offsets, regions, region_scale.T, tiles, expectations)


def split_product(rows_full, data_half):
    upper = rows_full.astype(jnp.bfloat16)
    remain = rows_full - upper.astype(jnp.float32)
    middle = remain.astype(jnp.bfloat16)
    lower = (remain - middle.astype(jnp.float32)).astype(jnp.bfloat16)
    total = jnp.dot(upper, data_half, preferred_element_type=jnp.float32)
    total = total + jnp.dot(middle, data_half, preferred_element_type=jnp.float32)
    return total + jnp.dot(lower, data_half, preferred_element_type=jnp.float32)


def shift_pairs(axis, step):
    count = lax.axis_size(axis)
    if step > 0:
        return [(i, i + 1) for i in range(count - 1)]
    return [(i + 1, i) for i in range(count - 1)]


def to_right(value):
    return lax.ppermute(value, ("state", "horizon"), shift_pairs(("state", "horizon"), 1))


def to_left(value):
    return lax.ppermute(value, ("state", "horizon"), shift_pairs(("state", "horizon"), -1))


def swap_edges(to_low, to_high):
    if lax.axis_size("horizon") != 2:
        return to_right(to_high), to_left(to_low)
    first = lax.axis_index("horizon") == 0
    return swap_links(jnp.where(first, to_high, to_low), jnp.where(first, to_low, to_high))


def swap_links(chip_part, cross_part):
    count = lax.axis_size(("state", "horizon"))
    first = lax.axis_index("horizon") == 0
    on_chip = lax.ppermute(chip_part, "horizon", [(0, 1), (1, 0)])
    pairs = []
    for chip in range(count // 2 - 1):
        pairs += [(2 * chip + 1, 2 * chip + 2), (2 * chip + 2, 2 * chip + 1)]
    across = lax.ppermute(cross_part, ("state", "horizon"), pairs)
    return jnp.where(first, across, on_chip), jnp.where(first, on_chip, across)


def band_parts(rows, moves):
    parts = jnp.einsum("cru,cun->crn", rows, moves, precision=lax.Precision.HIGH)
    size = rows.shape[-1]
    down, same, up = parts[..., :size], parts[..., size : 2 * size], parts[..., 2 * size :]
    zero = jnp.zeros_like(same[:1])
    inner = same + jnp.concatenate([down[1:], zero], 0) + jnp.concatenate([zero, up[:-1]], 0)
    return inner, down, up


def band_step(rows, moves):
    inner, down, up = band_parts(rows, moves)
    return inner, down[0], up[-1]


def ext_step(rows, moves):
    inner, down, up = band_parts(rows, moves)
    return inner, down[1], up[-2]


def exchange_round(rows, wide, steps):
    zero = jnp.zeros_like(rows[:1])
    held = jnp.concatenate([zero, rows, zero], 0)
    to_low, to_high, mine = [], [], []
    for _ in range(steps):
        held, out_low, out_high = ext_step(held, wide)
        to_low.append(out_low)
        to_high.append(out_high)
        mine.append(held[1:-1])
    from_low, from_high = swap_edges(jnp.stack(to_low), jnp.stack(to_high))
    levels = []
    carried = None
    for step in range(steps):
        if carried is None:
            carried = jnp.zeros_like(rows)
        else:
            edge = jnp.zeros_like(carried[:1])
            carried, _, _ = ext_step(jnp.concatenate([edge, carried, edge], 0), wide)
            carried = carried[1:-1]
        carried = carried.at[0].add(from_low[step]).at[-1].add(from_high[step])
        levels.append(mine[step] + carried)
    return levels


def shards(impulses, expectations, region_scale, regions, tiles, offsets, counts):
    block_count, band_count, tile_size, _ = tiles.shape
    state_count, input_count, horizon = impulses.shape
    output_count, expect_rows, _ = expectations.shape
    region_total = region_scale.shape[0]
    width = input_count * horizon
    sections = horizon // expect_rows
    row_count = output_count * expect_rows
    paired = lax.axis_size("horizon") == 2
    flip = jnp.where(lax.axis_index("horizon") == 0, 1, 0) if paired else 0
    flip = jnp.full((1,), flip, jnp.int32)
    moves, rows, inner, first_part, second_part = prepare(
        flip, counts, offsets, regions, region_scale, tiles, expectations
    )
    flat_start = impulses.reshape(state_count, width)
    if paired:
        from_low, from_high = swap_links(first_part, second_part)
    else:
        from_low, from_high = swap_edges(second_part, first_part)
    edge_in = jnp.zeros_like(inner[1:-1])
    levels = [
        inner
        + jnp.concatenate([from_low[None, :row_count], edge_in, from_high[None, :row_count]], 0),
    ]
    left_self = from_low[row_count : row_count + tile_size]
    left_up = from_low[row_count + tile_size :]
    right_down = from_high[row_count : row_count + tile_size]
    right_self = from_high[row_count + tile_size :]
    size = tile_size
    wide = moves.at[0, :, size : 2 * size].set(left_self).at[0, :, 2 * size :].set(left_up)
    wide = wide.at[-1, :, :size].set(right_down).at[-1, :, size : 2 * size].set(right_self)
    remaining = sections - 2
    while remaining > 0:
        steps = min(3, remaining)
        levels += exchange_round(levels[-1], wide, steps)
        remaining -= steps
    stacked = jnp.concatenate(
        [level.transpose(1, 0, 2).reshape(row_count, state_count) for level in levels], 0
    )
    product = jnp.dot(
        stacked,
        flat_start.astype(jnp.float32),
        precision=lax.Precision.HIGH,
        preferred_element_type=jnp.float32,
    )
    first = jnp.dot(rows, flat_start, preferred_element_type=jnp.float32)
    pieces = [
        piece.reshape(output_count, expect_rows, input_count, horizon).transpose(1, 0, 2, 3)
        for piece in [first] + jnp.split(product, sections - 1, 0)
    ]
    partial_news = jnp.concatenate(pieces, axis=0)
    jacobian = diagonal_sums(partial_news)
    return halving_scatter(jacobian)


def solution(mesh):
    return jax.shard_map(
        shards,
        mesh=mesh,
        in_specs=(
            P(("state", "horizon"), "input", "groups"),
            P("groups", None, ("state", "horizon")),
            P("groups", None),
            P(("state", "horizon")),
            P(("state", "horizon"), None, None, None),
            P(("state", "horizon"), None),
            P(("state", "horizon")),
        ),
        out_specs=P(("state", "horizon"), "groups", "input", None),
        check_vma=False,
    )
```

```python
import jax
import jax.numpy as jnp
from jax import lax
from jax.sharding import PartitionSpec as P
from jax.experimental import pallas as pl
from jax.experimental.pallas import tpu as pltpu


def diagonal_sums(news):
    rows = news.shape[0]
    width = news.shape[-1]
    total = news
    shift = 1
    while shift < rows:
        moved = lax.pad(
            total[: rows - shift, ..., : width - shift],
            jnp.zeros((), total.dtype),
            [(shift, 0, 0)] + [(0, 0, 0)] * (total.ndim - 2) + [(shift, 0, 0)],
        )
        total = total + moved
        shift *= 2
    return total


def halving_scatter(full):
    state_count = lax.axis_size("state")
    core_count = lax.axis_size("horizon")
    count = state_count * core_count
    if count & (count - 1) or core_count & (core_count - 1):
        return lax.psum_scatter(full, ("state", "horizon"), scatter_dimension=0, tiled=True)
    index = lax.axis_index(("state", "horizon"))
    held = full.reshape((count, full.shape[0] // count) + full.shape[1:])
    step = 1
    while step < count:
        if step < core_count:
            axis, size, flip = "horizon", core_count, step
        else:
            axis, size, flip = "state", state_count, step // core_count
        pairs = [(member, member ^ flip) for member in range(size)]
        bit = (index // step) % 2
        halves = held.reshape((held.shape[0] // 2, 2) + held.shape[1:])
        keep = lax.dynamic_index_in_dim(halves, bit, axis=1, keepdims=False)
        send = lax.dynamic_index_in_dim(halves, 1 - bit, axis=1, keepdims=False)
        held = keep + lax.ppermute(send, axis, pairs)
        step *= 2
    return held.reshape(held.shape[1:])


def prepare_kernel(flip, counts, offsets, regions, scales, tiles, expect, moves, rows, inner, up, down):
    block_count, band_count, tile_size, _ = tiles.shape
    output_count, expect_rows, _ = expect.shape
    row_count = output_count * expect_rows
    parts = []
    for block in range(block_count):
        count = counts[block]
        scale = lax.rsqrt(jnp.full((1, tile_size), count.astype(jnp.float32), jnp.float32))
        region = regions[block]
        pieces = []
        for out in range(output_count):
            part = expect[out, :, block * tile_size : (block + 1) * tile_size]
            pieces.append((part.astype(jnp.float32) * scales[out, region]).astype(jnp.bfloat16))
        half = jnp.concatenate(pieces, 0)
        rows[:, block * tile_size : (block + 1) * tile_size] = half
        carried = [
            jnp.dot(half, tiles[block, slot], preferred_element_type=jnp.float32)
            for slot in range(band_count)
        ]
        wide = [tiles[block, slot].astype(jnp.float32) for slot in range(band_count)]
        block_parts = []
        for shift in range(3):
            total = jnp.zeros((tile_size, tile_size), jnp.float32)
            flow = jnp.zeros((row_count, tile_size), jnp.float32)
            for slot in range(band_count):
                use = jnp.logical_and(slot < count, offsets[block, slot] == shift - 1)
                weight = jnp.where(use, 1.0, 0.0).astype(jnp.float32)
                total = total + weight * wide[slot]
                flow = flow + weight * carried[slot]
            total = total * scale
            moves[block, :, shift * tile_size : (shift + 1) * tile_size] = total
            block_parts.append(flow * scale)
            if block == block_count - 1 and shift > 0:
                up[row_count + (shift - 1) * tile_size : row_count + shift * tile_size, :] = total
            if block == 0 and shift < 2:
                down[row_count + shift * tile_size : row_count + (shift + 1) * tile_size, :] = total
        parts.append(block_parts)
    for block in range(block_count):
        total = parts[block][1]
        if block + 1 < block_count:
            total = total + parts[block + 1][0]
        if block > 0:
            total = total + parts[block - 1][2]
        inner[block] = total
    up[:row_count, :] = parts[-1][2]
    down[:row_count, :] = parts[0][0]
    keep_up = up[...]
    keep_down = down[...]
    swap = flip[0] == 1
    up[...] = jnp.where(swap, keep_up, keep_down)
    down[...] = jnp.where(swap, keep_down, keep_up)


def prepare(flip, counts, offsets, regions, region_scale, tiles, expectations):
    block_count, band_count, tile_size, _ = tiles.shape
    output_count, expect_rows, _ = expectations.shape
    row_count = output_count * expect_rows
    smem = pl.BlockSpec(memory_space=pltpu.SMEM)
    vmem = pl.BlockSpec(memory_space=pltpu.VMEM)
    edge = jax.ShapeDtypeStruct((row_count + 2 * tile_size, tile_size), jnp.float32)
    return pl.pallas_call(
        prepare_kernel,
        out_shape=(
            jax.ShapeDtypeStruct((block_count, tile_size, 3 * tile_size), jnp.float32),
            jax.ShapeDtypeStruct((row_count, block_count * tile_size), jnp.bfloat16),
            jax.ShapeDtypeStruct((block_count, row_count, tile_size), jnp.float32),
            edge,
            edge,
        ),
        in_specs=[smem, smem, smem, smem, smem, vmem, vmem],
        out_specs=(vmem, vmem, vmem, vmem, vmem),
    )(flip, counts, offsets, regions, region_scale.T, tiles, expectations)


def split_product(rows_full, data_half):
    upper = rows_full.astype(jnp.bfloat16)
    remain = rows_full - upper.astype(jnp.float32)
    middle = remain.astype(jnp.bfloat16)
    lower = (remain - middle.astype(jnp.float32)).astype(jnp.bfloat16)
    total = jnp.dot(upper, data_half, preferred_element_type=jnp.float32)
    total = total + jnp.dot(middle, data_half, preferred_element_type=jnp.float32)
    return total + jnp.dot(lower, data_half, preferred_element_type=jnp.float32)


def shift_pairs(axis, step):
    count = lax.axis_size(axis)
    if step > 0:
        return [(i, i + 1) for i in range(count - 1)]
    return [(i + 1, i) for i in range(count - 1)]


def to_right(value):
    return lax.ppermute(value, ("state", "horizon"), shift_pairs(("state", "horizon"), 1))


def to_left(value):
    return lax.ppermute(value, ("state", "horizon"), shift_pairs(("state", "horizon"), -1))


def swap_edges(to_low, to_high):
    if lax.axis_size("horizon") != 2:
        return to_right(to_high), to_left(to_low)
    first = lax.axis_index("horizon") == 0
    return swap_links(jnp.where(first, to_high, to_low), jnp.where(first, to_low, to_high))


def swap_links(chip_part, cross_part):
    count = lax.axis_size(("state", "horizon"))
    first = lax.axis_index("horizon") == 0
    on_chip = lax.ppermute(chip_part, "horizon", [(0, 1), (1, 0)])
    pairs = []
    for chip in range(count // 2 - 1):
        pairs += [(2 * chip + 1, 2 * chip + 2), (2 * chip + 2, 2 * chip + 1)]
    across = lax.ppermute(cross_part, ("state", "horizon"), pairs)
    return jnp.where(first, across, on_chip), jnp.where(first, on_chip, across)


def band_parts(rows, moves):
    parts = jnp.einsum("cru,cun->crn", rows, moves, precision=lax.Precision.HIGH)
    size = rows.shape[-1]
    down, same, up = parts[..., :size], parts[..., size : 2 * size], parts[..., 2 * size :]
    zero = jnp.zeros_like(same[:1])
    inner = same + jnp.concatenate([down[1:], zero], 0) + jnp.concatenate([zero, up[:-1]], 0)
    return inner, down, up


def band_step(rows, moves):
    inner, down, up = band_parts(rows, moves)
    return inner, down[0], up[-1]


def ext_step(rows, moves):
    inner, down, up = band_parts(rows, moves)
    return inner, down[1], up[-2]


def exchange_round(rows, moves, wide, steps):
    zero = jnp.zeros_like(rows[:1])
    held = jnp.concatenate([zero, rows, zero], 0)
    to_low, to_high, mine = [], [], []
    for _ in range(steps):
        held, out_low, out_high = ext_step(held, wide)
        to_low.append(out_low)
        to_high.append(out_high)
        mine.append(held[1:-1])
    from_low, from_high = swap_edges(jnp.stack(to_low), jnp.stack(to_high))
    levels = []
    carried = None
    for step in range(steps):
        if carried is None:
            carried = jnp.zeros_like(rows)
        else:
            carried, _, _ = band_step(carried, moves)
        carried = carried.at[0].add(from_low[step]).at[-1].add(from_high[step])
        levels.append(mine[step] + carried)
    return levels


def shards(impulses, expectations, region_scale, regions, tiles, offsets, counts):
    block_count, band_count, tile_size, _ = tiles.shape
    state_count, input_count, horizon = impulses.shape
    output_count, expect_rows, _ = expectations.shape
    region_total = region_scale.shape[0]
    width = input_count * horizon
    sections = horizon // expect_rows
    row_count = output_count * expect_rows
    paired = lax.axis_size("horizon") == 2
    flip = jnp.where(lax.axis_index("horizon") == 0, 1, 0) if paired else 0
    flip = jnp.full((1,), flip, jnp.int32)
    moves, rows, inner, first_part, second_part = prepare(
        flip, counts, offsets, regions, region_scale, tiles, expectations
    )
    flat_start = impulses.reshape(state_count, width)
    if paired:
        from_low, from_high = swap_links(first_part, second_part)
    else:
        from_low, from_high = swap_edges(second_part, first_part)
    edge_in = jnp.zeros_like(inner[1:-1])
    levels = [
        inner
        + jnp.concatenate([from_low[None, :row_count], edge_in, from_high[None, :row_count]], 0),
    ]
    left_self = from_low[row_count : row_count + tile_size]
    left_up = from_low[row_count + tile_size :]
    right_down = from_high[row_count : row_count + tile_size]
    right_self = from_high[row_count + tile_size :]
    blank = jnp.zeros_like(left_self)
    wide = jnp.concatenate(
        [
            jnp.concatenate([blank, left_self, left_up], 1)[None],
            moves,
            jnp.concatenate([right_down, right_self, blank], 1)[None],
        ],
        0,
    )
    remaining = sections - 2
    while remaining > 0:
        steps = min(3, remaining)
        levels += exchange_round(levels[-1], moves, wide, steps)
        remaining -= steps
    stacked = jnp.concatenate(
        [level.transpose(1, 0, 2).reshape(row_count, state_count) for level in levels], 0
    )
    product = jnp.dot(
        stacked,
        flat_start.astype(jnp.float32),
        precision=lax.Precision.HIGH,
        preferred_element_type=jnp.float32,
    )
    first = jnp.dot(rows, flat_start, preferred_element_type=jnp.float32)
    pieces = [
        piece.reshape(output_count, expect_rows, input_count, horizon).transpose(1, 0, 2, 3)
        for piece in [first] + jnp.split(product, sections - 1, 0)
    ]
    partial_news = jnp.concatenate(pieces, axis=0)
    jacobian = diagonal_sums(partial_news)
    return halving_scatter(jacobian)


def solution(mesh):
    return jax.shard_map(
        shards,
        mesh=mesh,
        in_specs=(
            P(("state", "horizon"), "input", "groups"),
            P("groups", None, ("state", "horizon")),
            P("groups", None),
            P(("state", "horizon")),
            P(("state", "horizon"), None, None, None),
            P(("state", "horizon"), None),
            P(("state", "horizon")),
        ),
        out_specs=P(("state", "horizon"), "groups", "input", None),
        check_vma=False,
    )
```

```python
import jax
import jax.numpy as jnp
from jax import lax
from jax.sharding import PartitionSpec as P
from jax.experimental import pallas as pl
from jax.experimental.pallas import tpu as pltpu


def diagonal_sums(news):
    rows = news.shape[0]
    width = news.shape[-1]
    total = news
    shift = 1
    while shift < rows:
        moved = lax.pad(
            total[: rows - shift, ..., : width - shift],
            jnp.zeros((), total.dtype),
            [(shift, 0, 0)] + [(0, 0, 0)] * (total.ndim - 2) + [(shift, 0, 0)],
        )
        total = total + moved
        shift *= 2
    return total


def halving_scatter(full):
    state_count = lax.axis_size("state")
    core_count = lax.axis_size("horizon")
    count = state_count * core_count
    if count & (count - 1) or core_count & (core_count - 1):
        return lax.psum_scatter(full, ("state", "horizon"), scatter_dimension=0, tiled=True)
    index = lax.axis_index(("state", "horizon"))
    held = full.reshape((count, full.shape[0] // count) + full.shape[1:])
    step = 1
    while step < count:
        if step < core_count:
            axis, size, flip = "horizon", core_count, step
        else:
            axis, size, flip = "state", state_count, step // core_count
        pairs = [(member, member ^ flip) for member in range(size)]
        bit = (index // step) % 2
        halves = held.reshape((held.shape[0] // 2, 2) + held.shape[1:])
        keep = lax.dynamic_index_in_dim(halves, bit, axis=1, keepdims=False)
        send = lax.dynamic_index_in_dim(halves, 1 - bit, axis=1, keepdims=False)
        held = keep + lax.ppermute(send, axis, pairs)
        step *= 2
    return held.reshape(held.shape[1:])


def prepare_kernel(flip, counts, offsets, regions, scales, tiles, expect, moves, rows, inner, up, down):
    block_count, band_count, tile_size, _ = tiles.shape
    output_count, expect_rows, _ = expect.shape
    row_count = output_count * expect_rows
    parts = []
    for block in range(block_count):
        count = counts[block]
        scale = lax.rsqrt(jnp.full((1, tile_size), count.astype(jnp.float32), jnp.float32))
        region = regions[block]
        pieces = []
        for out in range(output_count):
            part = expect[out, :, block * tile_size : (block + 1) * tile_size]
            pieces.append((part.astype(jnp.float32) * scales[out, region]).astype(jnp.bfloat16))
        half = jnp.concatenate(pieces, 0)
        rows[:, block * tile_size : (block + 1) * tile_size] = half
        carried = [
            jnp.dot(half, tiles[block, slot], preferred_element_type=jnp.float32)
            for slot in range(band_count)
        ]
        wide = [tiles[block, slot].astype(jnp.float32) for slot in range(band_count)]
        block_parts = []
        for shift in range(3):
            total = jnp.zeros((tile_size, tile_size), jnp.float32)
            flow = jnp.zeros((row_count, tile_size), jnp.float32)
            for slot in range(band_count):
                use = jnp.logical_and(slot < count, offsets[block, slot] == shift - 1)
                weight = jnp.where(use, 1.0, 0.0).astype(jnp.float32)
                total = total + weight * wide[slot]
                flow = flow + weight * carried[slot]
            total = total * scale
            moves[block, :, shift * tile_size : (shift + 1) * tile_size] = total
            block_parts.append(flow * scale)
            if block == block_count - 1 and shift > 0:
                up[row_count + (shift - 1) * tile_size : row_count + shift * tile_size, :] = total
            if block == 0 and shift < 2:
                down[row_count + shift * tile_size : row_count + (shift + 1) * tile_size, :] = total
        parts.append(block_parts)
    for block in range(block_count):
        total = parts[block][1]
        if block + 1 < block_count:
            total = total + parts[block + 1][0]
        if block > 0:
            total = total + parts[block - 1][2]
        inner[block] = total
    up[:row_count, :] = parts[-1][2]
    down[:row_count, :] = parts[0][0]
    keep_up = up[...]
    keep_down = down[...]
    swap = flip[0] == 1
    up[...] = jnp.where(swap, keep_up, keep_down)
    down[...] = jnp.where(swap, keep_down, keep_up)


def prepare(flip, counts, offsets, regions, region_scale, tiles, expectations):
    block_count, band_count, tile_size, _ = tiles.shape
    output_count, expect_rows, _ = expectations.shape
    row_count = output_count * expect_rows
    smem = pl.BlockSpec(memory_space=pltpu.SMEM)
    vmem = pl.BlockSpec(memory_space=pltpu.VMEM)
    edge = jax.ShapeDtypeStruct((row_count + 2 * tile_size, tile_size), jnp.float32)
    return pl.pallas_call(
        prepare_kernel,
        out_shape=(
            jax.ShapeDtypeStruct((block_count, tile_size, 3 * tile_size), jnp.float32),
            jax.ShapeDtypeStruct((row_count, block_count * tile_size), jnp.bfloat16),
            jax.ShapeDtypeStruct((block_count, row_count, tile_size), jnp.float32),
            edge,
            edge,
        ),
        in_specs=[smem, smem, smem, smem, smem, vmem, vmem],
        out_specs=(vmem, vmem, vmem, vmem, vmem),
    )(flip, counts, offsets, regions, region_scale.T, tiles, expectations)


def split_product(rows_full, data_half):
    upper = rows_full.astype(jnp.bfloat16)
    remain = rows_full - upper.astype(jnp.float32)
    middle = remain.astype(jnp.bfloat16)
    lower = (remain - middle.astype(jnp.float32)).astype(jnp.bfloat16)
    total = jnp.dot(upper, data_half, preferred_element_type=jnp.float32)
    total = total + jnp.dot(middle, data_half, preferred_element_type=jnp.float32)
    return total + jnp.dot(lower, data_half, preferred_element_type=jnp.float32)


def shift_pairs(axis, step):
    count = lax.axis_size(axis)
    if step > 0:
        return [(i, i + 1) for i in range(count - 1)]
    return [(i + 1, i) for i in range(count - 1)]


def to_right(value):
    return lax.ppermute(value, ("state", "horizon"), shift_pairs(("state", "horizon"), 1))


def to_left(value):
    return lax.ppermute(value, ("state", "horizon"), shift_pairs(("state", "horizon"), -1))


def swap_edges(to_low, to_high):
    if lax.axis_size("horizon") != 2:
        return to_right(to_high), to_left(to_low)
    pair = jnp.stack([to_low, to_high])
    core = lax.axis_index("horizon")
    chip_part = lax.dynamic_index_in_dim(pair, 1 - core, 0, keepdims=False)
    cross_part = lax.dynamic_index_in_dim(pair, core, 0, keepdims=False)
    return swap_links(chip_part, cross_part)


def swap_links(chip_part, cross_part):
    count = lax.axis_size(("state", "horizon"))
    first = lax.axis_index("horizon") == 0
    on_chip = lax.ppermute(chip_part, "horizon", [(0, 1), (1, 0)])
    pairs = []
    for chip in range(count // 2 - 1):
        pairs += [(2 * chip + 1, 2 * chip + 2), (2 * chip + 2, 2 * chip + 1)]
    across = lax.ppermute(cross_part, ("state", "horizon"), pairs)
    got = jnp.stack([across, on_chip])
    core = lax.axis_index("horizon")
    return (
        lax.dynamic_index_in_dim(got, core, 0, keepdims=False),
        lax.dynamic_index_in_dim(got, 1 - core, 0, keepdims=False),
    )


def band_parts(rows, moves):
    parts = jnp.einsum("cru,cun->crn", rows, moves, precision=lax.Precision.HIGH)
    size = rows.shape[-1]
    down, same, up = parts[..., :size], parts[..., size : 2 * size], parts[..., 2 * size :]
    zero = jnp.zeros_like(same[:1])
    inner = same + jnp.concatenate([down[1:], zero], 0) + jnp.concatenate([zero, up[:-1]], 0)
    return inner, down, up


def band_step(rows, moves):
    inner, down, up = band_parts(rows, moves)
    return inner, down[0], up[-1]


def ext_step(rows, moves):
    inner, down, up = band_parts(rows, moves)
    return inner, down[1], up[-2]


def exchange_round(rows, moves, wide, steps):
    zero = jnp.zeros_like(rows[:1])
    held = jnp.concatenate([zero, rows, zero], 0)
    to_low, to_high, mine = [], [], []
    for _ in range(steps):
        held, out_low, out_high = ext_step(held, wide)
        to_low.append(out_low)
        to_high.append(out_high)
        mine.append(held[1:-1])
    from_low, from_high = swap_edges(jnp.stack(to_low), jnp.stack(to_high))
    levels = []
    carried = None
    for step in range(steps):
        if carried is None:
            carried = jnp.zeros_like(rows)
        else:
            carried, _, _ = band_step(carried, moves)
        carried = carried.at[0].add(from_low[step]).at[-1].add(from_high[step])
        levels.append(mine[step] + carried)
    return levels


def shards(impulses, expectations, region_scale, regions, tiles, offsets, counts):
    block_count, band_count, tile_size, _ = tiles.shape
    state_count, input_count, horizon = impulses.shape
    output_count, expect_rows, _ = expectations.shape
    region_total = region_scale.shape[0]
    width = input_count * horizon
    sections = horizon // expect_rows
    row_count = output_count * expect_rows
    paired = lax.axis_size("horizon") == 2
    flip = jnp.where(lax.axis_index("horizon") == 0, 1, 0) if paired else 0
    flip = jnp.full((1,), flip, jnp.int32)
    moves, rows, inner, first_part, second_part = prepare(
        flip, counts, offsets, regions, region_scale, tiles, expectations
    )
    flat_start = impulses.reshape(state_count, width)
    if paired:
        from_low, from_high = swap_links(first_part, second_part)
    else:
        from_low, from_high = swap_edges(second_part, first_part)
    edge_in = jnp.zeros_like(inner[1:-1])
    levels = [
        inner
        + jnp.concatenate([from_low[None, :row_count], edge_in, from_high[None, :row_count]], 0),
    ]
    left_self = from_low[row_count : row_count + tile_size]
    left_up = from_low[row_count + tile_size :]
    right_down = from_high[row_count : row_count + tile_size]
    right_self = from_high[row_count + tile_size :]
    blank = jnp.zeros_like(left_self)
    wide = jnp.concatenate(
        [
            jnp.concatenate([blank, left_self, left_up], 1)[None],
            moves,
            jnp.concatenate([right_down, right_self, blank], 1)[None],
        ],
        0,
    )
    remaining = sections - 2
    while remaining > 0:
        steps = min(3, remaining)
        levels += exchange_round(levels[-1], moves, wide, steps)
        remaining -= steps
    stacked = jnp.concatenate(
        [level.transpose(1, 0, 2).reshape(row_count, state_count) for level in levels], 0
    )
    product = jnp.dot(
        stacked,
        flat_start.astype(jnp.float32),
        precision=lax.Precision.HIGH,
        preferred_element_type=jnp.float32,
    )
    first = jnp.dot(rows, flat_start, preferred_element_type=jnp.float32)
    pieces = [
        piece.reshape(output_count, expect_rows, input_count, horizon).transpose(1, 0, 2, 3)
        for piece in [first] + jnp.split(product, sections - 1, 0)
    ]
    partial_news = jnp.concatenate(pieces, axis=0)
    jacobian = diagonal_sums(partial_news)
    return halving_scatter(jacobian)


def solution(mesh):
    return jax.shard_map(
        shards,
        mesh=mesh,
        in_specs=(
            P(("state", "horizon"), "input", "groups"),
            P("groups", None, ("state", "horizon")),
            P("groups", None),
            P(("state", "horizon")),
            P(("state", "horizon"), None, None, None),
            P(("state", "horizon"), None),
            P(("state", "horizon")),
        ),
        out_specs=P(("state", "horizon"), "groups", "input", None),
        check_vma=False,
    )
```
